128 devices in a mesh: loop: 64 (over x, z, y), grp: 2 (over core).
Axes of the slice: x: 4, y: 4, z: 4, core: 2. Of those that a mesh axis runs over, the one named last changes fastest.
Arguments:
- particles: bfloat16 [8192, 3456], P('loop'), may hold values from -32 to 32
- references: bfloat16 [256, 3456], P(('loop', 'grp')), may hold values from -6 to 6
- classes: int32 [8192], P(('loop', 'grp')), may hold values from 0 to 255, as said below
- angles: int32 [8192], P(('loop', 'grp')), may hold values from 0 to 71
- weights: int32 [8192], P(('loop', 'grp')), may hold values from 1 to 4
Outputs:
- log_evidence: float32 [8192], P(('loop', 'grp'))
- class_average: float32 [256, 3456], P(('loop', 'grp'))
The draws below stay inside these ranges and needn't reach their ends.
Inputs may be any that keep to these rules, and one draw needn't show every extreme that they name: Call the classes c with the same value of c // 4 the classes of one owner. In each aligned block of 64 rows at most 2 particles name the classes of one owner, and one owner receives exactly 2 from every block. Every class is named by some particle.
All inputs are finite; a program needn't handle non-finite values.
Results may differ from the reference program's by a relative error of at most 0.0003.
Values may be sent and summed in bfloat16 or wider, within the bound.
No kernel may reach another device: no remote copies, remote signals or barrier semaphores. Data moves between devices by JAX's collectives and lax.ppermute only.
A program may use at most 128 MiB of HBM per device.

```python
import math
import jax
import jax.numpy as jnp
from jax import lax

RADII = 48
ANGLES = 72
CLS_DEV = 2
P_LOOP = 128
CAP = 2
CLASSES = 256
PARTICLES = 8192
N_LOOP = 64
N_GRP = 2


def planted_signs(key):
    base_key = jax.random.fold_in(key, 4242)
    signs = jnp.where(jax.random.bernoulli(base_key, 0.5, (2, RADII, ANGLES)), 1.0, -1.0).astype(jnp.float32)
    lower_mask = (jnp.arange(RADII) < RADII // 2).astype(jnp.float32)[:, None]
    return (signs[0] * lower_mask, signs[1] * (1.0 - lower_mask))


def draw_references(key, part):
    flat_len = RADII * ANGLES
    values = jnp.clip(jax.random.normal(jax.random.fold_in(key, 32), (CLASSES, flat_len), jnp.float32), -6.0, 6.0)
    lower_cycle, upper_cycle = planted_signs(key)
    values = values.at[0].set(lower_cycle.reshape(-1)).at[1].set(upper_cycle.reshape(-1))
    return values.astype(jnp.bfloat16)


def plant_rows(key, values, row_count, flat_len):
    planted = jax.random.randint(jax.random.fold_in(key, 23), (row_count,), 0, 32) == 0
    target = 150.0 + 50.0 * jax.random.randint(jax.random.fold_in(key, 24), (row_count,), 0, 4).astype(jnp.float32)
    spacing = jax.random.uniform(jax.random.fold_in(key, 25), (row_count,), jnp.float32, 1.0, 3.0)
    per_unit = 2.0 / math.sqrt(flat_len) * (RADII // 2) * ANGLES
    lower_cycle, upper_cycle = planted_signs(key)
    angle_grid = jnp.arange(ANGLES, dtype=jnp.int32)
    first_turn = jax.random.randint(jax.random.fold_in(key, 26), (row_count, 1), 0, ANGLES)
    second_turn = jax.random.randint(jax.random.fold_in(key, 27), (row_count, 1), 0, ANGLES)
    lower_rolled = jnp.take(lower_cycle, (angle_grid[None, :] + first_turn) % ANGLES, axis=1)
    upper_rolled = jnp.take(upper_cycle, (angle_grid[None, :] + second_turn) % ANGLES, axis=1)
    mixed = (target / per_unit)[None, :, None] * lower_rolled + ((target - spacing) / per_unit)[None, :, None] * upper_rolled
    mixed = jnp.transpose(mixed, (1, 0, 2)).reshape(row_count, flat_len)
    return jnp.where(planted[:, None], mixed, values)


def draw_particles(key, part):
    row_count = P_LOOP * N_LOOP
    flat_len = RADII * ANGLES
    values = jnp.clip(jax.random.normal(jax.random.fold_in(key, 28), (row_count, flat_len), jnp.float32), -6.0, 6.0)
    values = plant_rows(key, values, row_count, flat_len)
    return values.astype(jnp.bfloat16)


def draw_classes(key, part):
    half_rows = P_LOOP // 2
    owner_count = N_LOOP
    per_owner = CLS_DEV * N_GRP
    slot_count = owner_count * CAP
    ranking = jax.random.permutation(jax.random.fold_in(key, 11), owner_count)
    busiest = jnp.argmin(ranking)
    offset = jax.random.randint(jax.random.fold_in(key, 12), (), 0, owner_count)
    slot_index = jnp.arange(slot_count, dtype=jnp.int32)
    owner_of = slot_index // CAP
    lane_of = slot_index % CAP

    def one_block(block_index):
        block_key = jax.random.fold_in(key, 1000 + block_index)
        jitter = jax.random.randint(jax.random.fold_in(block_key, 1), (slot_count,), 0, 512)
        priority = 1024 + jitter + ranking[owner_of] * 512 // owner_count
        priority = jnp.where(owner_of == busiest, lane_of, priority)
        position = block_index % owner_count
        half_index = block_index // owner_count
        forced_member = jnp.zeros((slot_count,), jnp.int32) - 1
        for member in range(CLS_DEV):
            target_owner = (position + member + offset) % owner_count
            marked = (owner_of == target_owner) & (lane_of == 0)
            priority = jnp.where(marked, CAP + member, priority)
            forced_member = jnp.where(marked, half_index * CLS_DEV + member, forced_member)
        ordering = jnp.argsort(priority * slot_count + slot_index)
        chosen = ordering[:half_rows]
        random_member = jax.random.randint(jax.random.fold_in(block_key, 2), (half_rows,), 0, per_owner)
        picked_forced = forced_member[chosen]
        member_of = jnp.where(picked_forced >= 0, picked_forced, random_member)
        picked = owner_of[chosen] * per_owner + member_of
        shuffle = jax.random.permutation(jax.random.fold_in(block_key, 3), half_rows)
        return picked[shuffle]
    blocks = jax.vmap(one_block)(jnp.arange(N_LOOP * N_GRP, dtype=jnp.int32))
    return blocks.reshape(-1).astype(jnp.int32)


def set_ends(array, own_key, low, high):
    place = [jax.random.randint(jax.random.fold_in(own_key, axis), (), 0, length) for axis, length in enumerate(array.shape)]
    longest = array.shape.index(max(array.shape))
    neighbour = place[:longest] + [(place[longest] + 1) % array.shape[longest]] + place[longest + 1:]
    return array.at[tuple(place)].set(low).at[tuple(neighbour)].set(high)


def setup_inputs(seed: int = 0) -> dict:
    splits = jax.random.split(jax.random.key(seed), 6)
    particles = draw_particles(jax.random.fold_in(splits[5], 71), 0)
    references = draw_references(jax.random.fold_in(splits[5], 71), 0)
    classes = draw_classes(jax.random.fold_in(splits[5], 71), 0)
    angles = set_ends(jax.random.randint(splits[3], (PARTICLES,), 0, ANGLES), jax.random.fold_in(splits[3], 1), 0, ANGLES - 1).astype(jnp.int32)
    weights = set_ends(jax.random.randint(splits[4], (PARTICLES,), 1, 5), jax.random.fold_in(splits[4], 1), 1, 4).astype(jnp.int32)
    return {"particles": particles, "references": references, "classes": classes, "angles": angles, "weights": weights}


score_factor = 2.0

def turned_rows(ref_block, radius_count, angle_count):
    block_rows = ref_block.shape[0]
    polar_rows = ref_block.reshape(block_rows, radius_count, angle_count)
    angle_grid = jnp.arange(angle_count, dtype=jnp.int32)
    source_index = ((angle_grid[:, None] + angle_grid[None, :]) % angle_count).astype(jnp.int32)
    rotated = jnp.take(polar_rows, source_index, axis=2)
    rotated = jnp.transpose(rotated, (0, 2, 1, 3))
    return rotated.reshape(block_rows * angle_count, radius_count * angle_count)

def reference(particles, references, classes, angles, weights):
    flat_len = RADII * ANGLES
    score_scale = score_factor / math.sqrt(flat_len)
    group_size = CLS_DEV * N_GRP
    ref_groups = references.reshape(CLASSES // group_size, group_size, flat_len)
    row_count = particles.shape[0]

    def advance(running, ref_block):
        highest, summed = running
        rotated = turned_rows(ref_block, RADII, ANGLES)
        scores = lax.dot_general(particles, rotated, (((1,), (1,)), ((), ())), preferred_element_type=jnp.float32) * score_scale
        new_max = jnp.maximum(highest, lax.optimization_barrier(jnp.max(scores, axis=1)))
        summed = summed * jnp.exp(highest - new_max) + lax.optimization_barrier(jnp.sum(jnp.exp(scores - new_max[:, None]), axis=1))
        return ((new_max, summed), None)
    starting = (jnp.full((row_count,), -jnp.inf, jnp.float32), jnp.zeros((row_count,), jnp.float32))
    (highest, summed), _ = lax.scan(advance, starting, ref_groups)
    log_evidence = highest + jnp.log(summed)
    polar_rows = particles.reshape(row_count, RADII, ANGLES).astype(jnp.float32)
    source_angle = (jnp.arange(ANGLES, dtype=jnp.int32)[None, :] - angles[:, None]) % ANGLES
    aligned = jnp.take_along_axis(polar_rows, source_angle.astype(jnp.int32)[:, None, :], axis=2).reshape(row_count, flat_len)
    weighted = (jnp.arange(CLASSES, dtype=jnp.int32)[:, None] == classes[None, :]).astype(jnp.float32) * weights.astype(jnp.float32)[None, :]
    class_sums = jnp.dot(weighted, aligned, precision=lax.Precision.HIGHEST, preferred_element_type=jnp.float32)
    class_weight = lax.optimization_barrier(jnp.sum(weighted, axis=1))
    class_average = class_sums / class_weight[:, None]
    return (log_evidence, class_average)
```

```python
import functools
import math

import jax
import jax.numpy as jnp
from jax import lax
from jax.experimental import pallas as pl
from jax.experimental.pallas import tpu as pltpu
from jax.sharding import PartitionSpec as P

RADII = 48
ANGLES = 72


score_factor = 2.0


def angle_major(rows):
    count = rows.shape[0]
    return rows.reshape(count, RADII, ANGLES).transpose(0, 2, 1).reshape(count, RADII * ANGLES)


def score_kernel(p_ref, r_ref, max_ref, sum_ref, s_scr, *, scale):
    flat_len = p_ref.shape[1]
    images = p_ref[...]

    def shift_scores(s, carry):
        start = pl.multiple_of(s * RADII, 16)
        turned = r_ref[pl.ds(start, flat_len), :]
        scores = jnp.dot(images, turned, preferred_element_type=jnp.float32) * scale
        s_scr[s] = scores
        return jnp.maximum(carry, scores)

    first = jnp.full(s_scr.shape[1:], -jnp.inf, jnp.float32)
    lane_max = lax.fori_loop(0, ANGLES, shift_scores, first)
    highest = jnp.max(lane_max, axis=1, keepdims=True)

    def shift_sum(s, carry):
        return carry + jnp.exp(s_scr[s] - highest)

    lane_sum = lax.fori_loop(0, ANGLES, shift_sum, jnp.zeros(s_scr.shape[1:], jnp.float32))
    max_ref[...] = highest
    sum_ref[...] = jnp.sum(lane_sum, axis=1, keepdims=True)


def score_all(images, gathered):
    row_count, flat_len = images.shape
    ref_count = gathered.shape[0]
    scale = score_factor / math.sqrt(flat_len)
    lhs = angle_major(images)
    rhs = angle_major(gathered).T
    rhs = jnp.concatenate([rhs, rhs], axis=0)
    highest, summed = pl.pallas_call(
        functools.partial(score_kernel, scale=scale),
        out_shape=(
            jax.ShapeDtypeStruct((row_count, 1), jnp.float32),
            jax.ShapeDtypeStruct((row_count, 1), jnp.float32),
        ),
        scratch_shapes=[pltpu.VMEM((ANGLES, row_count, ref_count), jnp.float32)],
    )(lhs, rhs)
    return highest[:, 0], summed[:, 0]


def local(particles, references, classes, angles, weights):
    row_count, flat_len = particles.shape
    grp_size = lax.axis_size("grp")
    half_rows = row_count // grp_size
    grp_index = lax.axis_index("grp")
    own_rows = lax.dynamic_slice_in_dim(particles, grp_index * half_rows, half_rows, 0)
    gathered = lax.all_gather(references, "loop", axis=0, tiled=True)
    highest, summed = score_all(particles, gathered)
    joint_max = lax.pmax(highest, "grp")
    summed = lax.psum(summed * jnp.exp(highest - joint_max), "grp")
    highest = joint_max
    highest = lax.dynamic_slice_in_dim(highest, grp_index * half_rows, half_rows, 0)
    summed = lax.dynamic_slice_in_dim(summed, grp_index * half_rows, half_rows, 0)
    log_evidence = highest + jnp.log(summed)
    owner_count = lax.axis_size("loop")
    per_owner = references.shape[0] * grp_size
    capacity = max(2, row_count // owner_count)
    slot_count = owner_count * capacity
    owner_of = classes // per_owner
    member_of = classes % per_owner
    owner_hits = (owner_of[:, None] == jnp.arange(owner_count, dtype=jnp.int32)[None, :]).astype(
        jnp.int32
    )
    earlier = jnp.cumsum(owner_hits, axis=0) - owner_hits
    slot_index = jnp.sum(earlier * owner_hits, axis=1)
    target_slot = owner_of * capacity + slot_index
    placement = (jnp.arange(slot_count, dtype=jnp.int32)[:, None] == target_slot[None, :]).astype(
        jnp.bfloat16
    )
    outgoing = jnp.dot(placement, own_rows, preferred_element_type=jnp.float32).astype(jnp.bfloat16)
    outgoing = outgoing.reshape(owner_count, capacity, flat_len)
    labels = jnp.stack([member_of, angles, weights], axis=1).astype(jnp.bfloat16)
    labels_out = jnp.dot(placement, labels, preferred_element_type=jnp.float32).astype(jnp.bfloat16)
    labels_out = labels_out.reshape(owner_count, capacity, 3)
    incoming, labels_in = (
        lax.all_to_all(outgoing, "loop", split_axis=0, concat_axis=0, tiled=True),
        lax.all_to_all(labels_out, "loop", split_axis=0, concat_axis=0, tiled=True),
    )
    images = incoming.reshape(slot_count, RADII, ANGLES)
    labels_in = labels_in.reshape(slot_count, 3).astype(jnp.float32)
    member_in = labels_in[:, 0]
    rotation = labels_in[:, 1]
    weight_of = labels_in[:, 2]
    angle_grid = jnp.arange(ANGLES, dtype=jnp.float32)
    source_angle = jnp.mod(angle_grid[None, :] - rotation[:, None], float(ANGLES))
    rotator = (angle_grid[None, :, None] == source_angle[:, None, :]).astype(jnp.bfloat16)
    aligned = jnp.einsum("srt,stf->srf", images, rotator, preferred_element_type=jnp.float32)
    aligned = aligned.astype(jnp.bfloat16).reshape(slot_count, flat_len)
    member_grid = jnp.arange(per_owner, dtype=jnp.float32)
    weighted = (
        (member_grid[:, None] == member_in[None, :]).astype(jnp.float32) * weight_of[None, :]
    ).astype(jnp.bfloat16)
    partial_sums = jnp.dot(weighted, aligned, preferred_element_type=jnp.float32)
    partial_weight = jnp.sum(weighted.astype(jnp.float32), axis=1)
    class_sums, class_weight = (
        lax.psum_scatter(partial_sums, "grp", scatter_dimension=0, tiled=True),
        lax.psum_scatter(partial_weight, "grp", scatter_dimension=0, tiled=True),
    )
    class_average = class_sums / class_weight[:, None]
    return (log_evidence, class_average)


def solution(mesh):
    return jax.shard_map(
        local,
        mesh=mesh,
        in_specs=(
            P("loop", None),
            P(("loop", "grp"), None),
            P(("loop", "grp")),
            P(("loop", "grp")),
            P(("loop", "grp")),
        ),
        out_specs=(P(("loop", "grp")), P(("loop", "grp"), None)),
        check_vma=False,
    )
```

```python
import functools
import math

import jax
import jax.numpy as jnp
from jax import lax
from jax.experimental import pallas as pl
from jax.experimental.pallas import tpu as pltpu
from jax.sharding import PartitionSpec as P

RADII = 48
ANGLES = 72


score_factor = 2.0


def angle_major(rows):
    count = rows.shape[0]
    return rows.reshape(count, RADII, ANGLES).transpose(0, 2, 1).reshape(count, RADII * ANGLES)


def score_kernel(p_ref, r_ref, max_ref, sum_ref, s_scr, *, scale):
    flat_len = p_ref.shape[1]
    images = p_ref[...]

    def shift_scores(s, carry):
        start = pl.multiple_of(s * RADII, 16)
        turned = r_ref[pl.ds(start, flat_len), :]
        scores = jnp.dot(images, turned, preferred_element_type=jnp.float32) * scale
        s_scr[s] = scores
        return jnp.maximum(carry, scores)

    first = jnp.full(s_scr.shape[1:], -jnp.inf, jnp.float32)
    lane_max = lax.fori_loop(0, ANGLES, shift_scores, first)
    highest = jnp.max(lane_max, axis=1, keepdims=True)

    def shift_sum(s, carry):
        return carry + jnp.exp(s_scr[s] - highest)

    lane_sum = lax.fori_loop(0, ANGLES, shift_sum, jnp.zeros(s_scr.shape[1:], jnp.float32))
    max_ref[...] = highest
    sum_ref[...] = jnp.sum(lane_sum, axis=1, keepdims=True)


def score_all(images, gathered):
    row_count, flat_len = images.shape
    ref_count = gathered.shape[0]
    scale = score_factor / math.sqrt(flat_len)
    lhs = angle_major(images)
    rhs = angle_major(gathered).T
    rhs = jnp.concatenate([rhs, rhs], axis=0)
    highest, summed = pl.pallas_call(
        functools.partial(score_kernel, scale=scale),
        out_shape=(
            jax.ShapeDtypeStruct((row_count, 1), jnp.float32),
            jax.ShapeDtypeStruct((row_count, 1), jnp.float32),
        ),
        scratch_shapes=[pltpu.VMEM((ANGLES, row_count, ref_count), jnp.float32)],
    )(lhs, rhs)
    return highest[:, 0], summed[:, 0]


def ring_factors(count):
    factors = []
    while count > 1:
        factor = 4 if count % 4 == 0 else count
        factors.append(factor)
        count //= factor
    return factors


def staged_gather(rows, axis):
    count = lax.axis_size(axis)
    stride = 1
    for factor in ring_factors(count):
        parts = [rows]
        for step in range(1, factor):
            pairs = []
            for source in range(count):
                digit = (source // stride) % factor
                pairs.append((source, source + ((digit + step) % factor - digit) * stride))
            parts.append(lax.ppermute(rows, axis, pairs))
        rows = jnp.concatenate(parts, axis=0)
        stride *= factor
    return rows


def local(particles, references, classes, angles, weights):
    row_count, flat_len = particles.shape
    grp_size = lax.axis_size("grp")
    half_rows = row_count // grp_size
    grp_index = lax.axis_index("grp")
    own_rows = lax.dynamic_slice_in_dim(particles, grp_index * half_rows, half_rows, 0)
    gathered = staged_gather(references, "loop")
    highest, summed = score_all(particles, gathered)
    joint_max = lax.pmax(highest, "grp")
    summed = lax.psum(summed * jnp.exp(highest - joint_max), "grp")
    highest = joint_max
    highest = lax.dynamic_slice_in_dim(highest, grp_index * half_rows, half_rows, 0)
    summed = lax.dynamic_slice_in_dim(summed, grp_index * half_rows, half_rows, 0)
    log_evidence = highest + jnp.log(summed)
    owner_count = lax.axis_size("loop")
    per_owner = references.shape[0] * grp_size
    capacity = max(2, row_count // owner_count)
    slot_count = owner_count * capacity
    owner_of = classes // per_owner
    member_of = classes % per_owner
    owner_hits = (owner_of[:, None] == jnp.arange(owner_count, dtype=jnp.int32)[None, :]).astype(
        jnp.int32
    )
    earlier = jnp.cumsum(owner_hits, axis=0) - owner_hits
    slot_index = jnp.sum(earlier * owner_hits, axis=1)
    target_slot = owner_of * capacity + slot_index
    placement = (jnp.arange(slot_count, dtype=jnp.int32)[:, None] == target_slot[None, :]).astype(
        jnp.bfloat16
    )
    outgoing = jnp.dot(placement, own_rows, preferred_element_type=jnp.float32).astype(jnp.bfloat16)
    outgoing = outgoing.reshape(owner_count, capacity, flat_len)
    labels = jnp.stack([member_of, angles, weights], axis=1).astype(jnp.bfloat16)
    labels_out = jnp.dot(placement, labels, preferred_element_type=jnp.float32).astype(jnp.bfloat16)
    labels_out = labels_out.reshape(owner_count, capacity, 3)
    incoming, labels_in = (
        lax.all_to_all(outgoing, "loop", split_axis=0, concat_axis=0, tiled=True),
        lax.all_to_all(labels_out, "loop", split_axis=0, concat_axis=0, tiled=True),
    )
    images = incoming.reshape(slot_count, RADII, ANGLES)
    labels_in = labels_in.reshape(slot_count, 3).astype(jnp.float32)
    member_in = labels_in[:, 0]
    rotation = labels_in[:, 1]
    weight_of = labels_in[:, 2]
    angle_grid = jnp.arange(ANGLES, dtype=jnp.float32)
    source_angle = jnp.mod(angle_grid[None, :] - rotation[:, None], float(ANGLES))
    rotator = (angle_grid[None, :, None] == source_angle[:, None, :]).astype(jnp.bfloat16)
    aligned = jnp.einsum("srt,stf->srf", images, rotator, preferred_element_type=jnp.float32)
    aligned = aligned.astype(jnp.bfloat16).reshape(slot_count, flat_len)
    member_grid = jnp.arange(per_owner, dtype=jnp.float32)
    weighted = (
        (member_grid[:, None] == member_in[None, :]).astype(jnp.float32) * weight_of[None, :]
    ).astype(jnp.bfloat16)
    partial_sums = jnp.dot(weighted, aligned, preferred_element_type=jnp.float32)
    partial_weight = jnp.sum(weighted.astype(jnp.float32), axis=1)
    class_sums, class_weight = (
        lax.psum_scatter(partial_sums, "grp", scatter_dimension=0, tiled=True),
        lax.psum_scatter(partial_weight, "grp", scatter_dimension=0, tiled=True),
    )
    class_average = class_sums / class_weight[:, None]
    return (log_evidence, class_average)


def solution(mesh):
    return jax.shard_map(
        local,
        mesh=mesh,
        in_specs=(
            P("loop", None),
            P(("loop", "grp"), None),
            P(("loop", "grp")),
            P(("loop", "grp")),
            P(("loop", "grp")),
        ),
        out_specs=(P(("loop", "grp")), P(("loop", "grp"), None)),
        check_vma=False,
    )
```

```python
import functools
import math

import jax
import jax.numpy as jnp
from jax import lax
from jax.experimental import pallas as pl
from jax.experimental.pallas import tpu as pltpu
from jax.sharding import PartitionSpec as P

RADII = 48
ANGLES = 72


score_factor = 2.0


def angle_major(rows):
    count = rows.shape[0]
    return rows.reshape(count, RADII, ANGLES).transpose(0, 2, 1).reshape(count, RADII * ANGLES)


def score_kernel(p_ref, g_ref, max_ref, sum_ref, r_scr, s_scr, *, scale):
    flat_len = p_ref.shape[1]
    columns = g_ref[...].T
    r_scr[pl.ds(0, flat_len), :] = columns
    r_scr[pl.ds(flat_len, flat_len), :] = columns
    images = p_ref[...]

    def shift_scores(s, carry):
        start = pl.multiple_of(s * RADII, 16)
        turned = r_scr[pl.ds(start, flat_len), :]
        scores = jnp.dot(images, turned, preferred_element_type=jnp.float32) * scale
        s_scr[s] = scores
        return jnp.maximum(carry, scores)

    first = jnp.full(s_scr.shape[1:], -jnp.inf, jnp.float32)
    lane_max = lax.fori_loop(0, ANGLES, shift_scores, first)
    highest = jnp.max(lane_max, axis=1, keepdims=True)

    def shift_sum(s, carry):
        return carry + jnp.exp(s_scr[s] - highest)

    lane_sum = lax.fori_loop(0, ANGLES, shift_sum, jnp.zeros(s_scr.shape[1:], jnp.float32))
    max_ref[...] = highest
    sum_ref[...] = jnp.sum(lane_sum, axis=1, keepdims=True)


def score_all(lhs, gathered):
    row_count, flat_len = lhs.shape
    ref_count = gathered.shape[0]
    scale = score_factor / math.sqrt(flat_len)
    highest, summed = pl.pallas_call(
        functools.partial(score_kernel, scale=scale),
        out_shape=(
            jax.ShapeDtypeStruct((row_count, 1), jnp.float32),
            jax.ShapeDtypeStruct((row_count, 1), jnp.float32),
        ),
        scratch_shapes=[
            pltpu.VMEM((2 * flat_len, ref_count), jnp.bfloat16),
            pltpu.VMEM((ANGLES, row_count, ref_count), jnp.float32),
        ],
    )(lhs, gathered)
    return highest[:, 0], summed[:, 0]


def ring_factors(count):
    factors = []
    while count > 1:
        factor = 4 if count % 4 == 0 else count
        factors.append(factor)
        count //= factor
    return factors


def staged_gather(rows, axis):
    count = lax.axis_size(axis)
    stride = 1
    for factor in ring_factors(count):
        parts = [rows]
        for step in range(1, factor):
            pairs = []
            for source in range(count):
                digit = (source // stride) % factor
                pairs.append((source, source + ((digit + step) % factor - digit) * stride))
            parts.append(lax.ppermute(rows, axis, pairs))
        rows = jnp.concatenate(parts, axis=0)
        stride *= factor
    return rows


def local(particles, references, classes, angles, weights):
    row_count, flat_len = particles.shape
    grp_size = lax.axis_size("grp")
    half_rows = row_count // grp_size
    grp_index = lax.axis_index("grp")
    own_rows = lax.dynamic_slice_in_dim(particles, grp_index * half_rows, half_rows, 0)
    gathered = staged_gather(angle_major(references), "loop")
    highest, summed = score_all(angle_major(particles), gathered)
    joint_max = lax.pmax(highest, "grp")
    summed = lax.psum(summed * jnp.exp(highest - joint_max), "grp")
    highest = joint_max
    highest = lax.dynamic_slice_in_dim(highest, grp_index * half_rows, half_rows, 0)
    summed = lax.dynamic_slice_in_dim(summed, grp_index * half_rows, half_rows, 0)
    log_evidence = highest + jnp.log(summed)
    owner_count = lax.axis_size("loop")
    per_owner = references.shape[0] * grp_size
    capacity = max(2, row_count // owner_count)
    slot_count = owner_count * capacity
    owner_of = classes // per_owner
    member_of = classes % per_owner
    owner_hits = (owner_of[:, None] == jnp.arange(owner_count, dtype=jnp.int32)[None, :]).astype(
        jnp.int32
    )
    earlier = jnp.cumsum(owner_hits, axis=0) - owner_hits
    slot_index = jnp.sum(earlier * owner_hits, axis=1)
    target_slot = owner_of * capacity + slot_index
    placement = (jnp.arange(slot_count, dtype=jnp.int32)[:, None] == target_slot[None, :]).astype(
        jnp.bfloat16
    )
    labels = jnp.stack([member_of, angles, weights], axis=1).astype(jnp.bfloat16)
    label_lanes = 128
    labels = jnp.pad(labels, ((0, 0), (0, label_lanes - labels.shape[1])))
    own_rows = jnp.concatenate([own_rows, labels], axis=1)
    outgoing = jnp.dot(placement, own_rows, preferred_element_type=jnp.float32).astype(jnp.bfloat16)
    outgoing = outgoing.reshape(owner_count, capacity, flat_len + label_lanes)
    incoming = lax.all_to_all(outgoing, "loop", split_axis=0, concat_axis=0, tiled=True)
    incoming = incoming.reshape(slot_count, flat_len + label_lanes)
    labels_in = incoming[:, flat_len : flat_len + 3]
    incoming = incoming[:, :flat_len]
    images = incoming.reshape(slot_count, RADII, ANGLES)
    labels_in = labels_in.reshape(slot_count, 3).astype(jnp.float32)
    member_in = labels_in[:, 0]
    rotation = labels_in[:, 1]
    weight_of = labels_in[:, 2]
    angle_grid = jnp.arange(ANGLES, dtype=jnp.float32)
    source_angle = jnp.mod(angle_grid[None, :] - rotation[:, None], float(ANGLES))
    rotator = (angle_grid[None, :, None] == source_angle[:, None, :]).astype(jnp.bfloat16)
    aligned = jnp.einsum("srt,stf->srf", images, rotator, preferred_element_type=jnp.float32)
    aligned = aligned.astype(jnp.bfloat16).reshape(slot_count, flat_len)
    member_grid = jnp.arange(per_owner, dtype=jnp.float32)
    weighted = (
        (member_grid[:, None] == member_in[None, :]).astype(jnp.float32) * weight_of[None, :]
    ).astype(jnp.bfloat16)
    partial_sums = jnp.dot(weighted, aligned, preferred_element_type=jnp.float32)
    partial_weight = jnp.sum(weighted.astype(jnp.float32), axis=1)
    class_sums, class_weight = (
        lax.psum_scatter(partial_sums, "grp", scatter_dimension=0, tiled=True),
        lax.psum_scatter(partial_weight, "grp", scatter_dimension=0, tiled=True),
    )
    class_average = class_sums / class_weight[:, None]
    return (log_evidence, class_average)


def solution(mesh):
    return jax.shard_map(
        local,
        mesh=mesh,
        in_specs=(
            P("loop", None),
            P(("loop", "grp"), None),
            P(("loop", "grp")),
            P(("loop", "grp")),
            P(("loop", "grp")),
        ),
        out_specs=(P(("loop", "grp")), P(("loop", "grp"), None)),
        check_vma=False,
    )
```

```python
import functools
import math

import jax
import jax.numpy as jnp
from jax import lax
from jax.experimental import pallas as pl
from jax.experimental.pallas import tpu as pltpu
from jax.sharding import PartitionSpec as P

RADII = 48
ANGLES = 72


score_factor = 2.0


def angle_major(rows):
    count = rows.shape[0]
    return rows.reshape(count, RADII, ANGLES).transpose(0, 2, 1).reshape(count, RADII * ANGLES)


def score_kernel(p_ref, g_ref, max_ref, sum_ref, r_scr, s_scr, *, scale):
    flat_len = p_ref.shape[1]
    columns = g_ref[...].T
    r_scr[pl.ds(0, flat_len), :] = columns
    r_scr[pl.ds(flat_len, flat_len), :] = columns
    images = p_ref[...]
    half = ANGLES // 2

    def shift_scores(s, carry):
        turned = jnp.concatenate(
            [
                r_scr[pl.ds(pl.multiple_of(s * RADII, 16), flat_len), :],
                r_scr[pl.ds(pl.multiple_of((s + half) * RADII, 16), flat_len), :],
            ],
            axis=1,
        )
        scores = jnp.dot(images, turned, preferred_element_type=jnp.float32) * scale
        s_scr[s] = scores
        return jnp.maximum(carry, scores)

    first = jnp.full(s_scr.shape[1:], -jnp.inf, jnp.float32)
    lane_max = lax.fori_loop(0, half, shift_scores, first, unroll=4)
    highest = jnp.max(lane_max.T, axis=0, keepdims=True)
    highest_col = jnp.max(lane_max, axis=1, keepdims=True)

    def shift_sum(s, carry):
        return carry + jnp.exp(s_scr[s] - highest_col)

    lane_sum = lax.fori_loop(0, half, shift_sum, jnp.zeros(s_scr.shape[1:], jnp.float32))
    max_ref[...] = highest
    sum_ref[...] = jnp.sum(lane_sum.T, axis=0, keepdims=True)


def score_all(lhs, gathered):
    row_count, flat_len = lhs.shape
    ref_count = gathered.shape[0]
    scale = score_factor / math.sqrt(flat_len)
    highest, summed = pl.pallas_call(
        functools.partial(score_kernel, scale=scale),
        out_shape=(
            jax.ShapeDtypeStruct((1, row_count), jnp.float32),
            jax.ShapeDtypeStruct((1, row_count), jnp.float32),
        ),
        scratch_shapes=[
            pltpu.VMEM((2 * flat_len, ref_count), jnp.bfloat16),
            pltpu.VMEM((ANGLES // 2, row_count, 2 * ref_count), jnp.float32),
        ],
    )(lhs, gathered)
    return highest[0], summed[0]


def ring_factors(count):
    factors = []
    while count > 1:
        factor = 4 if count % 4 == 0 else count
        factors.append(factor)
        count //= factor
    return factors


def staged_gather(rows, axis):
    count = lax.axis_size(axis)
    stride = 1
    for factor in ring_factors(count):
        parts = [rows]
        for step in range(1, factor):
            pairs = []
            for source in range(count):
                digit = (source // stride) % factor
                pairs.append((source, source + ((digit + step) % factor - digit) * stride))
            parts.append(lax.ppermute(rows, axis, pairs))
        rows = jnp.concatenate(parts, axis=0)
        stride *= factor
    return rows


def local(particles, references, classes, angles, weights):
    row_count, flat_len = particles.shape
    grp_size = lax.axis_size("grp")
    half_rows = row_count // grp_size
    grp_index = lax.axis_index("grp")
    own_rows = lax.dynamic_slice_in_dim(particles, grp_index * half_rows, half_rows, 0)
    gathered = staged_gather(angle_major(references), "loop")
    highest, summed = score_all(angle_major(particles), gathered)
    stats = lax.all_gather(jnp.stack([highest, summed], axis=0), "grp", axis=0, tiled=False)
    stats = lax.dynamic_slice_in_dim(stats, grp_index * half_rows, half_rows, 2)
    highest = jnp.max(stats[:, 0], axis=0)
    summed = jnp.sum(stats[:, 1] * jnp.exp(stats[:, 0] - highest[None, :]), axis=0)
    log_evidence = highest + jnp.log(summed)
    owner_count = lax.axis_size("loop")
    per_owner = references.shape[0] * grp_size
    capacity = max(2, row_count // owner_count)
    slot_count = owner_count * capacity
    owner_of = classes // per_owner
    member_of = classes % per_owner
    owner_hits = (owner_of[:, None] == jnp.arange(owner_count, dtype=jnp.int32)[None, :]).astype(
        jnp.int32
    )
    earlier = jnp.cumsum(owner_hits, axis=0) - owner_hits
    slot_index = jnp.sum(earlier * owner_hits, axis=1)
    target_slot = owner_of * capacity + slot_index
    placement = (jnp.arange(slot_count, dtype=jnp.int32)[:, None] == target_slot[None, :]).astype(
        jnp.bfloat16
    )
    labels = jnp.stack([member_of, angles, weights], axis=1).astype(jnp.bfloat16)
    label_lanes = 128
    labels = jnp.pad(labels, ((0, 0), (0, label_lanes - labels.shape[1])))
    own_rows = jnp.concatenate([own_rows, labels], axis=1)
    outgoing = jnp.dot(placement, own_rows, preferred_element_type=jnp.float32).astype(jnp.bfloat16)
    outgoing = outgoing.reshape(owner_count, capacity, flat_len + label_lanes)
    incoming = lax.all_to_all(outgoing, "loop", split_axis=0, concat_axis=0, tiled=True)
    incoming = incoming.reshape(slot_count, flat_len + label_lanes)
    labels_in = incoming[:, flat_len : flat_len + 3]
    incoming = incoming[:, :flat_len]
    images = incoming.reshape(slot_count, RADII, ANGLES)
    labels_in = labels_in.reshape(slot_count, 3).astype(jnp.float32)
    member_in = labels_in[:, 0]
    rotation = labels_in[:, 1]
    weight_of = labels_in[:, 2]
    angle_grid = jnp.arange(ANGLES, dtype=jnp.float32)
    source_angle = jnp.mod(angle_grid[None, :] - rotation[:, None], float(ANGLES))
    rotator = (angle_grid[None, :, None] == source_angle[:, None, :]).astype(jnp.bfloat16)
    aligned = jnp.einsum("srt,stf->srf", images, rotator, preferred_element_type=jnp.float32)
    aligned = aligned.astype(jnp.bfloat16).reshape(slot_count, flat_len)
    member_grid = jnp.arange(per_owner, dtype=jnp.float32)
    weighted = (
        (member_grid[:, None] == member_in[None, :]).astype(jnp.float32) * weight_of[None, :]
    ).astype(jnp.bfloat16)
    partial_sums = jnp.dot(weighted, aligned, preferred_element_type=jnp.float32)
    partial_weight = jnp.sum(weighted.astype(jnp.float32), axis=1)
    class_sums, class_weight = (
        lax.psum_scatter(partial_sums, "grp", scatter_dimension=0, tiled=True),
        lax.psum_scatter(partial_weight, "grp", scatter_dimension=0, tiled=True),
    )
    class_average = class_sums / class_weight[:, None]
    return (log_evidence, class_average)


def solution(mesh):
    return jax.shard_map(
        local,
        mesh=mesh,
        in_specs=(
            P("loop", None),
            P(("loop", "grp"), None),
            P(("loop", "grp")),
            P(("loop", "grp")),
            P(("loop", "grp")),
        ),
        out_specs=(P(("loop", "grp")), P(("loop", "grp"), None)),
        check_vma=False,
    )
```

```python
import functools
import math

import jax
import jax.numpy as jnp
from jax import lax
from jax.experimental import pallas as pl
from jax.experimental.pallas import tpu as pltpu
from jax.sharding import PartitionSpec as P

RADII = 48
ANGLES = 72


score_factor = 2.0


def angle_major(rows):
    count = rows.shape[0]
    return rows.reshape(count, RADII, ANGLES).transpose(0, 2, 1).reshape(count, RADII * ANGLES)


def score_kernel(*refs, scale):
    p_ref, piece_refs = refs[0], refs[1:-4]
    max_ref, sum_ref, r_scr, s_scr = refs[-4:]
    flat_len = p_ref.shape[1]
    columns = jnp.concatenate([piece[...] for piece in piece_refs], axis=0).T
    r_scr[pl.ds(0, flat_len), :] = columns
    r_scr[pl.ds(flat_len, flat_len), :] = columns
    images = p_ref[...]
    half = ANGLES // 2

    def shift_scores(s, carry):
        turned = jnp.concatenate(
            [
                r_scr[pl.ds(pl.multiple_of(s * RADII, 16), flat_len), :],
                r_scr[pl.ds(pl.multiple_of((s + half) * RADII, 16), flat_len), :],
            ],
            axis=1,
        )
        scores = jnp.dot(images, turned, preferred_element_type=jnp.float32) * scale
        s_scr[s] = scores
        return jnp.maximum(carry, scores)

    first = jnp.full(s_scr.shape[1:], -jnp.inf, jnp.float32)
    lane_max = lax.fori_loop(0, half, shift_scores, first, unroll=4)
    highest = jnp.max(lane_max.T, axis=0, keepdims=True)
    highest_col = jnp.max(lane_max, axis=1, keepdims=True)

    def shift_sum(s, carry):
        return carry + jnp.exp(s_scr[s] - highest_col)

    lane_sum = lax.fori_loop(0, half, shift_sum, jnp.zeros(s_scr.shape[1:], jnp.float32))
    max_ref[...] = highest
    sum_ref[...] = jnp.sum(lane_sum.T, axis=0, keepdims=True)


def score_all(lhs, pieces):
    row_count, flat_len = lhs.shape
    ref_count = sum(piece.shape[0] for piece in pieces)
    scale = score_factor / math.sqrt(flat_len)
    highest, summed = pl.pallas_call(
        functools.partial(score_kernel, scale=scale),
        out_shape=(
            jax.ShapeDtypeStruct((1, row_count), jnp.float32),
            jax.ShapeDtypeStruct((1, row_count), jnp.float32),
        ),
        scratch_shapes=[
            pltpu.VMEM((2 * flat_len, ref_count), jnp.bfloat16),
            pltpu.VMEM((ANGLES // 2, row_count, 2 * ref_count), jnp.float32),
        ],
    )(lhs, *pieces)
    return highest[0], summed[0]


def ring_factors(count):
    factors = []
    while count > 1:
        factor = 4 if count % 4 == 0 else count
        factors.append(factor)
        count //= factor
    return factors


def staged_gather(rows, axis):
    count = lax.axis_size(axis)
    stride = 1
    for factor in ring_factors(count):
        parts = [rows]
        for step in range(1, factor):
            pairs = []
            for source in range(count):
                digit = (source // stride) % factor
                pairs.append((source, source + ((digit + step) % factor - digit) * stride))
            parts.append(lax.ppermute(rows, axis, pairs))
        rows = jnp.concatenate(parts, axis=0)
        stride *= factor
    return parts


def local(particles, references, classes, angles, weights):
    row_count, flat_len = particles.shape
    grp_size = lax.axis_size("grp")
    half_rows = row_count // grp_size
    grp_index = lax.axis_index("grp")
    own_rows = lax.dynamic_slice_in_dim(particles, grp_index * half_rows, half_rows, 0)
    pieces = staged_gather(angle_major(references), "loop")
    owner_count = lax.axis_size("loop")
    per_owner = references.shape[0] * grp_size
    capacity = max(2, row_count // owner_count)
    slot_count = owner_count * capacity
    owner_of = classes // per_owner
    member_of = classes % per_owner
    owner_hits = (owner_of[:, None] == jnp.arange(owner_count, dtype=jnp.int32)[None, :]).astype(
        jnp.int32
    )
    earlier = jnp.cumsum(owner_hits, axis=0) - owner_hits
    slot_index = jnp.sum(earlier * owner_hits, axis=1)
    target_slot = owner_of * capacity + slot_index
    placement = (jnp.arange(slot_count, dtype=jnp.int32)[:, None] == target_slot[None, :]).astype(
        jnp.bfloat16
    )
    labels = jnp.stack([member_of, angles, weights], axis=1).astype(jnp.bfloat16)
    label_lanes = 128
    labels = jnp.pad(labels, ((0, 0), (0, label_lanes - labels.shape[1])))
    own_rows = jnp.concatenate([own_rows, labels], axis=1)
    outgoing = jnp.dot(placement, own_rows, preferred_element_type=jnp.float32).astype(jnp.bfloat16)
    outgoing = outgoing.reshape(owner_count, capacity, flat_len + label_lanes)
    incoming = lax.all_to_all(outgoing, "loop", split_axis=0, concat_axis=0, tiled=True)
    incoming = incoming.reshape(slot_count, flat_len + label_lanes)
    labels_in = incoming[:, flat_len : flat_len + 3]
    incoming = incoming[:, :flat_len]
    images = incoming.reshape(slot_count, RADII, ANGLES)
    labels_in = labels_in.reshape(slot_count, 3).astype(jnp.float32)
    member_in = labels_in[:, 0]
    rotation = labels_in[:, 1]
    weight_of = labels_in[:, 2]
    angle_grid = jnp.arange(ANGLES, dtype=jnp.float32)
    source_angle = jnp.mod(angle_grid[None, :] - rotation[:, None], float(ANGLES))
    rotator = (angle_grid[None, :, None] == source_angle[:, None, :]).astype(jnp.bfloat16)
    aligned = jnp.einsum("srt,stf->srf", images, rotator, preferred_element_type=jnp.float32)
    aligned = aligned.astype(jnp.bfloat16).reshape(slot_count, flat_len)
    member_grid = jnp.arange(per_owner, dtype=jnp.float32)
    weighted = (
        (member_grid[:, None] == member_in[None, :]).astype(jnp.float32) * weight_of[None, :]
    ).astype(jnp.bfloat16)
    partial_sums = jnp.dot(weighted, aligned, preferred_element_type=jnp.float32)
    partial_weight = jnp.sum(weighted.astype(jnp.float32), axis=1)
    class_sums, class_weight = (
        lax.psum_scatter(partial_sums, "grp", scatter_dimension=0, tiled=True),
        lax.psum_scatter(partial_weight, "grp", scatter_dimension=0, tiled=True),
    )
    class_average = class_sums / class_weight[:, None]
    class_average, pieces = lax.optimization_barrier((class_average, pieces))
    highest, summed = score_all(angle_major(particles), pieces)
    stats = lax.all_gather(jnp.stack([highest, summed], axis=0), "grp", axis=0, tiled=False)
    stats = lax.dynamic_slice_in_dim(stats, grp_index * half_rows, half_rows, 2)
    highest = jnp.max(stats[:, 0], axis=0)
    summed = jnp.sum(stats[:, 1] * jnp.exp(stats[:, 0] - highest[None, :]), axis=0)
    log_evidence = highest + jnp.log(summed)
    return (log_evidence, class_average)


def solution(mesh):
    return jax.shard_map(
        local,
        mesh=mesh,
        in_specs=(
            P("loop", None),
            P(("loop", "grp"), None),
            P(("loop", "grp")),
            P(("loop", "grp")),
            P(("loop", "grp")),
        ),
        out_specs=(P(("loop", "grp")), P(("loop", "grp"), None)),
        check_vma=False,
    )
```

```python
import functools
import math

import jax
import jax.numpy as jnp
from jax import lax
from jax.experimental import pallas as pl
from jax.experimental.pallas import tpu as pltpu
from jax.sharding import PartitionSpec as P

RADII = 48
ANGLES = 72


score_factor = 2.0


def angle_major(rows):
    count = rows.shape[0]
    return rows.reshape(count, RADII, ANGLES).transpose(0, 2, 1).reshape(count, RADII * ANGLES)


def score_kernel(*refs, scale):
    p_ref, piece_refs = refs[0], refs[1:-4]
    max_ref, sum_ref, r_scr, s_scr = refs[-4:]
    flat_len = p_ref.shape[1]
    columns = jnp.concatenate([piece[...] for piece in piece_refs], axis=0).T
    r_scr[pl.ds(0, flat_len), :] = columns
    r_scr[pl.ds(flat_len, flat_len), :] = columns
    images = p_ref[...]
    half = ANGLES // 2

    def shift_scores(s, carry):
        turned = jnp.concatenate(
            [
                r_scr[pl.ds(pl.multiple_of(s * RADII, 16), flat_len), :],
                r_scr[pl.ds(pl.multiple_of((s + half) * RADII, 16), flat_len), :],
            ],
            axis=1,
        )
        scores = jnp.dot(images, turned, preferred_element_type=jnp.float32) * scale
        s_scr[s] = scores
        return jnp.maximum(carry, scores)

    first = jnp.full(s_scr.shape[1:], -jnp.inf, jnp.float32)
    lane_max = lax.fori_loop(0, half, shift_scores, first, unroll=9)
    highest = jnp.max(lane_max.T, axis=0, keepdims=True)
    highest_col = jnp.max(lane_max, axis=1, keepdims=True)

    def shift_sum(s, carry):
        return carry + jnp.exp(s_scr[s] - highest_col)

    lane_sum = lax.fori_loop(0, half, shift_sum, jnp.zeros(s_scr.shape[1:], jnp.float32), unroll=4)
    max_ref[...] = highest
    sum_ref[...] = jnp.sum(lane_sum.T, axis=0, keepdims=True)


def score_all(lhs, pieces):
    row_count, flat_len = lhs.shape
    ref_count = sum(piece.shape[0] for piece in pieces)
    scale = score_factor / math.sqrt(flat_len)
    highest, summed = pl.pallas_call(
        functools.partial(score_kernel, scale=scale),
        out_shape=(
            jax.ShapeDtypeStruct((1, row_count), jnp.float32),
            jax.ShapeDtypeStruct((1, row_count), jnp.float32),
        ),
        scratch_shapes=[
            pltpu.VMEM((2 * flat_len, ref_count), jnp.bfloat16),
            pltpu.VMEM((ANGLES // 2, row_count, 2 * ref_count), jnp.float32),
        ],
    )(lhs, *pieces)
    return highest[0], summed[0]


def ring_factors(count):
    factors = []
    while count > 1:
        factor = 4 if count % 4 == 0 else count
        factors.append(factor)
        count //= factor
    return factors


def staged_gather(rows, axis):
    count = lax.axis_size(axis)
    stride = 1
    for factor in ring_factors(count):
        parts = [rows]
        for step in range(1, factor):
            pairs = []
            for source in range(count):
                digit = (source // stride) % factor
                pairs.append((source, source + ((digit + step) % factor - digit) * stride))
            parts.append(lax.ppermute(rows, axis, pairs))
        rows = jnp.concatenate(parts, axis=0)
        stride *= factor
    return parts


def local(particles, references, classes, angles, weights):
    row_count, flat_len = particles.shape
    grp_size = lax.axis_size("grp")
    half_rows = row_count // grp_size
    grp_index = lax.axis_index("grp")
    own_rows = lax.dynamic_slice_in_dim(particles, grp_index * half_rows, half_rows, 0)
    pieces = staged_gather(angle_major(references), "loop")
    owner_count = lax.axis_size("loop")
    per_owner = references.shape[0] * grp_size
    capacity = max(2, row_count // owner_count)
    slot_count = owner_count * capacity
    owner_of = classes // per_owner
    member_of = classes % per_owner
    owner_hits = (owner_of[:, None] == jnp.arange(owner_count, dtype=jnp.int32)[None, :]).astype(
        jnp.int32
    )
    earlier = jnp.cumsum(owner_hits, axis=0) - owner_hits
    slot_index = jnp.sum(earlier * owner_hits, axis=1)
    target_slot = owner_of * capacity + slot_index
    placement = (jnp.arange(slot_count, dtype=jnp.int32)[:, None] == target_slot[None, :]).astype(
        jnp.bfloat16
    )
    labels = jnp.stack([member_of, angles, weights], axis=1).astype(jnp.bfloat16)
    label_lanes = 128
    labels = jnp.pad(labels, ((0, 0), (0, label_lanes - labels.shape[1])))
    own_rows = jnp.concatenate([own_rows, labels], axis=1)
    outgoing = jnp.dot(placement, own_rows, preferred_element_type=jnp.float32).astype(jnp.bfloat16)
    outgoing = outgoing.reshape(owner_count, capacity, flat_len + label_lanes)
    incoming = lax.all_to_all(outgoing, "loop", split_axis=0, concat_axis=0, tiled=True)
    incoming = incoming.reshape(slot_count, flat_len + label_lanes)
    labels_in = incoming[:, flat_len : flat_len + 3]
    incoming = incoming[:, :flat_len]
    images = incoming.reshape(slot_count, RADII, ANGLES)
    labels_in = labels_in.reshape(slot_count, 3).astype(jnp.float32)
    member_in = labels_in[:, 0]
    rotation = labels_in[:, 1]
    weight_of = labels_in[:, 2]
    angle_grid = jnp.arange(ANGLES, dtype=jnp.float32)
    source_angle = jnp.mod(angle_grid[None, :] - rotation[:, None], float(ANGLES))
    rotator = (angle_grid[None, :, None] == source_angle[:, None, :]).astype(jnp.bfloat16)
    aligned = jnp.einsum("srt,stf->srf", images, rotator, preferred_element_type=jnp.float32)
    aligned = aligned.astype(jnp.bfloat16).reshape(slot_count, flat_len)
    member_grid = jnp.arange(per_owner, dtype=jnp.float32)
    weighted = (
        (member_grid[:, None] == member_in[None, :]).astype(jnp.float32) * weight_of[None, :]
    ).astype(jnp.bfloat16)
    partial_sums = jnp.dot(weighted, aligned, preferred_element_type=jnp.float32)
    partial_weight = jnp.sum(weighted.astype(jnp.float32), axis=1)
    class_sums, class_weight = (
        lax.psum_scatter(partial_sums, "grp", scatter_dimension=0, tiled=True),
        lax.psum_scatter(partial_weight, "grp", scatter_dimension=0, tiled=True),
    )
    class_average = class_sums / class_weight[:, None]
    class_average, pieces = lax.optimization_barrier((class_average, pieces))
    highest, summed = score_all(angle_major(particles), pieces)
    stats = lax.all_gather(jnp.stack([highest, summed], axis=0), "grp", axis=0, tiled=False)
    stats = lax.dynamic_slice_in_dim(stats, grp_index * half_rows, half_rows, 2)
    highest = jnp.max(stats[:, 0], axis=0)
    summed = jnp.sum(stats[:, 1] * jnp.exp(stats[:, 0] - highest[None, :]), axis=0)
    log_evidence = highest + jnp.log(summed)
    return (log_evidence, class_average)


def solution(mesh):
    return jax.shard_map(
        local,
        mesh=mesh,
        in_specs=(
            P("loop", None),
            P(("loop", "grp"), None),
            P(("loop", "grp")),
            P(("loop", "grp")),
            P(("loop", "grp")),
        ),
        out_specs=(P(("loop", "grp")), P(("loop", "grp"), None)),
        check_vma=False,
    )
```

```python
import functools
import math

import jax
import jax.numpy as jnp
from jax import lax
from jax.experimental import pallas as pl
from jax.experimental.pallas import tpu as pltpu
from jax.sharding import PartitionSpec as P

RADII = 48
ANGLES = 72


score_factor = 2.0


def angle_major(rows):
    count = rows.shape[0]
    return rows.reshape(count, RADII, ANGLES).transpose(0, 2, 1).reshape(count, RADII * ANGLES)


def score_kernel(*refs, scale):
    p_ref, piece_refs = refs[0], refs[1:-4]
    max_ref, sum_ref, r_scr, s_scr = refs[-4:]
    flat_len = p_ref.shape[1]
    columns = jnp.concatenate([piece[...] for piece in piece_refs], axis=0).T
    r_scr[pl.ds(0, flat_len), :] = columns
    r_scr[pl.ds(flat_len, flat_len), :] = columns
    images = p_ref[...]
    half = ANGLES // 2

    def shift_scores(s, carry):
        turned = jnp.concatenate(
            [
                r_scr[pl.ds(pl.multiple_of(s * RADII, 16), flat_len), :],
                r_scr[pl.ds(pl.multiple_of((s + half) * RADII, 16), flat_len), :],
            ],
            axis=1,
        )
        scores = jnp.dot(images, turned, preferred_element_type=jnp.float32) * scale
        s_scr[s] = scores
        return jnp.maximum(carry, scores)

    first = jnp.full(s_scr.shape[1:], -jnp.inf, jnp.float32)
    lane_max = lax.fori_loop(0, half, shift_scores, first, unroll=9)
    highest = jnp.max(lane_max.T, axis=0, keepdims=True)
    highest_col = jnp.max(lane_max, axis=1, keepdims=True)

    def shift_sum(s, carry):
        return carry + jnp.exp(s_scr[s] - highest_col)

    lane_sum = lax.fori_loop(0, half, shift_sum, jnp.zeros(s_scr.shape[1:], jnp.float32), unroll=4)
    max_ref[...] = highest
    sum_ref[...] = jnp.sum(lane_sum.T, axis=0, keepdims=True)


def score_all(lhs, pieces):
    row_count, flat_len = lhs.shape
    ref_count = sum(piece.shape[0] for piece in pieces)
    scale = score_factor / math.sqrt(flat_len)
    highest, summed = pl.pallas_call(
        functools.partial(score_kernel, scale=scale),
        out_shape=(
            jax.ShapeDtypeStruct((1, row_count), jnp.float32),
            jax.ShapeDtypeStruct((1, row_count), jnp.float32),
        ),
        scratch_shapes=[
            pltpu.VMEM((2 * flat_len, ref_count), jnp.bfloat16),
            pltpu.VMEM((ANGLES // 2, row_count, 2 * ref_count), jnp.float32),
        ],
    )(lhs, *pieces)
    return highest[0], summed[0]


def average_kernel(w_ref, x_ref, o_ref, s_scr):
    block = o_ref.shape[0]
    s_scr[...] = jnp.dot(w_ref[...], x_ref[...], preferred_element_type=jnp.float32)
    total = s_scr[pl.ds(0, block), :]
    for angle in range(1, ANGLES):
        total = total + pltpu.roll(s_scr[pl.ds(angle * block, block), :], angle * RADII, 1)
    o_ref[...] = total


def ring_factors(count):
    factors = []
    while count > 1:
        factor = 4 if count % 4 == 0 else count
        factors.append(factor)
        count //= factor
    return factors


def staged_gather(rows, axis):
    count = lax.axis_size(axis)
    stride = 1
    for factor in ring_factors(count):
        parts = [rows]
        for step in range(1, factor):
            pairs = []
            for source in range(count):
                digit = (source // stride) % factor
                pairs.append((source, source + ((digit + step) % factor - digit) * stride))
            parts.append(lax.ppermute(rows, axis, pairs))
        rows = jnp.concatenate(parts, axis=0)
        stride *= factor
    return parts


def local(particles, references, classes, angles, weights):
    row_count, flat_len = particles.shape
    grp_size = lax.axis_size("grp")
    half_rows = row_count // grp_size
    grp_index = lax.axis_index("grp")
    pieces = staged_gather(angle_major(references), "loop")
    particle_rows = angle_major(particles)
    own_rows = lax.dynamic_slice_in_dim(particle_rows, grp_index * half_rows, half_rows, 0)
    owner_count = lax.axis_size("loop")
    per_owner = references.shape[0] * grp_size
    capacity = max(2, row_count // owner_count)
    slot_count = owner_count * capacity
    owner_of = classes // per_owner
    member_of = classes % per_owner
    owner_hits = (owner_of[:, None] == jnp.arange(owner_count, dtype=jnp.int32)[None, :]).astype(
        jnp.int32
    )
    earlier = jnp.cumsum(owner_hits, axis=0) - owner_hits
    slot_index = jnp.sum(earlier * owner_hits, axis=1)
    target_slot = owner_of * capacity + slot_index
    placement = (jnp.arange(slot_count, dtype=jnp.int32)[:, None] == target_slot[None, :]).astype(
        jnp.bfloat16
    )
    labels = jnp.stack([member_of, angles, weights], axis=1).astype(jnp.bfloat16)
    label_lanes = 128
    labels = jnp.pad(labels, ((0, 0), (0, label_lanes - labels.shape[1])))
    own_rows = jnp.concatenate([own_rows, labels], axis=1)
    outgoing = jnp.dot(placement, own_rows, preferred_element_type=jnp.float32).astype(jnp.bfloat16)
    outgoing = outgoing.reshape(owner_count, capacity, flat_len + label_lanes)
    incoming = lax.all_to_all(outgoing, "loop", split_axis=0, concat_axis=0, tiled=True)
    incoming = incoming.reshape(slot_count, flat_len + label_lanes)
    labels_in = incoming[:, flat_len : flat_len + 3]
    incoming = incoming[:, :flat_len]
    labels_in = labels_in.astype(jnp.float32)
    member_in = labels_in[:, 0]
    rotation = labels_in[:, 1]
    weight_of = labels_in[:, 2]
    block = -(-per_owner // 8) * 8
    angle_grid = jnp.arange(ANGLES, dtype=jnp.float32)
    member_grid = jnp.arange(block, dtype=jnp.float32)
    chosen = (angle_grid[:, None, None] == rotation[None, None, :]) & (
        member_grid[None, :, None] == member_in[None, None, :]
    )
    by_angle = jnp.where(chosen, weight_of[None, None, :], 0.0).astype(jnp.bfloat16)
    by_angle = by_angle.reshape(ANGLES * block, slot_count)
    partial_sums = pl.pallas_call(
        average_kernel,
        out_shape=jax.ShapeDtypeStruct((block, flat_len), jnp.float32),
        scratch_shapes=[pltpu.VMEM((ANGLES * block, flat_len), jnp.float32)],
    )(by_angle, incoming)
    partial_sums = partial_sums[:per_owner].reshape(per_owner, ANGLES, RADII).transpose(0, 2, 1)
    partial_sums = partial_sums.reshape(per_owner, flat_len)
    weighted = (member_grid[:per_owner, None] == member_in[None, :]).astype(jnp.float32) * weight_of[None, :]
    partial_weight = jnp.sum(weighted, axis=1)
    class_sums, class_weight = (
        lax.psum_scatter(partial_sums, "grp", scatter_dimension=0, tiled=True),
        lax.psum_scatter(partial_weight, "grp", scatter_dimension=0, tiled=True),
    )
    class_average = class_sums / class_weight[:, None]
    class_average, pieces = lax.optimization_barrier((class_average, pieces))
    highest, summed = score_all(particle_rows, pieces)
    stats = lax.all_gather(jnp.stack([highest, summed], axis=0), "grp", axis=0, tiled=False)
    stats = lax.dynamic_slice_in_dim(stats, grp_index * half_rows, half_rows, 2)
    highest = jnp.max(stats[:, 0], axis=0)
    summed = jnp.sum(stats[:, 1] * jnp.exp(stats[:, 0] - highest[None, :]), axis=0)
    log_evidence = highest + jnp.log(summed)
    return (log_evidence, class_average)


def solution(mesh):
    return jax.shard_map(
        local,
        mesh=mesh,
        in_specs=(
            P("loop", None),
            P(("loop", "grp"), None),
            P(("loop", "grp")),
            P(("loop", "grp")),
            P(("loop", "grp")),
        ),
        out_specs=(P(("loop", "grp")), P(("loop", "grp"), None)),
        check_vma=False,
    )
```

```python
import functools
import math

import jax
import jax.numpy as jnp
from jax import lax
from jax.experimental import pallas as pl
from jax.experimental.pallas import tpu as pltpu
from jax.sharding import PartitionSpec as P

RADII = 48
ANGLES = 72


score_factor = 2.0


def angle_major(rows):
    count = rows.shape[0]
    return rows.reshape(count, RADII, ANGLES).transpose(0, 2, 1).reshape(count, RADII * ANGLES)


def score_kernel(*refs, scale):
    p_ref, piece_refs = refs[0], refs[1:-4]
    max_ref, sum_ref, r_scr, s_scr = refs[-4:]
    flat_len = p_ref.shape[1]
    columns = jnp.concatenate([piece[...] for piece in piece_refs], axis=0).T
    r_scr[pl.ds(0, flat_len), :] = columns
    r_scr[pl.ds(flat_len, flat_len), :] = columns
    images = p_ref[...]
    half = ANGLES // 2

    def shift_scores(s, carry):
        turned = jnp.concatenate(
            [
                r_scr[pl.ds(pl.multiple_of(s * RADII, 16), flat_len), :],
                r_scr[pl.ds(pl.multiple_of((s + half) * RADII, 16), flat_len), :],
            ],
            axis=1,
        )
        scores = jnp.dot(images, turned, preferred_element_type=jnp.float32) * scale
        s_scr[s] = scores
        return jnp.maximum(carry, scores)

    first = jnp.full(s_scr.shape[1:], -jnp.inf, jnp.float32)
    lane_max = lax.fori_loop(0, half, shift_scores, first, unroll=9)
    highest = jnp.max(lane_max.T, axis=0, keepdims=True)
    highest_col = jnp.max(lane_max, axis=1, keepdims=True)

    def shift_sum(s, carry):
        return carry + jnp.exp(s_scr[s] - highest_col)

    lane_sum = lax.fori_loop(0, half, shift_sum, jnp.zeros(s_scr.shape[1:], jnp.float32), unroll=4)
    max_ref[...] = highest
    sum_ref[...] = jnp.sum(lane_sum.T, axis=0, keepdims=True)


def score_all(lhs, pieces):
    row_count, flat_len = lhs.shape
    ref_count = sum(piece.shape[0] for piece in pieces)
    scale = score_factor / math.sqrt(flat_len)
    highest, summed = pl.pallas_call(
        functools.partial(score_kernel, scale=scale),
        out_shape=(
            jax.ShapeDtypeStruct((1, row_count), jnp.float32),
            jax.ShapeDtypeStruct((1, row_count), jnp.float32),
        ),
        scratch_shapes=[
            pltpu.VMEM((2 * flat_len, ref_count), jnp.bfloat16),
            pltpu.VMEM((ANGLES // 2, row_count, 2 * ref_count), jnp.float32),
        ],
    )(lhs, *pieces)
    return highest[0], summed[0]


def average_kernel(w_ref, x_ref, o_ref, s_scr):
    block = o_ref.shape[0]
    flat_len = o_ref.shape[1]
    s_scr[...] = jnp.dot(w_ref[...], x_ref[:, :flat_len], preferred_element_type=jnp.float32)
    step = 8
    total = None
    for part in range(step):
        partial = None
        for whole in range(ANGLES // step):
            angle = whole * step + part
            rows = s_scr[pl.ds(angle * block, block), :]
            if whole:
                rows = pltpu.roll(rows, whole * step * RADII, 1)
            partial = rows if partial is None else partial + rows
        if part:
            partial = pltpu.roll(partial, part * RADII, 1)
        total = partial if total is None else total + partial
    o_ref[...] = total


def ring_factors(count):
    factors = []
    while count > 1:
        factor = 4 if count % 4 == 0 else count
        factors.append(factor)
        count //= factor
    return factors


def staged_gather(rows, axis):
    count = lax.axis_size(axis)
    stride = 1
    for factor in ring_factors(count):
        parts = [rows]
        for step in range(1, factor):
            pairs = []
            for source in range(count):
                digit = (source // stride) % factor
                pairs.append((source, source + ((digit + step) % factor - digit) * stride))
            parts.append(lax.ppermute(rows, axis, pairs))
        rows = jnp.concatenate(parts, axis=0)
        stride *= factor
    return parts


def local(particles, references, classes, angles, weights):
    row_count, flat_len = particles.shape
    grp_size = lax.axis_size("grp")
    half_rows = row_count // grp_size
    grp_index = lax.axis_index("grp")
    pieces = staged_gather(angle_major(references), "loop")
    particle_rows = angle_major(particles)
    own_rows = lax.dynamic_slice_in_dim(particle_rows, grp_index * half_rows, half_rows, 0)
    owner_count = lax.axis_size("loop")
    per_owner = references.shape[0] * grp_size
    capacity = max(2, row_count // owner_count)
    slot_count = owner_count * capacity
    owner_of = classes // per_owner
    member_of = classes % per_owner
    owner_hits = (owner_of[:, None] == jnp.arange(owner_count, dtype=jnp.int32)[None, :]).astype(
        jnp.int32
    )
    earlier = jnp.cumsum(owner_hits, axis=0) - owner_hits
    slot_index = jnp.sum(earlier * owner_hits, axis=1)
    target_slot = owner_of * capacity + slot_index
    placement = (jnp.arange(slot_count, dtype=jnp.int32)[:, None] == target_slot[None, :]).astype(
        jnp.bfloat16
    )
    labels = jnp.stack([member_of, angles, weights], axis=1).astype(jnp.bfloat16)
    label_lanes = 128
    labels = jnp.pad(labels, ((0, 0), (0, label_lanes - labels.shape[1])))
    own_rows = jnp.concatenate([own_rows, labels], axis=1)
    outgoing = jnp.dot(placement, own_rows, preferred_element_type=jnp.float32).astype(jnp.bfloat16)
    outgoing = outgoing.reshape(owner_count, capacity, flat_len + label_lanes)
    incoming = lax.all_to_all(outgoing, "loop", split_axis=0, concat_axis=0, tiled=True)
    incoming = incoming.reshape(slot_count, flat_len + label_lanes)
    labels_in = incoming[:, flat_len : flat_len + 3]
    labels_in = labels_in.astype(jnp.float32)
    member_in = labels_in[:, 0]
    rotation = labels_in[:, 1]
    weight_of = labels_in[:, 2]
    block = -(-per_owner // 8) * 8
    angle_grid = jnp.arange(ANGLES, dtype=jnp.float32)
    member_grid = jnp.arange(block, dtype=jnp.float32)
    chosen = (angle_grid[:, None, None] == rotation[None, None, :]) & (
        member_grid[None, :, None] == member_in[None, None, :]
    )
    by_angle = jnp.where(chosen, weight_of[None, None, :], 0.0).astype(jnp.bfloat16)
    by_angle = by_angle.reshape(ANGLES * block, slot_count)
    partial_sums = pl.pallas_call(
        average_kernel,
        out_shape=jax.ShapeDtypeStruct((block, flat_len), jnp.float32),
        scratch_shapes=[pltpu.VMEM((ANGLES * block, flat_len), jnp.float32)],
    )(by_angle, incoming)
    partial_sums = partial_sums[:per_owner].reshape(per_owner, ANGLES, RADII).transpose(0, 2, 1)
    partial_sums = partial_sums.reshape(per_owner, flat_len)
    weighted = (member_grid[:per_owner, None] == member_in[None, :]).astype(jnp.float32) * weight_of[None, :]
    partial_weight = jnp.sum(weighted, axis=1)
    partial_sums, partial_weight, pieces = lax.optimization_barrier((partial_sums, partial_weight, pieces))
    highest, summed = score_all(particle_rows, pieces)
    stats = jnp.stack([highest, summed], axis=0)
    slots = jnp.arange(grp_size, dtype=jnp.int32)[:, None, None] == grp_index
    stats = jnp.where(slots, stats[None], 0.0)
    partial_sums, partial_weight, stats = lax.psum((partial_sums, partial_weight, stats), "grp")
    class_sums = lax.dynamic_slice_in_dim(partial_sums, grp_index * references.shape[0], references.shape[0], 0)
    class_weight = lax.dynamic_slice_in_dim(partial_weight, grp_index * references.shape[0], references.shape[0], 0)
    class_average = class_sums / class_weight[:, None]
    stats = lax.dynamic_slice_in_dim(stats, grp_index * half_rows, half_rows, 2)
    highest = jnp.max(stats[:, 0], axis=0)
    summed = jnp.sum(stats[:, 1] * jnp.exp(stats[:, 0] - highest[None, :]), axis=0)
    log_evidence = highest + jnp.log(summed)
    return (log_evidence, class_average)


def solution(mesh):
    return jax.shard_map(
        local,
        mesh=mesh,
        in_specs=(
            P("loop", None),
            P(("loop", "grp"), None),
            P(("loop", "grp")),
            P(("loop", "grp")),
            P(("loop", "grp")),
        ),
        out_specs=(P(("loop", "grp")), P(("loop", "grp"), None)),
        check_vma=False,
    )
```

```python
import functools
import math

import jax
import jax.numpy as jnp
from jax import lax
from jax.experimental import pallas as pl
from jax.experimental.pallas import tpu as pltpu
from jax.sharding import PartitionSpec as P

RADII = 48
ANGLES = 72


score_factor = 2.0


def angle_major(rows):
    count = rows.shape[0]
    return rows.reshape(count, RADII, ANGLES).transpose(0, 2, 1).reshape(count, RADII * ANGLES)


def score_kernel(*refs, scale):
    p_ref, piece_refs = refs[0], refs[1:-4]
    max_ref, sum_ref, r_scr, s_scr = refs[-4:]
    flat_len = p_ref.shape[1]
    columns = jnp.concatenate([piece[...] for piece in piece_refs], axis=0).T
    r_scr[pl.ds(0, flat_len), :] = columns
    r_scr[pl.ds(flat_len, flat_len), :] = columns
    images = p_ref[...]
    half = ANGLES // 2

    def shift_scores(s, carry):
        turned = jnp.concatenate(
            [
                r_scr[pl.ds(pl.multiple_of(s * RADII, 16), flat_len), :],
                r_scr[pl.ds(pl.multiple_of((s + half) * RADII, 16), flat_len), :],
            ],
            axis=1,
        )
        scores = jnp.dot(images, turned, preferred_element_type=jnp.float32) * scale
        s_scr[s] = scores
        return jnp.maximum(carry, scores)

    first = jnp.full(s_scr.shape[1:], -jnp.inf, jnp.float32)
    lane_max = lax.fori_loop(0, half, shift_scores, first, unroll=9)
    highest = jnp.max(lane_max.T, axis=0, keepdims=True)
    highest_col = jnp.max(lane_max, axis=1, keepdims=True)

    def shift_sum(s, carry):
        return carry + jnp.exp(s_scr[s] - highest_col)

    lane_sum = lax.fori_loop(0, half, shift_sum, jnp.zeros(s_scr.shape[1:], jnp.float32), unroll=4)
    max_ref[...] = highest
    sum_ref[...] = jnp.sum(lane_sum.T, axis=0, keepdims=True)


def score_all(lhs, pieces):
    row_count, flat_len = lhs.shape
    ref_count = sum(piece.shape[0] for piece in pieces)
    scale = score_factor / math.sqrt(flat_len)
    highest, summed = pl.pallas_call(
        functools.partial(score_kernel, scale=scale),
        out_shape=(
            jax.ShapeDtypeStruct((1, row_count), jnp.float32),
            jax.ShapeDtypeStruct((1, row_count), jnp.float32),
        ),
        scratch_shapes=[
            pltpu.VMEM((2 * flat_len, ref_count), jnp.bfloat16),
            pltpu.VMEM((ANGLES // 2, row_count, 2 * ref_count), jnp.float32),
        ],
    )(lhs, *pieces)
    return highest[0], summed[0]


def average_kernel(w_ref, x_ref, o_ref, s_scr):
    block = o_ref.shape[0]
    flat_len = o_ref.shape[1]
    s_scr[...] = jnp.dot(w_ref[...], x_ref[:, :flat_len], preferred_element_type=jnp.float32)
    step = 8
    total = None
    for part in range(step):
        partial = None
        for whole in range(ANGLES // step):
            angle = whole * step + part
            rows = s_scr[pl.ds(angle * block, block), :]
            if whole:
                rows = pltpu.roll(rows, whole * step * RADII, 1)
            partial = rows if partial is None else partial + rows
        if part:
            partial = pltpu.roll(partial, part * RADII, 1)
        total = partial if total is None else total + partial
    o_ref[...] = total


def ring_factors(count):
    factors = []
    while count > 1:
        factor = 4 if count % 4 == 0 else count
        factors.append(factor)
        count //= factor
    return factors


def staged_gather(rows, axis, held):
    count = lax.axis_size(axis)
    stride = 1
    for factor in ring_factors(count):
        parts = [rows]
        for step in range(1, factor):
            pairs = []
            for source in range(count):
                digit = (source // stride) % factor
                pairs.append((source, source + ((digit + step) % factor - digit) * stride))
            parts.append(lax.ppermute(rows, axis, pairs))
        rows = jnp.concatenate(parts, axis=0)
        if stride == 1:
            rows, held = lax.optimization_barrier((rows, held))
        stride *= factor
    return parts, held


def local(particles, references, classes, angles, weights):
    row_count, flat_len = particles.shape
    grp_size = lax.axis_size("grp")
    half_rows = row_count // grp_size
    grp_index = lax.axis_index("grp")
    particle_rows = angle_major(particles)
    own_rows = lax.dynamic_slice_in_dim(particle_rows, grp_index * half_rows, half_rows, 0)
    owner_count = lax.axis_size("loop")
    per_owner = references.shape[0] * grp_size
    capacity = max(2, row_count // owner_count)
    slot_count = owner_count * capacity
    owner_of = classes // per_owner
    member_of = classes % per_owner
    owner_hits = (owner_of[:, None] == jnp.arange(owner_count, dtype=jnp.int32)[None, :]).astype(
        jnp.int32
    )
    earlier = jnp.cumsum(owner_hits, axis=0) - owner_hits
    slot_index = jnp.sum(earlier * owner_hits, axis=1)
    target_slot = owner_of * capacity + slot_index
    placement = (jnp.arange(slot_count, dtype=jnp.int32)[:, None] == target_slot[None, :]).astype(
        jnp.bfloat16
    )
    labels = jnp.stack([member_of, angles, weights], axis=1).astype(jnp.bfloat16)
    label_lanes = 128
    labels = jnp.pad(labels, ((0, 0), (0, label_lanes - labels.shape[1])))
    own_rows = jnp.concatenate([own_rows, labels], axis=1)
    outgoing = jnp.dot(placement, own_rows, preferred_element_type=jnp.float32).astype(jnp.bfloat16)
    outgoing = outgoing.reshape(owner_count, capacity, flat_len + label_lanes)
    pieces, outgoing = staged_gather(angle_major(references), "loop", outgoing)
    incoming = lax.all_to_all(outgoing, "loop", split_axis=0, concat_axis=0, tiled=True)
    incoming = incoming.reshape(slot_count, flat_len + label_lanes)
    labels_in = incoming[:, flat_len : flat_len + 3]
    labels_in = labels_in.astype(jnp.float32)
    member_in = labels_in[:, 0]
    rotation = labels_in[:, 1]
    weight_of = labels_in[:, 2]
    block = -(-per_owner // 8) * 8
    angle_grid = jnp.arange(ANGLES, dtype=jnp.float32)
    member_grid = jnp.arange(block, dtype=jnp.float32)
    chosen = (angle_grid[:, None, None] == rotation[None, None, :]) & (
        member_grid[None, :, None] == member_in[None, None, :]
    )
    by_angle = jnp.where(chosen, weight_of[None, None, :], 0.0).astype(jnp.bfloat16)
    by_angle = by_angle.reshape(ANGLES * block, slot_count)
    partial_sums = pl.pallas_call(
        average_kernel,
        out_shape=jax.ShapeDtypeStruct((block, flat_len), jnp.float32),
        scratch_shapes=[pltpu.VMEM((ANGLES * block, flat_len), jnp.float32)],
    )(by_angle, incoming)
    partial_sums = partial_sums[:per_owner].reshape(per_owner, ANGLES, RADII).transpose(0, 2, 1)
    partial_sums = partial_sums.reshape(per_owner, flat_len)
    weighted = (member_grid[:per_owner, None] == member_in[None, :]).astype(jnp.float32) * weight_of[None, :]
    partial_weight = jnp.sum(weighted, axis=1)
    partial_sums, partial_weight, pieces = lax.optimization_barrier((partial_sums, partial_weight, pieces))
    highest, summed = score_all(particle_rows, pieces)
    stats = jnp.stack([highest, summed], axis=0)
    slots = jnp.arange(grp_size, dtype=jnp.int32)[:, None, None] == grp_index
    stats = jnp.where(slots, stats[None], 0.0)
    partial_sums, partial_weight, stats = lax.psum((partial_sums, partial_weight, stats), "grp")
    class_sums = lax.dynamic_slice_in_dim(partial_sums, grp_index * references.shape[0], references.shape[0], 0)
    class_weight = lax.dynamic_slice_in_dim(partial_weight, grp_index * references.shape[0], references.shape[0], 0)
    class_average = class_sums / class_weight[:, None]
    stats = lax.dynamic_slice_in_dim(stats, grp_index * half_rows, half_rows, 2)
    highest = jnp.max(stats[:, 0], axis=0)
    summed = jnp.sum(stats[:, 1] * jnp.exp(stats[:, 0] - highest[None, :]), axis=0)
    log_evidence = highest + jnp.log(summed)
    return (log_evidence, class_average)


def solution(mesh):
    return jax.shard_map(
        local,
        mesh=mesh,
        in_specs=(
            P("loop", None),
            P(("loop", "grp"), None),
            P(("loop", "grp")),
            P(("loop", "grp")),
            P(("loop", "grp")),
        ),
        out_specs=(P(("loop", "grp")), P(("loop", "grp"), None)),
        check_vma=False,
    )
```

```python
import functools
import math

import jax
import jax.numpy as jnp
from jax import lax
from jax.experimental import pallas as pl
from jax.experimental.pallas import tpu as pltpu
from jax.sharding import PartitionSpec as P

RADII = 48
ANGLES = 72


score_factor = 2.0


def angle_major(rows):
    count = rows.shape[0]
    return rows.reshape(count, RADII, ANGLES).transpose(0, 2, 1).reshape(count, RADII * ANGLES)


def score_kernel(*refs, scale):
    p_ref, piece_refs = refs[0], refs[1:-4]
    max_ref, sum_ref, r_scr, s_scr = refs[-4:]
    flat_len = p_ref.shape[1]
    columns = jnp.concatenate([piece[...] for piece in piece_refs], axis=0).T
    r_scr[pl.ds(0, flat_len), :] = columns
    r_scr[pl.ds(flat_len, flat_len), :] = columns
    images = p_ref[...]
    half = ANGLES // 2

    def shift_scores(s, carry):
        turned = jnp.concatenate(
            [
                r_scr[pl.ds(pl.multiple_of(s * RADII, 16), flat_len), :],
                r_scr[pl.ds(pl.multiple_of((s + half) * RADII, 16), flat_len), :],
            ],
            axis=1,
        )
        scores = jnp.dot(images, turned, preferred_element_type=jnp.float32) * scale
        s_scr[s] = scores
        return jnp.maximum(carry, scores)

    first = jnp.full(s_scr.shape[1:], -jnp.inf, jnp.float32)
    lane_max = lax.fori_loop(0, half, shift_scores, first, unroll=9)
    highest = jnp.max(lane_max.T, axis=0, keepdims=True)
    highest_col = jnp.max(lane_max, axis=1, keepdims=True)

    def shift_sum(s, carry):
        return carry + jnp.exp(s_scr[s] - highest_col)

    lane_sum = lax.fori_loop(0, half, shift_sum, jnp.zeros(s_scr.shape[1:], jnp.float32), unroll=4)
    max_ref[...] = highest
    sum_ref[...] = jnp.sum(lane_sum.T, axis=0, keepdims=True)


def score_all(lhs, pieces):
    row_count, flat_len = lhs.shape
    ref_count = sum(piece.shape[0] for piece in pieces)
    scale = score_factor / math.sqrt(flat_len)
    highest, summed = pl.pallas_call(
        functools.partial(score_kernel, scale=scale),
        out_shape=(
            jax.ShapeDtypeStruct((1, row_count), jnp.float32),
            jax.ShapeDtypeStruct((1, row_count), jnp.float32),
        ),
        scratch_shapes=[
            pltpu.VMEM((2 * flat_len, ref_count), jnp.bfloat16),
            pltpu.VMEM((ANGLES // 2, row_count, 2 * ref_count), jnp.float32),
        ],
    )(lhs, *pieces)
    return highest[0], summed[0]


def average_kernel(w_ref, x_ref, o_ref, s_scr):
    block = o_ref.shape[0]
    flat_len = o_ref.shape[1]
    s_scr[...] = jnp.dot(w_ref[...], x_ref[:, :flat_len], preferred_element_type=jnp.float32)
    step = 8
    total = None
    for part in range(step):
        partial = None
        for whole in range(ANGLES // step):
            angle = whole * step + part
            rows = s_scr[pl.ds(angle * block, block), :]
            if whole:
                rows = pltpu.roll(rows, whole * step * RADII, 1)
            partial = rows if partial is None else partial + rows
        if part:
            partial = pltpu.roll(partial, part * RADII, 1)
        total = partial if total is None else total + partial
    o_ref[...] = total


def ring_factors(count):
    factors = []
    while count > 1:
        factor = 4 if count % 4 == 0 else count
        factors.append(factor)
        count //= factor
    return factors


def staged_gather(rows, axis, held):
    count = lax.axis_size(axis)
    stride = 1
    for factor in ring_factors(count):
        parts = [rows]
        for step in range(1, factor):
            pairs = []
            for source in range(count):
                digit = (source // stride) % factor
                pairs.append((source, source + ((digit + step) % factor - digit) * stride))
            parts.append(lax.ppermute(rows, axis, pairs))
        rows = jnp.concatenate(parts, axis=0)
        if stride == 1:
            rows, held = lax.optimization_barrier((rows, held))
        stride *= factor
    return parts, held


def local(particles, references, classes, angles, weights):
    row_count, flat_len = particles.shape
    grp_size = lax.axis_size("grp")
    half_rows = row_count // grp_size
    grp_index = lax.axis_index("grp")
    particle_rows = angle_major(particles)
    own_rows = lax.dynamic_slice_in_dim(particle_rows, grp_index * half_rows, half_rows, 0)
    owner_count = lax.axis_size("loop")
    per_owner = references.shape[0] * grp_size
    capacity = max(2, row_count // owner_count)
    slot_count = owner_count * capacity
    owner_of = classes // per_owner
    member_of = classes % per_owner
    owner_hits = (owner_of[:, None] == jnp.arange(owner_count, dtype=jnp.int32)[None, :]).astype(
        jnp.int32
    )
    earlier = jnp.cumsum(owner_hits, axis=0) - owner_hits
    slot_index = jnp.sum(earlier * owner_hits, axis=1)
    target_slot = owner_of * capacity + slot_index
    placement = (jnp.arange(slot_count, dtype=jnp.int32)[:, None] == target_slot[None, :]).astype(
        jnp.bfloat16
    )
    labels = jnp.stack([member_of, angles, weights], axis=1).astype(jnp.bfloat16)
    label_lanes = 128
    labels = jnp.pad(labels, ((0, 0), (0, label_lanes - labels.shape[1])))
    own_rows = jnp.concatenate([own_rows, labels], axis=1)
    outgoing = jnp.dot(placement, own_rows, preferred_element_type=jnp.float32).astype(jnp.bfloat16)
    outgoing = outgoing.reshape(owner_count, capacity, flat_len + label_lanes)
    pieces, outgoing = staged_gather(angle_major(references), "loop", outgoing)
    incoming = lax.all_to_all(outgoing, "loop", split_axis=0, concat_axis=0, tiled=True)
    highest, summed = score_all(particle_rows, pieces)
    incoming, highest, summed = lax.optimization_barrier((incoming, highest, summed))
    incoming = incoming.reshape(slot_count, flat_len + label_lanes)
    labels_in = incoming[:, flat_len : flat_len + 3]
    labels_in = labels_in.astype(jnp.float32)
    member_in = labels_in[:, 0]
    rotation = labels_in[:, 1]
    weight_of = labels_in[:, 2]
    block = -(-per_owner // 8) * 8
    angle_grid = jnp.arange(ANGLES, dtype=jnp.float32)
    member_grid = jnp.arange(block, dtype=jnp.float32)
    chosen = (angle_grid[:, None, None] == rotation[None, None, :]) & (
        member_grid[None, :, None] == member_in[None, None, :]
    )
    by_angle = jnp.where(chosen, weight_of[None, None, :], 0.0).astype(jnp.bfloat16)
    by_angle = by_angle.reshape(ANGLES * block, slot_count)
    partial_sums = pl.pallas_call(
        average_kernel,
        out_shape=jax.ShapeDtypeStruct((block, flat_len), jnp.float32),
        scratch_shapes=[pltpu.VMEM((ANGLES * block, flat_len), jnp.float32)],
    )(by_angle, incoming)
    partial_sums = partial_sums[:per_owner].reshape(per_owner, ANGLES, RADII).transpose(0, 2, 1)
    partial_sums = partial_sums.reshape(per_owner, flat_len)
    weighted = (member_grid[:per_owner, None] == member_in[None, :]).astype(jnp.float32) * weight_of[None, :]
    partial_weight = jnp.sum(weighted, axis=1)
    stats = jnp.stack([highest, summed], axis=0)
    slots = jnp.arange(grp_size, dtype=jnp.int32)[:, None, None] == grp_index
    stats = jnp.where(slots, stats[None], 0.0)
    partial_sums, partial_weight, stats = lax.psum((partial_sums, partial_weight, stats), "grp")
    class_sums = lax.dynamic_slice_in_dim(partial_sums, grp_index * references.shape[0], references.shape[0], 0)
    class_weight = lax.dynamic_slice_in_dim(partial_weight, grp_index * references.shape[0], references.shape[0], 0)
    class_average = class_sums / class_weight[:, None]
    stats = lax.dynamic_slice_in_dim(stats, grp_index * half_rows, half_rows, 2)
    highest = jnp.max(stats[:, 0], axis=0)
    summed = jnp.sum(stats[:, 1] * jnp.exp(stats[:, 0] - highest[None, :]), axis=0)
    log_evidence = highest + jnp.log(summed)
    return (log_evidence, class_average)


def solution(mesh):
    return jax.shard_map(
        local,
        mesh=mesh,
        in_specs=(
            P("loop", None),
            P(("loop", "grp"), None),
            P(("loop", "grp")),
            P(("loop", "grp")),
            P(("loop", "grp")),
        ),
        out_specs=(P(("loop", "grp")), P(("loop", "grp"), None)),
        check_vma=False,
    )
```

```python
import functools
import math

import jax
import jax.numpy as jnp
from jax import lax
from jax.experimental import pallas as pl
from jax.experimental.pallas import tpu as pltpu
from jax.sharding import PartitionSpec as P

RADII = 48
ANGLES = 72


score_factor = 2.0


def angle_major(rows):
    count = rows.shape[0]
    return rows.reshape(count, RADII, ANGLES).transpose(0, 2, 1).reshape(count, RADII * ANGLES)


def score_kernel(*refs, scale):
    p_ref, piece_refs = refs[0], refs[1:-4]
    max_ref, sum_ref, r_scr, s_scr = refs[-4:]
    flat_len = p_ref.shape[1]
    columns = jnp.concatenate([piece[...] for piece in piece_refs], axis=0).T
    r_scr[pl.ds(0, flat_len), :] = columns
    r_scr[pl.ds(flat_len, flat_len), :] = columns
    images = p_ref[...]
    half = ANGLES // 2

    def shift_scores(s, carry):
        turned = jnp.concatenate(
            [
                r_scr[pl.ds(pl.multiple_of(s * RADII, 16), flat_len), :],
                r_scr[pl.ds(pl.multiple_of((s + half) * RADII, 16), flat_len), :],
            ],
            axis=1,
        )
        scores = jnp.dot(images, turned, preferred_element_type=jnp.float32) * scale
        s_scr[s] = scores
        return jnp.maximum(carry, scores)

    first = jnp.full(s_scr.shape[1:], -jnp.inf, jnp.float32)
    lane_max = lax.fori_loop(0, half, shift_scores, first, unroll=9)
    highest = jnp.max(lane_max.T, axis=0, keepdims=True)
    highest_col = jnp.max(lane_max, axis=1, keepdims=True)

    def shift_sum(s, carry):
        return carry + jnp.exp(s_scr[s] - highest_col)

    lane_sum = lax.fori_loop(0, half, shift_sum, jnp.zeros(s_scr.shape[1:], jnp.float32), unroll=4)
    max_ref[...] = highest
    sum_ref[...] = jnp.sum(lane_sum.T, axis=0, keepdims=True)


def score_all(lhs, pieces):
    row_count, flat_len = lhs.shape
    ref_count = sum(piece.shape[0] for piece in pieces)
    scale = score_factor / math.sqrt(flat_len)
    highest, summed = pl.pallas_call(
        functools.partial(score_kernel, scale=scale),
        out_shape=(
            jax.ShapeDtypeStruct((1, row_count), jnp.float32),
            jax.ShapeDtypeStruct((1, row_count), jnp.float32),
        ),
        scratch_shapes=[
            pltpu.VMEM((2 * flat_len, ref_count), jnp.bfloat16),
            pltpu.VMEM((ANGLES // 2, row_count, 2 * ref_count), jnp.float32),
        ],
    )(lhs, *pieces)
    return highest[0], summed[0]


def average_kernel(w_ref, x_ref, o_ref, s_scr):
    block = o_ref.shape[0]
    flat_len = o_ref.shape[1]
    s_scr[...] = jnp.dot(w_ref[...], x_ref[:, :flat_len], preferred_element_type=jnp.float32)
    step = 8
    total = None
    for part in range(step):
        partial = None
        for whole in range(ANGLES // step):
            angle = whole * step + part
            rows = s_scr[pl.ds(angle * block, block), :]
            if whole:
                rows = pltpu.roll(rows, whole * step * RADII, 1)
            partial = rows if partial is None else partial + rows
        if part:
            partial = pltpu.roll(partial, part * RADII, 1)
        total = partial if total is None else total + partial
    o_ref[...] = total


def ring_factors(count):
    factors = []
    while count > 1:
        factor = 4 if count % 4 == 0 else count
        factors.append(factor)
        count //= factor
    return factors


def staged_gather(rows, axis, held):
    count = lax.axis_size(axis)
    stride = 1
    factors = ring_factors(count)
    for round_index, factor in enumerate(factors):
        parts = [rows]
        for step in range(1, factor):
            pairs = []
            for source in range(count):
                digit = (source // stride) % factor
                pairs.append((source, source + ((digit + step) % factor - digit) * stride))
            parts.append(lax.ppermute(rows, axis, pairs))
        rows = jnp.concatenate(parts, axis=0)
        if round_index == len(factors) - 1:
            parts, held = lax.optimization_barrier((parts, held))
        stride *= factor
    return parts, held


def local(particles, references, classes, angles, weights):
    row_count, flat_len = particles.shape
    grp_size = lax.axis_size("grp")
    half_rows = row_count // grp_size
    grp_index = lax.axis_index("grp")
    particle_rows = angle_major(particles)
    own_rows = lax.dynamic_slice_in_dim(particle_rows, grp_index * half_rows, half_rows, 0)
    owner_count = lax.axis_size("loop")
    per_owner = references.shape[0] * grp_size
    capacity = max(2, row_count // owner_count)
    slot_count = owner_count * capacity
    owner_of = classes // per_owner
    member_of = classes % per_owner
    owner_hits = (owner_of[:, None] == jnp.arange(owner_count, dtype=jnp.int32)[None, :]).astype(
        jnp.int32
    )
    earlier = jnp.cumsum(owner_hits, axis=0) - owner_hits
    slot_index = jnp.sum(earlier * owner_hits, axis=1)
    target_slot = owner_of * capacity + slot_index
    placement = (jnp.arange(slot_count, dtype=jnp.int32)[:, None] == target_slot[None, :]).astype(
        jnp.bfloat16
    )
    labels = jnp.stack([member_of, angles, weights], axis=1).astype(jnp.bfloat16)
    label_lanes = 128
    labels = jnp.pad(labels, ((0, 0), (0, label_lanes - labels.shape[1])))
    own_rows = jnp.concatenate([own_rows, labels], axis=1)
    outgoing = jnp.dot(placement, own_rows, preferred_element_type=jnp.float32).astype(jnp.bfloat16)
    outgoing = outgoing.reshape(owner_count, capacity, flat_len + label_lanes)
    pieces, outgoing = staged_gather(angle_major(references), "loop", outgoing)
    incoming = lax.all_to_all(outgoing, "loop", split_axis=0, concat_axis=0, tiled=True)
    highest, summed = score_all(particle_rows, pieces)
    incoming, highest, summed = lax.optimization_barrier((incoming, highest, summed))
    incoming = incoming.reshape(slot_count, flat_len + label_lanes)
    labels_in = incoming[:, flat_len : flat_len + 3]
    labels_in = labels_in.astype(jnp.float32)
    member_in = labels_in[:, 0]
    rotation = labels_in[:, 1]
    weight_of = labels_in[:, 2]
    block = -(-per_owner // 8) * 8
    angle_grid = jnp.arange(ANGLES, dtype=jnp.float32)
    member_grid = jnp.arange(block, dtype=jnp.float32)
    chosen = (angle_grid[:, None, None] == rotation[None, None, :]) & (
        member_grid[None, :, None] == member_in[None, None, :]
    )
    by_angle = jnp.where(chosen, weight_of[None, None, :], 0.0).astype(jnp.bfloat16)
    by_angle = by_angle.reshape(ANGLES * block, slot_count)
    partial_sums = pl.pallas_call(
        average_kernel,
        out_shape=jax.ShapeDtypeStruct((block, flat_len), jnp.float32),
        scratch_shapes=[pltpu.VMEM((ANGLES * block, flat_len), jnp.float32)],
    )(by_angle, incoming)
    partial_sums = partial_sums[:per_owner].reshape(per_owner, ANGLES, RADII).transpose(0, 2, 1)
    partial_sums = partial_sums.reshape(per_owner, flat_len)
    weighted = (member_grid[:per_owner, None] == member_in[None, :]).astype(jnp.float32) * weight_of[None, :]
    partial_weight = jnp.sum(weighted, axis=1)
    stats = jnp.stack([highest, summed], axis=0)
    slots = jnp.arange(grp_size, dtype=jnp.int32)[:, None, None] == grp_index
    stats = jnp.where(slots, stats[None], 0.0)
    partial_sums, partial_weight, stats = lax.psum((partial_sums, partial_weight, stats), "grp")
    class_sums = lax.dynamic_slice_in_dim(partial_sums, grp_index * references.shape[0], references.shape[0], 0)
    class_weight = lax.dynamic_slice_in_dim(partial_weight, grp_index * references.shape[0], references.shape[0], 0)
    class_average = class_sums / class_weight[:, None]
    stats = lax.dynamic_slice_in_dim(stats, grp_index * half_rows, half_rows, 2)
    highest = jnp.max(stats[:, 0], axis=0)
    summed = jnp.sum(stats[:, 1] * jnp.exp(stats[:, 0] - highest[None, :]), axis=0)
    log_evidence = highest + jnp.log(summed)
    return (log_evidence, class_average)


def solution(mesh):
    return jax.shard_map(
        local,
        mesh=mesh,
        in_specs=(
            P("loop", None),
            P(("loop", "grp"), None),
            P(("loop", "grp")),
            P(("loop", "grp")),
            P(("loop", "grp")),
        ),
        out_specs=(P(("loop", "grp")), P(("loop", "grp"), None)),
        check_vma=False,
    )
```

```python
import functools
import math

import jax
import jax.numpy as jnp
from jax import lax
from jax.experimental import pallas as pl
from jax.experimental.pallas import tpu as pltpu
from jax.sharding import PartitionSpec as P

RADII = 48
ANGLES = 72


score_factor = 2.0


def angle_major(rows):
    count = rows.shape[0]
    return rows.reshape(count, RADII, ANGLES).transpose(0, 2, 1).reshape(count, RADII * ANGLES)


def score_kernel(*refs, scale):
    p_ref, piece_refs = refs[0], refs[1:-4]
    max_ref, sum_ref, r_scr, s_scr = refs[-4:]
    flat_len = p_ref.shape[1]
    columns = jnp.concatenate([piece[...] for piece in piece_refs], axis=0).T
    r_scr[pl.ds(0, flat_len), :] = columns
    r_scr[pl.ds(flat_len, flat_len), :] = columns
    images = p_ref[...]
    half = ANGLES // 2

    def shift_scores(s, carry):
        turned = jnp.concatenate(
            [
                r_scr[pl.ds(pl.multiple_of(s * RADII, 16), flat_len), :],
                r_scr[pl.ds(pl.multiple_of((s + half) * RADII, 16), flat_len), :],
            ],
            axis=1,
        )
        scores = jnp.dot(images, turned, preferred_element_type=jnp.float32) * scale
        s_scr[s] = scores
        return jnp.maximum(carry, scores)

    first = jnp.full(s_scr.shape[1:], -jnp.inf, jnp.float32)
    lane_max = lax.fori_loop(0, half, shift_scores, first, unroll=9)
    highest = jnp.max(lane_max.T, axis=0, keepdims=True)
    highest_col = jnp.max(lane_max, axis=1, keepdims=True)

    def shift_sum(s, carry):
        return carry + jnp.exp(s_scr[s] - highest_col)

    lane_sum = lax.fori_loop(0, half, shift_sum, jnp.zeros(s_scr.shape[1:], jnp.float32), unroll=4)
    max_ref[...] = highest
    sum_ref[...] = jnp.sum(lane_sum.T, axis=0, keepdims=True)


def score_all(lhs, pieces):
    row_count, flat_len = lhs.shape
    ref_count = sum(piece.shape[0] for piece in pieces)
    scale = score_factor / math.sqrt(flat_len)
    highest, summed = pl.pallas_call(
        functools.partial(score_kernel, scale=scale),
        out_shape=(
            jax.ShapeDtypeStruct((1, row_count), jnp.float32),
            jax.ShapeDtypeStruct((1, row_count), jnp.float32),
        ),
        scratch_shapes=[
            pltpu.VMEM((2 * flat_len, ref_count), jnp.bfloat16),
            pltpu.VMEM((ANGLES // 2, row_count, 2 * ref_count), jnp.float32),
        ],
    )(lhs, *pieces)
    return highest[0], summed[0]


def average_kernel(w_ref, x_ref, o_ref, s_scr):
    block = o_ref.shape[0]
    flat_len = o_ref.shape[1]
    s_scr[...] = jnp.dot(w_ref[...], x_ref[:, :flat_len], preferred_element_type=jnp.float32)
    step = 8
    total = None
    for part in range(step):
        partial = None
        for whole in range(ANGLES // step):
            angle = whole * step + part
            rows = s_scr[pl.ds(angle * block, block), :]
            if whole:
                rows = pltpu.roll(rows, whole * step * RADII, 1)
            partial = rows if partial is None else partial + rows
        if part:
            partial = pltpu.roll(partial, part * RADII, 1)
        total = partial if total is None else total + partial
    o_ref[...] = total


def ring_factors(count):
    factors = []
    while count > 1:
        factor = 4 if count % 4 == 0 else count
        factors.append(factor)
        count //= factor
    return factors


def staged_gather(rows, axis, held):
    count = lax.axis_size(axis)
    stride = 1
    factors = ring_factors(count)
    for round_index, factor in enumerate(factors):
        parts = [rows]
        for step in range(1, factor):
            pairs = []
            for source in range(count):
                digit = (source // stride) % factor
                pairs.append((source, source + ((digit + step) % factor - digit) * stride))
            parts.append(lax.ppermute(rows, axis, pairs))
        rows = jnp.concatenate(parts, axis=0)
        if round_index == len(factors) - 1:
            parts, held = lax.optimization_barrier((parts, held))
        stride *= factor
    return parts, held


def local(particles, references, classes, angles, weights):
    row_count, flat_len = particles.shape
    grp_size = lax.axis_size("grp")
    half_rows = row_count // grp_size
    grp_index = lax.axis_index("grp")
    particle_rows = angle_major(particles)
    own_rows = lax.dynamic_slice_in_dim(particle_rows, grp_index * half_rows, half_rows, 0)
    owner_count = lax.axis_size("loop")
    per_owner = references.shape[0] * grp_size
    capacity = max(2, row_count // owner_count)
    slot_count = owner_count * capacity
    owner_of = classes // per_owner
    member_of = classes % per_owner
    owner_hits = (owner_of[:, None] == jnp.arange(owner_count, dtype=jnp.int32)[None, :]).astype(
        jnp.int32
    )
    earlier = jnp.cumsum(owner_hits, axis=0) - owner_hits
    slot_index = jnp.sum(earlier * owner_hits, axis=1)
    target_slot = owner_of * capacity + slot_index
    placement = (jnp.arange(slot_count, dtype=jnp.int32)[:, None] == target_slot[None, :]).astype(
        jnp.bfloat16
    )
    labels = jnp.stack([member_of, angles, weights], axis=1).astype(jnp.bfloat16)
    label_lanes = 128
    labels = jnp.pad(labels, ((0, 0), (0, label_lanes - labels.shape[1])))
    own_rows = jnp.concatenate([own_rows, labels], axis=1)
    outgoing = jnp.dot(placement, own_rows, preferred_element_type=jnp.float32).astype(jnp.bfloat16)
    outgoing = outgoing.reshape(owner_count, capacity, flat_len + label_lanes)
    pieces, (outgoing, particle_rows) = staged_gather(angle_major(references), "loop", (outgoing, particle_rows))
    incoming = lax.all_to_all(outgoing, "loop", split_axis=0, concat_axis=0, tiled=True)
    highest, summed = score_all(particle_rows, pieces)
    incoming, highest, summed = lax.optimization_barrier((incoming, highest, summed))
    incoming = incoming.reshape(slot_count, flat_len + label_lanes)
    labels_in = incoming[:, flat_len : flat_len + 3]
    labels_in = labels_in.astype(jnp.float32)
    member_in = labels_in[:, 0]
    rotation = labels_in[:, 1]
    weight_of = labels_in[:, 2]
    block = -(-per_owner // 8) * 8
    angle_grid = jnp.arange(ANGLES, dtype=jnp.float32)
    member_grid = jnp.arange(block, dtype=jnp.float32)
    chosen = (angle_grid[:, None, None] == rotation[None, None, :]) & (
        member_grid[None, :, None] == member_in[None, None, :]
    )
    by_angle = jnp.where(chosen, weight_of[None, None, :], 0.0).astype(jnp.bfloat16)
    by_angle = by_angle.reshape(ANGLES * block, slot_count)
    partial_sums = pl.pallas_call(
        average_kernel,
        out_shape=jax.ShapeDtypeStruct((block, flat_len), jnp.float32),
        scratch_shapes=[pltpu.VMEM((ANGLES * block, flat_len), jnp.float32)],
    )(by_angle, incoming)
    partial_sums = partial_sums[:per_owner]
    weighted = (member_grid[:per_owner, None] == member_in[None, :]).astype(jnp.float32) * weight_of[None, :]
    partial_weight = jnp.sum(weighted, axis=1)
    stats = jnp.stack([highest, summed], axis=0)
    slots = jnp.arange(grp_size, dtype=jnp.int32)[:, None, None] == grp_index
    stats = jnp.where(slots, stats[None], 0.0)
    partial_sums, partial_weight, stats = lax.psum((partial_sums, partial_weight, stats), "grp")
    class_sums = lax.dynamic_slice_in_dim(partial_sums, grp_index * references.shape[0], references.shape[0], 0)
    class_weight = lax.dynamic_slice_in_dim(partial_weight, grp_index * references.shape[0], references.shape[0], 0)
    class_average = class_sums / class_weight[:, None]
    class_average = class_average.reshape(-1, ANGLES, RADII).transpose(0, 2, 1).reshape(-1, flat_len)
    stats = lax.dynamic_slice_in_dim(stats, grp_index * half_rows, half_rows, 2)
    highest = jnp.max(stats[:, 0], axis=0)
    summed = jnp.sum(stats[:, 1] * jnp.exp(stats[:, 0] - highest[None, :]), axis=0)
    log_evidence = highest + jnp.log(summed)
    return (log_evidence, class_average)


def solution(mesh):
    return jax.shard_map(
        local,
        mesh=mesh,
        in_specs=(
            P("loop", None),
            P(("loop", "grp"), None),
            P(("loop", "grp")),
            P(("loop", "grp")),
            P(("loop", "grp")),
        ),
        out_specs=(P(("loop", "grp")), P(("loop", "grp"), None)),
        check_vma=False,
    )
```

```python
import functools
import math

import jax
import jax.numpy as jnp
from jax import lax
from jax.experimental import pallas as pl
from jax.experimental.pallas import tpu as pltpu
from jax.sharding import PartitionSpec as P

RADII = 48
ANGLES = 72


score_factor = 2.0


def angle_major(rows):
    count = rows.shape[0]
    return rows.reshape(count, RADII, ANGLES).transpose(0, 2, 1).reshape(count, RADII * ANGLES)


def angle_major_kernel(x_ref, o_ref, t_scr, a_scr):
    t_scr[...] = x_ref[...].astype(jnp.float32).T
    for angle in range(ANGLES):
        a_scr[pl.ds(angle * RADII, RADII), :] = t_scr[pl.ds(angle, RADII, stride=ANGLES), :]
    o_ref[...] = a_scr[...].T.astype(o_ref.dtype)


def angle_major_rows(rows):
    count, flat_len = rows.shape
    return pl.pallas_call(
        angle_major_kernel,
        out_shape=jax.ShapeDtypeStruct((count, flat_len), rows.dtype),
        scratch_shapes=[
            pltpu.VMEM((flat_len, count), jnp.float32),
            pltpu.VMEM((flat_len, count), jnp.float32),
        ],
    )(rows)


def score_kernel(*refs, scale):
    p_ref, piece_refs = refs[0], refs[1:-4]
    max_ref, sum_ref, r_scr, s_scr = refs[-4:]
    flat_len = p_ref.shape[1]
    columns = jnp.concatenate([piece[...] for piece in piece_refs], axis=0).T
    r_scr[pl.ds(0, flat_len), :] = columns
    r_scr[pl.ds(flat_len, flat_len), :] = columns
    images = p_ref[...]
    half = ANGLES // 2

    def shift_scores(s, carry):
        turned = jnp.concatenate(
            [
                r_scr[pl.ds(pl.multiple_of(s * RADII, 16), flat_len), :],
                r_scr[pl.ds(pl.multiple_of((s + half) * RADII, 16), flat_len), :],
            ],
            axis=1,
        )
        scores = jnp.dot(images, turned, preferred_element_type=jnp.float32) * scale
        s_scr[s] = scores
        return jnp.maximum(carry, scores)

    first = jnp.full(s_scr.shape[1:], -jnp.inf, jnp.float32)
    lane_max = lax.fori_loop(0, half, shift_scores, first, unroll=9)
    highest = jnp.max(lane_max.T, axis=0, keepdims=True)
    highest_col = jnp.max(lane_max, axis=1, keepdims=True)

    def shift_sum(s, carry):
        return carry + jnp.exp(s_scr[s] - highest_col)

    lane_sum = lax.fori_loop(0, half, shift_sum, jnp.zeros(s_scr.shape[1:], jnp.float32), unroll=4)
    max_ref[...] = highest
    sum_ref[...] = jnp.sum(lane_sum.T, axis=0, keepdims=True)


def score_all(lhs, pieces):
    row_count, flat_len = lhs.shape
    ref_count = sum(piece.shape[0] for piece in pieces)
    scale = score_factor / math.sqrt(flat_len)
    highest, summed = pl.pallas_call(
        functools.partial(score_kernel, scale=scale),
        out_shape=(
            jax.ShapeDtypeStruct((1, row_count), jnp.float32),
            jax.ShapeDtypeStruct((1, row_count), jnp.float32),
        ),
        scratch_shapes=[
            pltpu.VMEM((2 * flat_len, ref_count), jnp.bfloat16),
            pltpu.VMEM((ANGLES // 2, row_count, 2 * ref_count), jnp.float32),
        ],
    )(lhs, *pieces)
    return highest[0], summed[0]


def average_kernel(w_ref, x_ref, o_ref, s_scr):
    block = o_ref.shape[0]
    flat_len = o_ref.shape[1]
    s_scr[...] = jnp.dot(w_ref[...], x_ref[:, :flat_len], preferred_element_type=jnp.float32)
    step = 8
    total = None
    for part in range(step):
        partial = None
        for whole in range(ANGLES // step):
            angle = whole * step + part
            rows = s_scr[pl.ds(angle * block, block), :]
            if whole:
                rows = pltpu.roll(rows, whole * step * RADII, 1)
            partial = rows if partial is None else partial + rows
        if part:
            partial = pltpu.roll(partial, part * RADII, 1)
        total = partial if total is None else total + partial
    o_ref[...] = total


def ring_factors(count):
    factors = []
    while count > 1:
        factor = 4 if count % 4 == 0 else count
        factors.append(factor)
        count //= factor
    return factors


def staged_gather(rows, axis, held):
    count = lax.axis_size(axis)
    stride = 1
    factors = ring_factors(count)
    for round_index, factor in enumerate(factors):
        parts = [rows]
        for step in range(1, factor):
            pairs = []
            for source in range(count):
                digit = (source // stride) % factor
                pairs.append((source, source + ((digit + step) % factor - digit) * stride))
            parts.append(lax.ppermute(rows, axis, pairs))
        rows = jnp.concatenate(parts, axis=0)
        if round_index == len(factors) - 1:
            parts, held = lax.optimization_barrier((parts, held))
        stride *= factor
    return parts, held


def local(particles, references, classes, angles, weights):
    row_count, flat_len = particles.shape
    grp_size = lax.axis_size("grp")
    half_rows = row_count // grp_size
    grp_index = lax.axis_index("grp")
    particle_rows = angle_major_rows(particles)
    own_rows = lax.dynamic_slice_in_dim(particle_rows, grp_index * half_rows, half_rows, 0)
    owner_count = lax.axis_size("loop")
    per_owner = references.shape[0] * grp_size
    capacity = max(2, row_count // owner_count)
    slot_count = owner_count * capacity
    owner_of = classes // per_owner
    member_of = classes % per_owner
    owner_hits = (owner_of[:, None] == jnp.arange(owner_count, dtype=jnp.int32)[None, :]).astype(
        jnp.int32
    )
    earlier = jnp.cumsum(owner_hits, axis=0) - owner_hits
    slot_index = jnp.sum(earlier * owner_hits, axis=1)
    target_slot = owner_of * capacity + slot_index
    placement = (jnp.arange(slot_count, dtype=jnp.int32)[:, None] == target_slot[None, :]).astype(
        jnp.bfloat16
    )
    labels = jnp.stack([member_of, angles, weights], axis=1).astype(jnp.bfloat16)
    label_lanes = 128
    labels = jnp.pad(labels, ((0, 0), (0, label_lanes - labels.shape[1])))
    own_rows = jnp.concatenate([own_rows, labels], axis=1)
    outgoing = jnp.dot(placement, own_rows, preferred_element_type=jnp.float32).astype(jnp.bfloat16)
    outgoing = outgoing.reshape(owner_count, capacity, flat_len + label_lanes)
    pieces, outgoing = staged_gather(angle_major(references), "loop", outgoing)
    incoming = lax.all_to_all(outgoing, "loop", split_axis=0, concat_axis=0, tiled=True)
    highest, summed = score_all(particle_rows, pieces)
    incoming, highest, summed = lax.optimization_barrier((incoming, highest, summed))
    incoming = incoming.reshape(slot_count, flat_len + label_lanes)
    labels_in = incoming[:, flat_len : flat_len + 3]
    labels_in = labels_in.astype(jnp.float32)
    member_in = labels_in[:, 0]
    rotation = labels_in[:, 1]
    weight_of = labels_in[:, 2]
    block = -(-per_owner // 8) * 8
    angle_grid = jnp.arange(ANGLES, dtype=jnp.float32)
    member_grid = jnp.arange(block, dtype=jnp.float32)
    chosen = (angle_grid[:, None, None] == rotation[None, None, :]) & (
        member_grid[None, :, None] == member_in[None, None, :]
    )
    by_angle = jnp.where(chosen, weight_of[None, None, :], 0.0).astype(jnp.bfloat16)
    by_angle = by_angle.reshape(ANGLES * block, slot_count)
    partial_sums = pl.pallas_call(
        average_kernel,
        out_shape=jax.ShapeDtypeStruct((block, flat_len), jnp.float32),
        scratch_shapes=[pltpu.VMEM((ANGLES * block, flat_len), jnp.float32)],
    )(by_angle, incoming)
    partial_sums = partial_sums[:per_owner].reshape(per_owner, ANGLES, RADII).transpose(0, 2, 1)
    partial_sums = partial_sums.reshape(per_owner, flat_len)
    weighted = (member_grid[:per_owner, None] == member_in[None, :]).astype(jnp.float32) * weight_of[None, :]
    partial_weight = jnp.sum(weighted, axis=1)
    stats = jnp.stack([highest, summed], axis=0)
    slots = jnp.arange(grp_size, dtype=jnp.int32)[:, None, None] == grp_index
    stats = jnp.where(slots, stats[None], 0.0)
    partial_sums, partial_weight, stats = lax.psum((partial_sums, partial_weight, stats), "grp")
    class_sums = lax.dynamic_slice_in_dim(partial_sums, grp_index * references.shape[0], references.shape[0], 0)
    class_weight = lax.dynamic_slice_in_dim(partial_weight, grp_index * references.shape[0], references.shape[0], 0)
    class_average = class_sums / class_weight[:, None]
    stats = lax.dynamic_slice_in_dim(stats, grp_index * half_rows, half_rows, 2)
    highest = jnp.max(stats[:, 0], axis=0)
    summed = jnp.sum(stats[:, 1] * jnp.exp(stats[:, 0] - highest[None, :]), axis=0)
    log_evidence = highest + jnp.log(summed)
    return (log_evidence, class_average)


def solution(mesh):
    return jax.shard_map(
        local,
        mesh=mesh,
        in_specs=(
            P("loop", None),
            P(("loop", "grp"), None),
            P(("loop", "grp")),
            P(("loop", "grp")),
            P(("loop", "grp")),
        ),
        out_specs=(P(("loop", "grp")), P(("loop", "grp"), None)),
        check_vma=False,
    )
```

```python
import functools
import math

import jax
import jax.numpy as jnp
from jax import lax
from jax.experimental import pallas as pl
from jax.experimental.pallas import tpu as pltpu
from jax.sharding import PartitionSpec as P

RADII = 48
ANGLES = 72


score_factor = 2.0


def angle_major(rows):
    count = rows.shape[0]
    return rows.reshape(count, RADII, ANGLES).transpose(0, 2, 1).reshape(count, RADII * ANGLES)


def angle_major_kernel(x_ref, o_ref, t_scr, a_scr):
    t_scr[...] = x_ref[...].astype(jnp.float32).T
    for angle in range(ANGLES):
        a_scr[pl.ds(angle * RADII, RADII), :] = t_scr[pl.ds(angle, RADII, stride=ANGLES), :]
    o_ref[...] = a_scr[...].T.astype(o_ref.dtype)


def angle_major_rows(rows):
    count, flat_len = rows.shape
    return pl.pallas_call(
        angle_major_kernel,
        out_shape=jax.ShapeDtypeStruct((count, flat_len), rows.dtype),
        scratch_shapes=[
            pltpu.VMEM((flat_len, count), jnp.float32),
            pltpu.VMEM((flat_len, count), jnp.float32),
        ],
    )(rows)


def score_kernel(*refs, scale):
    p_ref, piece_refs = refs[0], refs[1:-4]
    max_ref, sum_ref, r_scr, s_scr = refs[-4:]
    flat_len = p_ref.shape[1]
    columns = jnp.concatenate([piece[...] for piece in piece_refs], axis=0).T
    r_scr[pl.ds(0, flat_len), :] = columns
    r_scr[pl.ds(flat_len, flat_len), :] = columns
    images = p_ref[...]
    half = ANGLES // 2

    def shift_scores(s, carry):
        turned = jnp.concatenate(
            [
                r_scr[pl.ds(pl.multiple_of(s * RADII, 16), flat_len), :],
                r_scr[pl.ds(pl.multiple_of((s + half) * RADII, 16), flat_len), :],
            ],
            axis=1,
        )
        scores = jnp.dot(images, turned, preferred_element_type=jnp.float32) * scale
        s_scr[s] = scores
        return jnp.maximum(carry, scores)

    first = jnp.full(s_scr.shape[1:], -jnp.inf, jnp.float32)
    lane_max = lax.fori_loop(0, half, shift_scores, first, unroll=9)
    highest = jnp.max(lane_max.T, axis=0, keepdims=True)
    highest_col = jnp.max(lane_max, axis=1, keepdims=True)

    def shift_sum(s, carry):
        return carry + jnp.exp(s_scr[s] - highest_col)

    lane_sum = lax.fori_loop(0, half, shift_sum, jnp.zeros(s_scr.shape[1:], jnp.float32), unroll=4)
    max_ref[...] = highest
    sum_ref[...] = jnp.sum(lane_sum.T, axis=0, keepdims=True)


def score_all(lhs, pieces):
    row_count, flat_len = lhs.shape
    ref_count = sum(piece.shape[0] for piece in pieces)
    scale = score_factor / math.sqrt(flat_len)
    highest, summed = pl.pallas_call(
        functools.partial(score_kernel, scale=scale),
        out_shape=(
            jax.ShapeDtypeStruct((1, row_count), jnp.float32),
            jax.ShapeDtypeStruct((1, row_count), jnp.float32),
        ),
        scratch_shapes=[
            pltpu.VMEM((2 * flat_len, ref_count), jnp.bfloat16),
            pltpu.VMEM((ANGLES // 2, row_count, 2 * ref_count), jnp.float32),
        ],
    )(lhs, *pieces)
    return highest[0], summed[0]


def average_kernel(w_ref, x_ref, o_ref, s_scr):
    block = o_ref.shape[0]
    flat_len = o_ref.shape[1]
    s_scr[...] = jnp.dot(w_ref[...], x_ref[:, :flat_len], preferred_element_type=jnp.float32)
    step = 8
    total = None
    for part in range(step):
        partial = None
        for whole in range(ANGLES // step):
            angle = whole * step + part
            rows = s_scr[pl.ds(angle * block, block), :]
            if whole:
                rows = pltpu.roll(rows, whole * step * RADII, 1)
            partial = rows if partial is None else partial + rows
        if part:
            partial = pltpu.roll(partial, part * RADII, 1)
        total = partial if total is None else total + partial
    o_ref[...] = total


def ring_factors(count):
    factors = []
    while count > 1:
        factor = 4 if count % 4 == 0 else count
        factors.append(factor)
        count //= factor
    return factors


def staged_gather(rows, axis, held):
    count = lax.axis_size(axis)
    stride = 1
    factors = ring_factors(count)
    for round_index, factor in enumerate(factors):
        parts = [rows]
        for step in range(1, factor):
            pairs = []
            for source in range(count):
                digit = (source // stride) % factor
                pairs.append((source, source + ((digit + step) % factor - digit) * stride))
            parts.append(lax.ppermute(rows, axis, pairs))
        rows = jnp.concatenate(parts, axis=0)
        if round_index == len(factors) - 1:
            parts, held = lax.optimization_barrier((parts, held))
        stride *= factor
    return parts, held


def local(particles, references, classes, angles, weights):
    row_count, flat_len = particles.shape
    grp_size = lax.axis_size("grp")
    half_rows = row_count // grp_size
    grp_index = lax.axis_index("grp")
    particle_rows = angle_major_rows(particles)
    own_rows = lax.dynamic_slice_in_dim(particle_rows, grp_index * half_rows, half_rows, 0)
    owner_count = lax.axis_size("loop")
    per_owner = references.shape[0] * grp_size
    capacity = max(2, row_count // owner_count)
    slot_count = owner_count * capacity
    owner_of = classes // per_owner
    member_of = classes % per_owner
    owner_hits = (owner_of[:, None] == jnp.arange(owner_count, dtype=jnp.int32)[None, :]).astype(
        jnp.int32
    )
    earlier = jnp.cumsum(owner_hits, axis=0) - owner_hits
    slot_index = jnp.sum(earlier * owner_hits, axis=1)
    target_slot = owner_of * capacity + slot_index
    placement = (jnp.arange(slot_count, dtype=jnp.int32)[:, None] == target_slot[None, :]).astype(
        jnp.bfloat16
    )
    labels = jnp.stack([member_of, angles, weights], axis=1).astype(jnp.bfloat16)
    label_lanes = 128
    labels = jnp.pad(labels, ((0, 0), (0, label_lanes - labels.shape[1])))
    own_rows = jnp.concatenate([own_rows, labels], axis=1)
    outgoing = jnp.dot(placement, own_rows, preferred_element_type=jnp.float32).astype(jnp.bfloat16)
    outgoing = outgoing.reshape(owner_count, capacity, flat_len + label_lanes)
    pieces, outgoing = staged_gather(angle_major(references), "loop", outgoing)
    incoming = lax.all_to_all(outgoing, "loop", split_axis=0, concat_axis=0, tiled=True)
    highest, summed = score_all(particle_rows, pieces)
    stats = lax.all_gather(jnp.stack([highest, summed], axis=0), "grp", axis=0, tiled=False)
    stats = lax.dynamic_slice_in_dim(stats, grp_index * half_rows, half_rows, 2)
    highest = jnp.max(stats[:, 0], axis=0)
    summed = jnp.sum(stats[:, 1] * jnp.exp(stats[:, 0] - highest[None, :]), axis=0)
    log_evidence = highest + jnp.log(summed)
    incoming, log_evidence = lax.optimization_barrier((incoming, log_evidence))
    incoming = incoming.reshape(slot_count, flat_len + label_lanes)
    labels_in = incoming[:, flat_len : flat_len + 3]
    labels_in = labels_in.astype(jnp.float32)
    member_in = labels_in[:, 0]
    rotation = labels_in[:, 1]
    weight_of = labels_in[:, 2]
    block = -(-per_owner // 8) * 8
    angle_grid = jnp.arange(ANGLES, dtype=jnp.float32)
    member_grid = jnp.arange(block, dtype=jnp.float32)
    chosen = (angle_grid[:, None, None] == rotation[None, None, :]) & (
        member_grid[None, :, None] == member_in[None, None, :]
    )
    by_angle = jnp.where(chosen, weight_of[None, None, :], 0.0).astype(jnp.bfloat16)
    by_angle = by_angle.reshape(ANGLES * block, slot_count)
    partial_sums = pl.pallas_call(
        average_kernel,
        out_shape=jax.ShapeDtypeStruct((block, flat_len), jnp.float32),
        scratch_shapes=[pltpu.VMEM((ANGLES * block, flat_len), jnp.float32)],
    )(by_angle, incoming)
    partial_sums = partial_sums[:per_owner].reshape(per_owner, ANGLES, RADII).transpose(0, 2, 1)
    partial_sums = partial_sums.reshape(per_owner, flat_len)
    weighted = (member_grid[:per_owner, None] == member_in[None, :]).astype(jnp.float32) * weight_of[None, :]
    partial_weight = jnp.sum(weighted, axis=1)
    class_sums, class_weight = lax.psum((partial_sums, partial_weight), "grp")
    class_sums = lax.dynamic_slice_in_dim(class_sums, grp_index * references.shape[0], references.shape[0], 0)
    class_weight = lax.dynamic_slice_in_dim(class_weight, grp_index * references.shape[0], references.shape[0], 0)
    class_average = class_sums / class_weight[:, None]
    return (log_evidence, class_average)


def solution(mesh):
    return jax.shard_map(
        local,
        mesh=mesh,
        in_specs=(
            P("loop", None),
            P(("loop", "grp"), None),
            P(("loop", "grp")),
            P(("loop", "grp")),
            P(("loop", "grp")),
        ),
        out_specs=(P(("loop", "grp")), P(("loop", "grp"), None)),
        check_vma=False,
    )
```

```python
import functools
import math

import jax
import jax.numpy as jnp
from jax import lax
from jax.experimental import pallas as pl
from jax.experimental.pallas import tpu as pltpu
from jax.sharding import PartitionSpec as P

RADII = 48
ANGLES = 72


score_factor = 2.0


def angle_major(rows):
    count = rows.shape[0]
    return rows.reshape(count, RADII, ANGLES).transpose(0, 2, 1).reshape(count, RADII * ANGLES)


def score_kernel(*refs, scale):
    p_ref, piece_refs = refs[0], refs[1:-4]
    max_ref, sum_ref, r_scr, s_scr = refs[-4:]
    flat_len = p_ref.shape[1]
    columns = jnp.concatenate([piece[...] for piece in piece_refs], axis=0).T
    r_scr[pl.ds(0, flat_len), :] = columns
    r_scr[pl.ds(flat_len, flat_len), :] = columns
    images = p_ref[...]
    half = ANGLES // 2

    def shift_scores(s, carry):
        turned = jnp.concatenate(
            [
                r_scr[pl.ds(pl.multiple_of(s * RADII, 16), flat_len), :],
                r_scr[pl.ds(pl.multiple_of((s + half) * RADII, 16), flat_len), :],
            ],
            axis=1,
        )
        scores = jnp.dot(images, turned, preferred_element_type=jnp.float32) * scale
        s_scr[s] = scores
        return jnp.maximum(carry, scores)

    first = jnp.full(s_scr.shape[1:], -jnp.inf, jnp.float32)
    lane_max = lax.fori_loop(0, half, shift_scores, first, unroll=9)
    highest = jnp.max(lane_max.T, axis=0, keepdims=True)
    highest_col = jnp.max(lane_max, axis=1, keepdims=True)

    def shift_sum(s, carry):
        return carry + jnp.exp(s_scr[s] - highest_col)

    lane_sum = lax.fori_loop(0, half, shift_sum, jnp.zeros(s_scr.shape[1:], jnp.float32), unroll=4)
    max_ref[...] = highest
    sum_ref[...] = jnp.sum(lane_sum.T, axis=0, keepdims=True)


def score_all(lhs, pieces):
    row_count, flat_len = lhs.shape
    ref_count = sum(piece.shape[0] for piece in pieces)
    scale = score_factor / math.sqrt(flat_len)
    highest, summed = pl.pallas_call(
        functools.partial(score_kernel, scale=scale),
        out_shape=(
            jax.ShapeDtypeStruct((1, row_count), jnp.float32),
            jax.ShapeDtypeStruct((1, row_count), jnp.float32),
        ),
        scratch_shapes=[
            pltpu.VMEM((2 * flat_len, ref_count), jnp.bfloat16),
            pltpu.VMEM((ANGLES // 2, row_count, 2 * ref_count), jnp.float32),
        ],
    )(lhs, *pieces)
    return highest[0], summed[0]


def average_kernel(x_ref, o_ref, w_out_ref, w_scr, s_scr):
    block = o_ref.shape[0]
    flat_len = o_ref.shape[1]
    labels = x_ref[:, flat_len:].astype(jnp.float32).T
    member, rotation, weight = labels[0:1, :], labels[1:2, :], labels[2:3, :]
    row = lax.broadcasted_iota(jnp.int32, w_scr.shape, 0)
    chosen = ((row // block).astype(jnp.float32) == rotation) & ((row % block).astype(jnp.float32) == member)
    w_scr[...] = jnp.where(chosen, weight, 0.0).astype(w_scr.dtype)
    class_row = lax.broadcasted_iota(jnp.int32, (block, x_ref.shape[0]), 0).astype(jnp.float32)
    w_out_ref[...] = jnp.sum(jnp.where(class_row == member, weight, 0.0), axis=1, keepdims=True)
    s_scr[...] = jnp.dot(w_scr[...], x_ref[:, :flat_len], preferred_element_type=jnp.float32)
    step = 8
    total = None
    for part in range(step):
        partial = None
        for whole in range(ANGLES // step):
            angle = whole * step + part
            rows = s_scr[pl.ds(angle * block, block), :]
            if whole:
                rows = pltpu.roll(rows, whole * step * RADII, 1)
            partial = rows if partial is None else partial + rows
        if part:
            partial = pltpu.roll(partial, part * RADII, 1)
        total = partial if total is None else total + partial
    o_ref[...] = total


def ring_factors(count):
    factors = []
    while count > 1:
        factor = 4 if count % 4 == 0 else count
        factors.append(factor)
        count //= factor
    return factors


def staged_gather(rows, axis, held):
    count = lax.axis_size(axis)
    stride = 1
    factors = ring_factors(count)
    for round_index, factor in enumerate(factors):
        parts = [rows]
        for step in range(1, factor):
            pairs = []
            for source in range(count):
                digit = (source // stride) % factor
                pairs.append((source, source + ((digit + step) % factor - digit) * stride))
            parts.append(lax.ppermute(rows, axis, pairs))
        rows = jnp.concatenate(parts, axis=0)
        if round_index == len(factors) - 1:
            parts, held = lax.optimization_barrier((parts, held))
        stride *= factor
    return parts, held


def local(particles, references, classes, angles, weights):
    row_count, flat_len = particles.shape
    grp_size = lax.axis_size("grp")
    half_rows = row_count // grp_size
    grp_index = lax.axis_index("grp")
    particle_rows = angle_major(particles)
    own_rows = lax.dynamic_slice_in_dim(particle_rows, grp_index * half_rows, half_rows, 0)
    owner_count = lax.axis_size("loop")
    per_owner = references.shape[0] * grp_size
    capacity = max(2, row_count // owner_count)
    slot_count = owner_count * capacity
    owner_of = classes // per_owner
    member_of = classes % per_owner
    owner_hits = (owner_of[:, None] == jnp.arange(owner_count, dtype=jnp.int32)[None, :]).astype(
        jnp.int32
    )
    earlier = jnp.cumsum(owner_hits, axis=0) - owner_hits
    slot_index = jnp.sum(earlier * owner_hits, axis=1)
    target_slot = owner_of * capacity + slot_index
    placement = (jnp.arange(slot_count, dtype=jnp.int32)[:, None] == target_slot[None, :]).astype(
        jnp.bfloat16
    )
    labels = jnp.stack([member_of, angles, weights], axis=1).astype(jnp.bfloat16)
    label_lanes = 128
    labels = jnp.pad(labels, ((0, 0), (0, label_lanes - labels.shape[1])))
    own_rows = jnp.concatenate([own_rows, labels], axis=1)
    outgoing = jnp.dot(placement, own_rows, preferred_element_type=jnp.float32).astype(jnp.bfloat16)
    outgoing = outgoing.reshape(owner_count, capacity, flat_len + label_lanes)
    pieces, outgoing = staged_gather(angle_major(references), "loop", outgoing)
    incoming = lax.all_to_all(outgoing, "loop", split_axis=0, concat_axis=0, tiled=True)
    highest, summed = score_all(particle_rows, pieces)
    incoming, highest, summed = lax.optimization_barrier((incoming, highest, summed))
    incoming = incoming.reshape(slot_count, flat_len + label_lanes)
    block = -(-per_owner // 8) * 8
    partial_sums, partial_weight = pl.pallas_call(
        average_kernel,
        out_shape=(
            jax.ShapeDtypeStruct((block, flat_len), jnp.float32),
            jax.ShapeDtypeStruct((block, 1), jnp.float32),
        ),
        scratch_shapes=[
            pltpu.VMEM((ANGLES * block, slot_count), jnp.bfloat16),
            pltpu.VMEM((ANGLES * block, flat_len), jnp.float32),
        ],
    )(incoming)
    partial_sums = partial_sums[:per_owner].reshape(per_owner, ANGLES, RADII).transpose(0, 2, 1)
    partial_sums = partial_sums.reshape(per_owner, flat_len)
    partial_weight = partial_weight[:per_owner, 0]
    stats = jnp.stack([highest, summed], axis=0)
    slots = jnp.arange(grp_size, dtype=jnp.int32)[:, None, None] == grp_index
    stats = jnp.where(slots, stats[None], 0.0)
    partial_sums, partial_weight, stats = lax.psum((partial_sums, partial_weight, stats), "grp")
    class_sums = lax.dynamic_slice_in_dim(partial_sums, grp_index * references.shape[0], references.shape[0], 0)
    class_weight = lax.dynamic_slice_in_dim(partial_weight, grp_index * references.shape[0], references.shape[0], 0)
    class_average = class_sums / class_weight[:, None]
    stats = lax.dynamic_slice_in_dim(stats, grp_index * half_rows, half_rows, 2)
    highest = jnp.max(stats[:, 0], axis=0)
    summed = jnp.sum(stats[:, 1] * jnp.exp(stats[:, 0] - highest[None, :]), axis=0)
    log_evidence = highest + jnp.log(summed)
    return (log_evidence, class_average)


def solution(mesh):
    return jax.shard_map(
        local,
        mesh=mesh,
        in_specs=(
            P("loop", None),
            P(("loop", "grp"), None),
            P(("loop", "grp")),
            P(("loop", "grp")),
            P(("loop", "grp")),
        ),
        out_specs=(P(("loop", "grp")), P(("loop", "grp"), None)),
        check_vma=False,
    )
```

```python
import functools
import math

import jax
import jax.numpy as jnp
from jax import lax
from jax.experimental import pallas as pl
from jax.experimental.pallas import tpu as pltpu
from jax.sharding import PartitionSpec as P

RADII = 48
ANGLES = 72


score_factor = 2.0


def angle_major(rows):
    count = rows.shape[0]
    return rows.reshape(count, RADII, ANGLES).transpose(0, 2, 1).reshape(count, RADII * ANGLES)


def score_kernel(*refs, scale):
    p_ref, piece_refs = refs[0], refs[1:-4]
    max_ref, sum_ref, r_scr, s_scr = refs[-4:]
    flat_len = p_ref.shape[1]
    columns = jnp.concatenate([piece[...] for piece in piece_refs], axis=0).T
    r_scr[pl.ds(0, flat_len), :] = columns
    r_scr[pl.ds(flat_len, flat_len), :] = columns
    images = p_ref[...]
    half = ANGLES // 2

    def shift_scores(s, carry):
        turned = jnp.concatenate(
            [
                r_scr[pl.ds(pl.multiple_of(s * RADII, 16), flat_len), :],
                r_scr[pl.ds(pl.multiple_of((s + half) * RADII, 16), flat_len), :],
            ],
            axis=1,
        )
        scores = jnp.dot(images, turned, preferred_element_type=jnp.float32) * scale
        s_scr[s] = scores
        return jnp.maximum(carry, scores)

    first = jnp.full(s_scr.shape[1:], -jnp.inf, jnp.float32)
    lane_max = lax.fori_loop(0, half, shift_scores, first, unroll=9)
    highest = jnp.max(lane_max.T, axis=0, keepdims=True)
    highest_col = jnp.max(lane_max, axis=1, keepdims=True)

    def shift_sum(s, carry):
        return carry + jnp.exp(s_scr[s] - highest_col)

    lane_sum = lax.fori_loop(0, half, shift_sum, jnp.zeros(s_scr.shape[1:], jnp.float32), unroll=4)
    max_ref[...] = highest
    sum_ref[...] = jnp.sum(lane_sum.T, axis=0, keepdims=True)


def score_all(lhs, pieces):
    row_count, flat_len = lhs.shape
    ref_count = sum(piece.shape[0] for piece in pieces)
    scale = score_factor / math.sqrt(flat_len)
    highest, summed = pl.pallas_call(
        functools.partial(score_kernel, scale=scale),
        out_shape=(
            jax.ShapeDtypeStruct((1, row_count), jnp.float32),
            jax.ShapeDtypeStruct((1, row_count), jnp.float32),
        ),
        scratch_shapes=[
            pltpu.VMEM((2 * flat_len, ref_count), jnp.bfloat16),
            pltpu.VMEM((ANGLES // 2, row_count, 2 * ref_count), jnp.float32),
        ],
    )(lhs, *pieces)
    return highest[0], summed[0]


def average_kernel(w_ref, x_ref, o_ref, s_scr):
    block = o_ref.shape[0]
    flat_len = o_ref.shape[1]
    s_scr[...] = jnp.dot(w_ref[...], x_ref[:, :flat_len], preferred_element_type=jnp.float32)
    step = 8
    total = None
    for part in range(step):
        partial = None
        for whole in range(ANGLES // step):
            angle = whole * step + part
            rows = s_scr[pl.ds(angle * block, block), :]
            if whole:
                rows = pltpu.roll(rows, whole * step * RADII, 1)
            partial = rows if partial is None else partial + rows
        if part:
            partial = pltpu.roll(partial, part * RADII, 1)
        total = partial if total is None else total + partial
    o_ref[...] = total


def ring_factors(count):
    factors = []
    while count > 1:
        factor = 4 if count % 4 == 0 else count
        factors.append(factor)
        count //= factor
    return factors


def staged_gather(rows, axis, held):
    count = lax.axis_size(axis)
    stride = 1
    factors = ring_factors(count)
    for round_index, factor in enumerate(factors):
        parts = [rows]
        for step in range(1, factor):
            pairs = []
            for source in range(count):
                digit = (source // stride) % factor
                pairs.append((source, source + ((digit + step) % factor - digit) * stride))
            parts.append(lax.ppermute(rows, axis, pairs))
        rows = jnp.concatenate(parts, axis=0)
        if round_index == len(factors) - 1:
            parts, held = lax.optimization_barrier((parts, held))
        stride *= factor
    return parts, held


def local(particles, references, classes, angles, weights):
    row_count, flat_len = particles.shape
    grp_size = lax.axis_size("grp")
    half_rows = row_count // grp_size
    grp_index = lax.axis_index("grp")
    particle_rows = angle_major(particles)
    own_rows = lax.dynamic_slice_in_dim(particle_rows, grp_index * half_rows, half_rows, 0)
    owner_count = lax.axis_size("loop")
    per_owner = references.shape[0] * grp_size
    capacity = max(2, row_count // owner_count)
    slot_count = owner_count * capacity
    owner_of = classes // per_owner
    member_of = classes % per_owner
    owner_hits = (owner_of[:, None] == jnp.arange(owner_count, dtype=jnp.int32)[None, :]).astype(
        jnp.int32
    )
    earlier = jnp.cumsum(owner_hits, axis=0) - owner_hits
    slot_index = jnp.sum(earlier * owner_hits, axis=1)
    target_slot = owner_of * capacity + slot_index
    placement = (jnp.arange(slot_count, dtype=jnp.int32)[:, None] == target_slot[None, :]).astype(
        jnp.bfloat16
    )
    labels = jnp.stack([member_of, angles, weights], axis=1).astype(jnp.bfloat16)
    label_lanes = 128
    labels = jnp.pad(labels, ((0, 0), (0, label_lanes - labels.shape[1])))
    own_rows = jnp.concatenate([own_rows, labels], axis=1)
    outgoing = jnp.dot(placement, own_rows, preferred_element_type=jnp.float32).astype(jnp.bfloat16)
    outgoing = outgoing.reshape(owner_count, capacity, flat_len + label_lanes)
    pieces, outgoing = staged_gather(angle_major(references), "loop", outgoing)
    incoming = lax.all_to_all(outgoing, "loop", split_axis=0, concat_axis=0, tiled=True)
    highest, summed = score_all(particle_rows, pieces)
    incoming, highest, summed = lax.optimization_barrier((incoming, highest, summed))
    incoming = incoming.reshape(slot_count, flat_len + label_lanes)
    labels_in = incoming[:, flat_len : flat_len + 3]
    labels_in = labels_in.astype(jnp.float32)
    member_in = labels_in[:, 0]
    rotation = labels_in[:, 1]
    weight_of = labels_in[:, 2]
    block = -(-per_owner // 8) * 8
    angle_grid = jnp.arange(ANGLES, dtype=jnp.float32)
    member_grid = jnp.arange(block, dtype=jnp.float32)
    chosen = (angle_grid[:, None, None] == rotation[None, None, :]) & (
        member_grid[None, :, None] == member_in[None, None, :]
    )
    by_angle = jnp.where(chosen, weight_of[None, None, :], 0.0).astype(jnp.bfloat16)
    by_angle = by_angle.reshape(ANGLES * block, slot_count)
    partial_sums = pl.pallas_call(
        average_kernel,
        out_shape=jax.ShapeDtypeStruct((block, flat_len), jnp.float32),
        scratch_shapes=[pltpu.VMEM((ANGLES * block, flat_len), jnp.float32)],
    )(by_angle, incoming)
    partial_sums = partial_sums[:per_owner].reshape(per_owner, ANGLES, RADII).transpose(0, 2, 1)
    partial_sums = partial_sums.reshape(per_owner, flat_len)
    weighted = (member_grid[:per_owner, None] == member_in[None, :]).astype(jnp.float32) * weight_of[None, :]
    partial_weight = jnp.sum(weighted, axis=1)
    own_classes = references.shape[0]
    stats = jnp.stack([highest, summed], axis=0)
    if grp_size == 2:
        partner = 1 - grp_index
        weight_row = jnp.zeros((1, flat_len), jnp.float32)
        weight_row = lax.dynamic_update_slice_in_dim(
            weight_row, lax.dynamic_slice_in_dim(partial_weight, partner * own_classes, own_classes, 0)[None], 0, 1
        )
        stat_rows = jnp.pad(
            lax.dynamic_slice_in_dim(stats, partner * half_rows, half_rows, 1), ((0, 0), (0, flat_len - half_rows))
        )
        sent = jnp.concatenate(
            [lax.dynamic_slice_in_dim(partial_sums, partner * own_classes, own_classes, 0), weight_row, stat_rows], axis=0
        )
        got = lax.ppermute(sent, "grp", [(0, 1), (1, 0)])
        class_sums = lax.dynamic_slice_in_dim(partial_sums, grp_index * own_classes, own_classes, 0) + got[:own_classes]
        class_weight = (
            lax.dynamic_slice_in_dim(partial_weight, grp_index * own_classes, own_classes, 0)
            + got[own_classes, :own_classes]
        )
        stats = jnp.stack(
            [lax.dynamic_slice_in_dim(stats, grp_index * half_rows, half_rows, 1), got[own_classes + 1 :, :half_rows]],
            axis=0,
        )
    else:
        slots = jnp.arange(grp_size, dtype=jnp.int32)[:, None, None] == grp_index
        stats = jnp.where(slots, stats[None], 0.0)
        partial_sums, partial_weight, stats = lax.psum((partial_sums, partial_weight, stats), "grp")
        class_sums = lax.dynamic_slice_in_dim(partial_sums, grp_index * own_classes, own_classes, 0)
        class_weight = lax.dynamic_slice_in_dim(partial_weight, grp_index * own_classes, own_classes, 0)
        stats = lax.dynamic_slice_in_dim(stats, grp_index * half_rows, half_rows, 2)
    class_average = class_sums / class_weight[:, None]
    highest = jnp.max(stats[:, 0], axis=0)
    summed = jnp.sum(stats[:, 1] * jnp.exp(stats[:, 0] - highest[None, :]), axis=0)
    log_evidence = highest + jnp.log(summed)
    return (log_evidence, class_average)


def solution(mesh):
    return jax.shard_map(
        local,
        mesh=mesh,
        in_specs=(
            P("loop", None),
            P(("loop", "grp"), None),
            P(("loop", "grp")),
            P(("loop", "grp")),
            P(("loop", "grp")),
        ),
        out_specs=(P(("loop", "grp")), P(("loop", "grp"), None)),
        check_vma=False,
    )
```

```python
import functools
import math

import jax
import jax.numpy as jnp
from jax import lax
from jax.experimental import pallas as pl
from jax.experimental.pallas import tpu as pltpu
from jax.sharding import PartitionSpec as P

RADII = 48
ANGLES = 72


score_factor = 2.0


def angle_major(rows):
    count = rows.shape[0]
    return rows.reshape(count, RADII, ANGLES).transpose(0, 2, 1).reshape(count, RADII * ANGLES)


def angle_major_kernel(x_ref, o_ref, t_scr, a_scr):
    t_scr[...] = x_ref[...].astype(jnp.float32).T
    for angle in range(ANGLES):
        a_scr[pl.ds(angle * RADII, RADII), :] = t_scr[pl.ds(angle, RADII, stride=ANGLES), :]
    o_ref[...] = a_scr[...].T.astype(o_ref.dtype)


def angle_major_rows(rows):
    count, flat_len = rows.shape
    return pl.pallas_call(
        angle_major_kernel,
        out_shape=jax.ShapeDtypeStruct((count, flat_len), rows.dtype),
        scratch_shapes=[
            pltpu.VMEM((flat_len, count), jnp.float32),
            pltpu.VMEM((flat_len, count), jnp.float32),
        ],
    )(rows)


def score_kernel(*refs, scale):
    p_ref, piece_refs = refs[0], refs[1:-4]
    max_ref, sum_ref, r_scr, s_scr = refs[-4:]
    flat_len = p_ref.shape[1]
    columns = jnp.concatenate([piece[...] for piece in piece_refs], axis=0).T
    r_scr[pl.ds(0, flat_len), :] = columns
    r_scr[pl.ds(flat_len, flat_len), :] = columns
    images = p_ref[...]
    half = ANGLES // 2

    def shift_scores(s, carry):
        turned = jnp.concatenate(
            [
                r_scr[pl.ds(pl.multiple_of(s * RADII, 16), flat_len), :],
                r_scr[pl.ds(pl.multiple_of((s + half) * RADII, 16), flat_len), :],
            ],
            axis=1,
        )
        scores = jnp.dot(images, turned, preferred_element_type=jnp.float32) * scale
        s_scr[s] = scores
        return jnp.maximum(carry, scores)

    first = jnp.full(s_scr.shape[1:], -jnp.inf, jnp.float32)
    lane_max = lax.fori_loop(0, half, shift_scores, first, unroll=9)
    highest = jnp.max(lane_max.T, axis=0, keepdims=True)
    highest_col = jnp.max(lane_max, axis=1, keepdims=True)

    def shift_sum(s, carry):
        return carry + jnp.exp(s_scr[s] - highest_col)

    lane_sum = lax.fori_loop(0, half, shift_sum, jnp.zeros(s_scr.shape[1:], jnp.float32), unroll=4)
    max_ref[...] = highest
    sum_ref[...] = jnp.sum(lane_sum.T, axis=0, keepdims=True)


def score_all(lhs, pieces):
    row_count, flat_len = lhs.shape
    ref_count = sum(piece.shape[0] for piece in pieces)
    scale = score_factor / math.sqrt(flat_len)
    highest, summed = pl.pallas_call(
        functools.partial(score_kernel, scale=scale),
        out_shape=(
            jax.ShapeDtypeStruct((1, row_count), jnp.float32),
            jax.ShapeDtypeStruct((1, row_count), jnp.float32),
        ),
        scratch_shapes=[
            pltpu.VMEM((2 * flat_len, ref_count), jnp.bfloat16),
            pltpu.VMEM((ANGLES // 2, row_count, 2 * ref_count), jnp.float32),
        ],
    )(lhs, *pieces)
    return highest[0], summed[0]


def average_kernel(w_ref, x_ref, o_ref, s_scr):
    block = o_ref.shape[0]
    flat_len = o_ref.shape[1]
    s_scr[...] = jnp.dot(w_ref[...], x_ref[:, :flat_len], preferred_element_type=jnp.float32)
    step = 8
    total = None
    for part in range(step):
        partial = None
        for whole in range(ANGLES // step):
            angle = whole * step + part
            rows = s_scr[pl.ds(angle * block, block), :]
            if whole:
                rows = pltpu.roll(rows, whole * step * RADII, 1)
            partial = rows if partial is None else partial + rows
        if part:
            partial = pltpu.roll(partial, part * RADII, 1)
        total = partial if total is None else total + partial
    o_ref[...] = total


def ring_factors(count):
    factors = []
    while count > 1:
        factor = 4 if count % 4 == 0 else count
        factors.append(factor)
        count //= factor
    return factors


def staged_gather(rows, axis, held):
    count = lax.axis_size(axis)
    stride = 1
    factors = ring_factors(count)
    for round_index, factor in enumerate(factors):
        parts = [rows]
        for step in range(1, factor):
            pairs = []
            for source in range(count):
                digit = (source // stride) % factor
                pairs.append((source, source + ((digit + step) % factor - digit) * stride))
            parts.append(lax.ppermute(rows, axis, pairs))
        rows = jnp.concatenate(parts, axis=0)
        if round_index == len(factors) - 1:
            parts, held = lax.optimization_barrier((parts, held))
        stride *= factor
    return parts, held


def local(particles, references, classes, angles, weights):
    row_count, flat_len = particles.shape
    grp_size = lax.axis_size("grp")
    half_rows = row_count // grp_size
    grp_index = lax.axis_index("grp")
    particle_rows = angle_major_rows(particles)
    own_rows = lax.dynamic_slice_in_dim(particle_rows, grp_index * half_rows, half_rows, 0)
    owner_count = lax.axis_size("loop")
    per_owner = references.shape[0] * grp_size
    capacity = max(2, row_count // owner_count)
    slot_count = owner_count * capacity
    owner_of = classes // per_owner
    member_of = classes % per_owner
    owner_hits = (owner_of[:, None] == jnp.arange(owner_count, dtype=jnp.int32)[None, :]).astype(
        jnp.int32
    )
    earlier = jnp.cumsum(owner_hits, axis=0) - owner_hits
    slot_index = jnp.sum(earlier * owner_hits, axis=1)
    target_slot = owner_of * capacity + slot_index
    placement = (jnp.arange(slot_count, dtype=jnp.int32)[:, None] == target_slot[None, :]).astype(
        jnp.bfloat16
    )
    labels = jnp.stack([member_of, angles, weights], axis=1).astype(jnp.bfloat16)
    label_lanes = 128
    labels = jnp.pad(labels, ((0, 0), (0, label_lanes - labels.shape[1])))
    own_rows = jnp.concatenate([own_rows, labels], axis=1)
    outgoing = jnp.dot(placement, own_rows, preferred_element_type=jnp.float32).astype(jnp.bfloat16)
    outgoing = outgoing.reshape(owner_count, capacity, flat_len + label_lanes)
    pieces, outgoing = staged_gather(angle_major(references), "loop", outgoing)
    incoming = lax.all_to_all(outgoing, "loop", split_axis=0, concat_axis=0, tiled=True)
    highest, summed = score_all(particle_rows, pieces)
    incoming, highest, summed = lax.optimization_barrier((incoming, highest, summed))
    incoming = incoming.reshape(slot_count, flat_len + label_lanes)
    labels_in = incoming[:, flat_len : flat_len + 3]
    labels_in = labels_in.astype(jnp.float32)
    member_in = labels_in[:, 0]
    rotation = labels_in[:, 1]
    weight_of = labels_in[:, 2]
    block = -(-per_owner // 8) * 8
    angle_grid = jnp.arange(ANGLES, dtype=jnp.float32)
    member_grid = jnp.arange(block, dtype=jnp.float32)
    chosen = (angle_grid[:, None, None] == rotation[None, None, :]) & (
        member_grid[None, :, None] == member_in[None, None, :]
    )
    by_angle = jnp.where(chosen, weight_of[None, None, :], 0.0).astype(jnp.bfloat16)
    by_angle = by_angle.reshape(ANGLES * block, slot_count)
    partial_sums = pl.pallas_call(
        average_kernel,
        out_shape=jax.ShapeDtypeStruct((block, flat_len), jnp.float32),
        scratch_shapes=[pltpu.VMEM((ANGLES * block, flat_len), jnp.float32)],
    )(by_angle, incoming)
    partial_sums = partial_sums[:per_owner].reshape(per_owner, ANGLES, RADII).transpose(0, 2, 1)
    partial_sums = partial_sums.reshape(per_owner, flat_len)
    weighted = (member_grid[:per_owner, None] == member_in[None, :]).astype(jnp.float32) * weight_of[None, :]
    partial_weight = jnp.sum(weighted, axis=1)
    own_classes = references.shape[0]
    stats = jnp.stack([highest, summed], axis=0)
    if grp_size == 2:
        partner = 1 - grp_index
        weight_row = jnp.zeros((1, flat_len), jnp.float32)
        weight_row = lax.dynamic_update_slice_in_dim(
            weight_row, lax.dynamic_slice_in_dim(partial_weight, partner * own_classes, own_classes, 0)[None], 0, 1
        )
        stat_rows = jnp.pad(
            lax.dynamic_slice_in_dim(stats, partner * half_rows, half_rows, 1), ((0, 0), (0, flat_len - half_rows))
        )
        sent = jnp.concatenate(
            [lax.dynamic_slice_in_dim(partial_sums, partner * own_classes, own_classes, 0), weight_row, stat_rows], axis=0
        )
        got = lax.ppermute(sent, "grp", [(0, 1), (1, 0)])
        class_sums = lax.dynamic_slice_in_dim(partial_sums, grp_index * own_classes, own_classes, 0) + got[:own_classes]
        class_weight = (
            lax.dynamic_slice_in_dim(partial_weight, grp_index * own_classes, own_classes, 0)
            + got[own_classes, :own_classes]
        )
        stats = jnp.stack(
            [lax.dynamic_slice_in_dim(stats, grp_index * half_rows, half_rows, 1), got[own_classes + 1 :, :half_rows]],
            axis=0,
        )
    else:
        slots = jnp.arange(grp_size, dtype=jnp.int32)[:, None, None] == grp_index
        stats = jnp.where(slots, stats[None], 0.0)
        partial_sums, partial_weight, stats = lax.psum((partial_sums, partial_weight, stats), "grp")
        class_sums = lax.dynamic_slice_in_dim(partial_sums, grp_index * own_classes, own_classes, 0)
        class_weight = lax.dynamic_slice_in_dim(partial_weight, grp_index * own_classes, own_classes, 0)
        stats = lax.dynamic_slice_in_dim(stats, grp_index * half_rows, half_rows, 2)
    class_average = class_sums / class_weight[:, None]
    highest = jnp.max(stats[:, 0], axis=0)
    summed = jnp.sum(stats[:, 1] * jnp.exp(stats[:, 0] - highest[None, :]), axis=0)
    log_evidence = highest + jnp.log(summed)
    return (log_evidence, class_average)


def solution(mesh):
    return jax.shard_map(
        local,
        mesh=mesh,
        in_specs=(
            P("loop", None),
            P(("loop", "grp"), None),
            P(("loop", "grp")),
            P(("loop", "grp")),
            P(("loop", "grp")),
        ),
        out_specs=(P(("loop", "grp")), P(("loop", "grp"), None)),
        check_vma=False,
    )
```

```python
import functools
import math

import jax
import jax.numpy as jnp
from jax import lax
from jax.experimental import pallas as pl
from jax.experimental.pallas import tpu as pltpu
from jax.sharding import PartitionSpec as P

RADII = 48
ANGLES = 72


score_factor = 2.0


def angle_major(rows):
    count = rows.shape[0]
    return rows.reshape(count, RADII, ANGLES).transpose(0, 2, 1).reshape(count, RADII * ANGLES)


def score_kernel(*refs, scale):
    p_ref, piece_refs = refs[0], refs[1:-4]
    max_ref, sum_ref, r_scr, s_scr = refs[-4:]
    flat_len = p_ref.shape[1]
    columns = jnp.concatenate([piece[...] for piece in piece_refs], axis=0).T
    r_scr[pl.ds(0, flat_len), :] = columns
    r_scr[pl.ds(flat_len, flat_len), :] = columns
    images = p_ref[...]
    half = ANGLES // 2

    def shift_scores(s, carry):
        turned = jnp.concatenate(
            [
                r_scr[pl.ds(pl.multiple_of(s * RADII, 16), flat_len), :],
                r_scr[pl.ds(pl.multiple_of((s + half) * RADII, 16), flat_len), :],
            ],
            axis=1,
        )
        scores = jnp.dot(images, turned, preferred_element_type=jnp.float32) * scale
        s_scr[s] = scores
        return jnp.maximum(carry, scores)

    first = jnp.full(s_scr.shape[1:], -jnp.inf, jnp.float32)
    lane_max = lax.fori_loop(0, half, shift_scores, first, unroll=9)
    highest = jnp.max(lane_max.T, axis=0, keepdims=True)
    highest_col = jnp.max(lane_max, axis=1, keepdims=True)

    def shift_sum(s, carry):
        return carry + jnp.exp(s_scr[s] - highest_col)

    lane_sum = lax.fori_loop(0, half, shift_sum, jnp.zeros(s_scr.shape[1:], jnp.float32), unroll=4)
    max_ref[...] = highest
    sum_ref[...] = jnp.sum(lane_sum.T, axis=0, keepdims=True)


def score_all(lhs, pieces):
    row_count, flat_len = lhs.shape
    ref_count = sum(piece.shape[0] for piece in pieces)
    scale = score_factor / math.sqrt(flat_len)
    highest, summed = pl.pallas_call(
        functools.partial(score_kernel, scale=scale),
        out_shape=(
            jax.ShapeDtypeStruct((1, row_count), jnp.float32),
            jax.ShapeDtypeStruct((1, row_count), jnp.float32),
        ),
        scratch_shapes=[
            pltpu.VMEM((2 * flat_len, ref_count), jnp.bfloat16),
            pltpu.VMEM((ANGLES // 2, row_count, 2 * ref_count), jnp.float32),
        ],
    )(lhs, *pieces)
    return highest[0], summed[0]


def average_kernel(w_ref, x_ref, o_ref, s_scr):
    block = o_ref.shape[0]
    flat_len = o_ref.shape[1]
    s_scr[...] = jnp.dot(w_ref[...], x_ref[:, :flat_len], preferred_element_type=jnp.float32)
    step = 8
    total = None
    for part in range(step):
        partial = None
        for whole in range(ANGLES // step):
            angle = whole * step + part
            rows = s_scr[pl.ds(angle * block, block), :]
            if whole:
                rows = pltpu.roll(rows, whole * step * RADII, 1)
            partial = rows if partial is None else partial + rows
        if part:
            partial = pltpu.roll(partial, part * RADII, 1)
        total = partial if total is None else total + partial
    o_ref[...] = total


def ring_factors(count):
    factors = []
    while count > 1:
        factor = 4 if count % 4 == 0 else count
        factors.append(factor)
        count //= factor
    return factors


def ring_pairs(count, stride, factor, step):
    pairs = []
    for source in range(count):
        digit = (source // stride) % factor
        pairs.append((source, source + ((digit + step) % factor - digit) * stride))
    return pairs


def staged_gather(rows, axis, held):
    count = lax.axis_size(axis)
    stride = 1
    factors = ring_factors(count)
    for round_index, factor in enumerate(factors):
        if factor == 4 and round_index < len(factors) - 1:
            from_below = lax.ppermute(rows, axis, ring_pairs(count, stride, factor, 1))
            from_above = lax.ppermute(rows, axis, ring_pairs(count, stride, factor, factor - 1))
            two_below = lax.ppermute(from_below, axis, ring_pairs(count, stride, factor, 1))
            parts = [rows, from_below, two_below, from_above]
        else:
            parts = [rows]
            for step in range(1, factor):
                parts.append(lax.ppermute(rows, axis, ring_pairs(count, stride, factor, step)))
        rows = jnp.concatenate(parts, axis=0)
        if round_index == len(factors) - 1:
            parts, held = lax.optimization_barrier((parts, held))
        stride *= factor
    return parts, held


def local(particles, references, classes, angles, weights):
    row_count, flat_len = particles.shape
    grp_size = lax.axis_size("grp")
    half_rows = row_count // grp_size
    grp_index = lax.axis_index("grp")
    particle_rows = angle_major(particles)
    own_rows = lax.dynamic_slice_in_dim(particle_rows, grp_index * half_rows, half_rows, 0)
    owner_count = lax.axis_size("loop")
    per_owner = references.shape[0] * grp_size
    capacity = max(2, row_count // owner_count)
    slot_count = owner_count * capacity
    owner_of = classes // per_owner
    member_of = classes % per_owner
    owner_hits = (owner_of[:, None] == jnp.arange(owner_count, dtype=jnp.int32)[None, :]).astype(
        jnp.int32
    )
    earlier = jnp.cumsum(owner_hits, axis=0) - owner_hits
    slot_index = jnp.sum(earlier * owner_hits, axis=1)
    target_slot = owner_of * capacity + slot_index
    placement = (jnp.arange(slot_count, dtype=jnp.int32)[:, None] == target_slot[None, :]).astype(
        jnp.bfloat16
    )
    labels = jnp.stack([member_of, angles, weights], axis=1).astype(jnp.bfloat16)
    label_lanes = 128
    labels = jnp.pad(labels, ((0, 0), (0, label_lanes - labels.shape[1])))
    own_rows = jnp.concatenate([own_rows, labels], axis=1)
    outgoing = jnp.dot(placement, own_rows, preferred_element_type=jnp.float32).astype(jnp.bfloat16)
    outgoing = outgoing.reshape(owner_count, capacity, flat_len + label_lanes)
    pieces, outgoing = staged_gather(angle_major(references), "loop", outgoing)
    incoming = lax.all_to_all(outgoing, "loop", split_axis=0, concat_axis=0, tiled=True)
    highest, summed = score_all(particle_rows, pieces)
    incoming, highest, summed = lax.optimization_barrier((incoming, highest, summed))
    incoming = incoming.reshape(slot_count, flat_len + label_lanes)
    labels_in = incoming[:, flat_len : flat_len + 3]
    labels_in = labels_in.astype(jnp.float32)
    member_in = labels_in[:, 0]
    rotation = labels_in[:, 1]
    weight_of = labels_in[:, 2]
    block = -(-per_owner // 8) * 8
    angle_grid = jnp.arange(ANGLES, dtype=jnp.float32)
    member_grid = jnp.arange(block, dtype=jnp.float32)
    chosen = (angle_grid[:, None, None] == rotation[None, None, :]) & (
        member_grid[None, :, None] == member_in[None, None, :]
    )
    by_angle = jnp.where(chosen, weight_of[None, None, :], 0.0).astype(jnp.bfloat16)
    by_angle = by_angle.reshape(ANGLES * block, slot_count)
    partial_sums = pl.pallas_call(
        average_kernel,
        out_shape=jax.ShapeDtypeStruct((block, flat_len), jnp.float32),
        scratch_shapes=[pltpu.VMEM((ANGLES * block, flat_len), jnp.float32)],
    )(by_angle, incoming)
    partial_sums = partial_sums[:per_owner].reshape(per_owner, ANGLES, RADII).transpose(0, 2, 1)
    partial_sums = partial_sums.reshape(per_owner, flat_len)
    weighted = (member_grid[:per_owner, None] == member_in[None, :]).astype(jnp.float32) * weight_of[None, :]
    partial_weight = jnp.sum(weighted, axis=1)
    own_classes = references.shape[0]
    stats = jnp.stack([highest, summed], axis=0)
    if grp_size == 2:
        partner = 1 - grp_index
        weight_row = jnp.zeros((1, flat_len), jnp.float32)
        weight_row = lax.dynamic_update_slice_in_dim(
            weight_row, lax.dynamic_slice_in_dim(partial_weight, partner * own_classes, own_classes, 0)[None], 0, 1
        )
        stat_rows = jnp.pad(
            lax.dynamic_slice_in_dim(stats, partner * half_rows, half_rows, 1), ((0, 0), (0, flat_len - half_rows))
        )
        sent = jnp.concatenate(
            [lax.dynamic_slice_in_dim(partial_sums, partner * own_classes, own_classes, 0), weight_row, stat_rows], axis=0
        )
        got = lax.ppermute(sent, "grp", [(0, 1), (1, 0)])
        class_sums = lax.dynamic_slice_in_dim(partial_sums, grp_index * own_classes, own_classes, 0) + got[:own_classes]
        class_weight = (
            lax.dynamic_slice_in_dim(partial_weight, grp_index * own_classes, own_classes, 0)
            + got[own_classes, :own_classes]
        )
        stats = jnp.stack(
            [lax.dynamic_slice_in_dim(stats, grp_index * half_rows, half_rows, 1), got[own_classes + 1 :, :half_rows]],
            axis=0,
        )
    else:
        slots = jnp.arange(grp_size, dtype=jnp.int32)[:, None, None] == grp_index
        stats = jnp.where(slots, stats[None], 0.0)
        partial_sums, partial_weight, stats = lax.psum((partial_sums, partial_weight, stats), "grp")
        class_sums = lax.dynamic_slice_in_dim(partial_sums, grp_index * own_classes, own_classes, 0)
        class_weight = lax.dynamic_slice_in_dim(partial_weight, grp_index * own_classes, own_classes, 0)
        stats = lax.dynamic_slice_in_dim(stats, grp_index * half_rows, half_rows, 2)
    class_average = class_sums / class_weight[:, None]
    highest = jnp.max(stats[:, 0], axis=0)
    summed = jnp.sum(stats[:, 1] * jnp.exp(stats[:, 0] - highest[None, :]), axis=0)
    log_evidence = highest + jnp.log(summed)
    return (log_evidence, class_average)


def solution(mesh):
    return jax.shard_map(
        local,
        mesh=mesh,
        in_specs=(
            P("loop", None),
            P(("loop", "grp"), None),
            P(("loop", "grp")),
            P(("loop", "grp")),
            P(("loop", "grp")),
        ),
        out_specs=(P(("loop", "grp")), P(("loop", "grp"), None)),
        check_vma=False,
    )
```

```python
import functools
import math

import jax
import jax.numpy as jnp
from jax import lax
from jax.experimental import pallas as pl
from jax.experimental.pallas import tpu as pltpu
from jax.sharding import PartitionSpec as P

RADII = 48
ANGLES = 72


score_factor = 2.0


def angle_major(rows):
    count = rows.shape[0]
    return rows.reshape(count, RADII, ANGLES).transpose(0, 2, 1).reshape(count, RADII * ANGLES)


def score_kernel(*refs, scale):
    p_ref, piece_refs = refs[0], refs[1:-5]
    max_ref, sum_ref, r_scr, t_scr, s_scr = refs[-5:]
    flat_len = p_ref.shape[1]
    t_scr[...] = jnp.concatenate([piece[...] for piece in piece_refs], axis=0).astype(jnp.float32).T
    for angle in range(ANGLES):
        picked = t_scr[pl.ds(angle, RADII, stride=ANGLES), :].astype(r_scr.dtype)
        r_scr[pl.ds(angle * RADII, RADII), :] = picked
        r_scr[pl.ds(flat_len + angle * RADII, RADII), :] = picked
    images = p_ref[...]
    half = ANGLES // 2

    def shift_scores(s, carry):
        turned = jnp.concatenate(
            [
                r_scr[pl.ds(pl.multiple_of(s * RADII, 16), flat_len), :],
                r_scr[pl.ds(pl.multiple_of((s + half) * RADII, 16), flat_len), :],
            ],
            axis=1,
        )
        scores = jnp.dot(images, turned, preferred_element_type=jnp.float32) * scale
        s_scr[s] = scores
        return jnp.maximum(carry, scores)

    first = jnp.full(s_scr.shape[1:], -jnp.inf, jnp.float32)
    lane_max = lax.fori_loop(0, half, shift_scores, first, unroll=9)
    highest = jnp.max(lane_max.T, axis=0, keepdims=True)
    highest_col = jnp.max(lane_max, axis=1, keepdims=True)

    def shift_sum(s, carry):
        return carry + jnp.exp(s_scr[s] - highest_col)

    lane_sum = lax.fori_loop(0, half, shift_sum, jnp.zeros(s_scr.shape[1:], jnp.float32), unroll=4)
    max_ref[...] = highest
    sum_ref[...] = jnp.sum(lane_sum.T, axis=0, keepdims=True)


def score_all(lhs, pieces):
    row_count, flat_len = lhs.shape
    ref_count = sum(piece.shape[0] for piece in pieces)
    scale = score_factor / math.sqrt(flat_len)
    highest, summed = pl.pallas_call(
        functools.partial(score_kernel, scale=scale),
        out_shape=(
            jax.ShapeDtypeStruct((1, row_count), jnp.float32),
            jax.ShapeDtypeStruct((1, row_count), jnp.float32),
        ),
        scratch_shapes=[
            pltpu.VMEM((2 * flat_len, ref_count), jnp.bfloat16),
            pltpu.VMEM((flat_len, ref_count), jnp.float32),
            pltpu.VMEM((ANGLES // 2, row_count, 2 * ref_count), jnp.float32),
        ],
    )(lhs, *pieces)
    return highest[0], summed[0]


def average_kernel(w_ref, x_ref, o_ref, s_scr):
    block = o_ref.shape[0]
    flat_len = o_ref.shape[1]
    s_scr[...] = jnp.dot(w_ref[...], x_ref[:, :flat_len], preferred_element_type=jnp.float32)
    step = 8
    total = None
    for part in range(step):
        partial = None
        for whole in range(ANGLES // step):
            angle = whole * step + part
            rows = s_scr[pl.ds(angle * block, block), :]
            if whole:
                rows = pltpu.roll(rows, whole * step * RADII, 1)
            partial = rows if partial is None else partial + rows
        if part:
            partial = pltpu.roll(partial, part * RADII, 1)
        total = partial if total is None else total + partial
    o_ref[...] = total


def ring_factors(count):
    factors = []
    while count > 1:
        factor = 4 if count % 4 == 0 else count
        factors.append(factor)
        count //= factor
    return factors


def staged_gather(rows, axis, held):
    count = lax.axis_size(axis)
    stride = 1
    factors = ring_factors(count)
    for round_index, factor in enumerate(factors):
        parts = [rows]
        for step in range(1, factor):
            pairs = []
            for source in range(count):
                digit = (source // stride) % factor
                pairs.append((source, source + ((digit + step) % factor - digit) * stride))
            parts.append(lax.ppermute(rows, axis, pairs))
        rows = jnp.concatenate(parts, axis=0)
        if round_index == len(factors) - 1:
            parts, held = lax.optimization_barrier((parts, held))
        stride *= factor
    return parts, held


def local(particles, references, classes, angles, weights):
    row_count, flat_len = particles.shape
    grp_size = lax.axis_size("grp")
    half_rows = row_count // grp_size
    grp_index = lax.axis_index("grp")
    particle_rows = angle_major(particles)
    own_rows = lax.dynamic_slice_in_dim(particle_rows, grp_index * half_rows, half_rows, 0)
    owner_count = lax.axis_size("loop")
    per_owner = references.shape[0] * grp_size
    capacity = max(2, row_count // owner_count)
    slot_count = owner_count * capacity
    owner_of = classes // per_owner
    member_of = classes % per_owner
    owner_hits = (owner_of[:, None] == jnp.arange(owner_count, dtype=jnp.int32)[None, :]).astype(
        jnp.int32
    )
    earlier = jnp.cumsum(owner_hits, axis=0) - owner_hits
    slot_index = jnp.sum(earlier * owner_hits, axis=1)
    target_slot = owner_of * capacity + slot_index
    placement = (jnp.arange(slot_count, dtype=jnp.int32)[:, None] == target_slot[None, :]).astype(
        jnp.bfloat16
    )
    labels = jnp.stack([member_of, angles, weights], axis=1).astype(jnp.bfloat16)
    label_lanes = 128
    labels = jnp.pad(labels, ((0, 0), (0, label_lanes - labels.shape[1])))
    own_rows = jnp.concatenate([own_rows, labels], axis=1)
    outgoing = jnp.dot(placement, own_rows, preferred_element_type=jnp.float32).astype(jnp.bfloat16)
    outgoing = outgoing.reshape(owner_count, capacity, flat_len + label_lanes)
    pieces, outgoing = staged_gather(references, "loop", outgoing)
    incoming = lax.all_to_all(outgoing, "loop", split_axis=0, concat_axis=0, tiled=True)
    highest, summed = score_all(particle_rows, pieces)
    incoming, highest, summed = lax.optimization_barrier((incoming, highest, summed))
    incoming = incoming.reshape(slot_count, flat_len + label_lanes)
    labels_in = incoming[:, flat_len : flat_len + 3]
    labels_in = labels_in.astype(jnp.float32)
    member_in = labels_in[:, 0]
    rotation = labels_in[:, 1]
    weight_of = labels_in[:, 2]
    block = -(-per_owner // 8) * 8
    angle_grid = jnp.arange(ANGLES, dtype=jnp.float32)
    member_grid = jnp.arange(block, dtype=jnp.float32)
    chosen = (angle_grid[:, None, None] == rotation[None, None, :]) & (
        member_grid[None, :, None] == member_in[None, None, :]
    )
    by_angle = jnp.where(chosen, weight_of[None, None, :], 0.0).astype(jnp.bfloat16)
    by_angle = by_angle.reshape(ANGLES * block, slot_count)
    partial_sums = pl.pallas_call(
        average_kernel,
        out_shape=jax.ShapeDtypeStruct((block, flat_len), jnp.float32),
        scratch_shapes=[pltpu.VMEM((ANGLES * block, flat_len), jnp.float32)],
    )(by_angle, incoming)
    partial_sums = partial_sums[:per_owner].reshape(per_owner, ANGLES, RADII).transpose(0, 2, 1)
    partial_sums = partial_sums.reshape(per_owner, flat_len)
    weighted = (member_grid[:per_owner, None] == member_in[None, :]).astype(jnp.float32) * weight_of[None, :]
    partial_weight = jnp.sum(weighted, axis=1)
    own_classes = references.shape[0]
    stats = jnp.stack([highest, summed], axis=0)
    if grp_size == 2:
        partner = 1 - grp_index
        weight_row = jnp.zeros((1, flat_len), jnp.float32)
        weight_row = lax.dynamic_update_slice_in_dim(
            weight_row, lax.dynamic_slice_in_dim(partial_weight, partner * own_classes, own_classes, 0)[None], 0, 1
        )
        stat_rows = jnp.pad(
            lax.dynamic_slice_in_dim(stats, partner * half_rows, half_rows, 1), ((0, 0), (0, flat_len - half_rows))
        )
        sent = jnp.concatenate(
            [lax.dynamic_slice_in_dim(partial_sums, partner * own_classes, own_classes, 0), weight_row, stat_rows], axis=0
        )
        got = lax.ppermute(sent, "grp", [(0, 1), (1, 0)])
        class_sums = lax.dynamic_slice_in_dim(partial_sums, grp_index * own_classes, own_classes, 0) + got[:own_classes]
        class_weight = (
            lax.dynamic_slice_in_dim(partial_weight, grp_index * own_classes, own_classes, 0)
            + got[own_classes, :own_classes]
        )
        stats = jnp.stack(
            [lax.dynamic_slice_in_dim(stats, grp_index * half_rows, half_rows, 1), got[own_classes + 1 :, :half_rows]],
            axis=0,
        )
    else:
        slots = jnp.arange(grp_size, dtype=jnp.int32)[:, None, None] == grp_index
        stats = jnp.where(slots, stats[None], 0.0)
        partial_sums, partial_weight, stats = lax.psum((partial_sums, partial_weight, stats), "grp")
        class_sums = lax.dynamic_slice_in_dim(partial_sums, grp_index * own_classes, own_classes, 0)
        class_weight = lax.dynamic_slice_in_dim(partial_weight, grp_index * own_classes, own_classes, 0)
        stats = lax.dynamic_slice_in_dim(stats, grp_index * half_rows, half_rows, 2)
    class_average = class_sums / class_weight[:, None]
    highest = jnp.max(stats[:, 0], axis=0)
    summed = jnp.sum(stats[:, 1] * jnp.exp(stats[:, 0] - highest[None, :]), axis=0)
    log_evidence = highest + jnp.log(summed)
    return (log_evidence, class_average)


def solution(mesh):
    return jax.shard_map(
        local,
        mesh=mesh,
        in_specs=(
            P("loop", None),
            P(("loop", "grp"), None),
            P(("loop", "grp")),
            P(("loop", "grp")),
            P(("loop", "grp")),
        ),
        out_specs=(P(("loop", "grp")), P(("loop", "grp"), None)),
        check_vma=False,
    )
```

```python
import functools
import math

import jax
import jax.numpy as jnp
from jax import lax
from jax.experimental import pallas as pl
from jax.experimental.pallas import tpu as pltpu
from jax.sharding import PartitionSpec as P

RADII = 48
ANGLES = 72


score_factor = 2.0


def angle_major(rows):
    count = rows.shape[0]
    return rows.reshape(count, RADII, ANGLES).transpose(0, 2, 1).reshape(count, RADII * ANGLES)


def score_kernel(*refs, scale):
    p_ref, piece_refs = refs[0], refs[1:-5]
    max_ref, sum_ref, r_scr, t_scr, s_scr = refs[-5:]
    flat_len = p_ref.shape[1]
    t_scr[...] = jnp.concatenate([piece[...] for piece in piece_refs], axis=0).astype(jnp.float32).T
    for angle in range(ANGLES):
        picked = t_scr[pl.ds(angle, RADII, stride=ANGLES), :].astype(r_scr.dtype)
        r_scr[pl.ds(angle * RADII, RADII), :] = picked
        r_scr[pl.ds(flat_len + angle * RADII, RADII), :] = picked
    images = p_ref[...]
    half = ANGLES // 2

    def shift_scores(s, carry):
        turned = jnp.concatenate(
            [
                r_scr[pl.ds(pl.multiple_of(s * RADII, 16), flat_len), :],
                r_scr[pl.ds(pl.multiple_of((s + half) * RADII, 16), flat_len), :],
            ],
            axis=1,
        )
        scores = jnp.dot(images, turned, preferred_element_type=jnp.float32) * scale
        s_scr[s] = scores
        return jnp.maximum(carry, scores)

    first = jnp.full(s_scr.shape[1:], -jnp.inf, jnp.float32)
    lane_max = lax.fori_loop(0, half, shift_scores, first, unroll=9)
    highest = jnp.max(lane_max.T, axis=0, keepdims=True)
    highest_col = jnp.max(lane_max, axis=1, keepdims=True)

    def shift_sum(s, carry):
        return carry + jnp.exp(s_scr[s] - highest_col)

    lane_sum = lax.fori_loop(0, half, shift_sum, jnp.zeros(s_scr.shape[1:], jnp.float32), unroll=4)
    max_ref[...] = highest
    sum_ref[...] = jnp.sum(lane_sum.T, axis=0, keepdims=True)


def score_all(lhs, pieces):
    row_count, flat_len = lhs.shape
    ref_count = sum(piece.shape[0] for piece in pieces)
    scale = score_factor / math.sqrt(flat_len)
    highest, summed = pl.pallas_call(
        functools.partial(score_kernel, scale=scale),
        out_shape=(
            jax.ShapeDtypeStruct((1, row_count), jnp.float32),
            jax.ShapeDtypeStruct((1, row_count), jnp.float32),
        ),
        scratch_shapes=[
            pltpu.VMEM((2 * flat_len, ref_count), jnp.bfloat16),
            pltpu.VMEM((flat_len, ref_count), jnp.float32),
            pltpu.VMEM((ANGLES // 2, row_count, 2 * ref_count), jnp.float32),
        ],
    )(lhs, *pieces)
    return highest[0], summed[0]


def average_kernel(x_ref, o_ref, w_out_ref, w_scr, s_scr):
    block = o_ref.shape[0]
    flat_len = o_ref.shape[1]
    labels = x_ref[:, flat_len:].astype(jnp.float32).T
    member, rotation, weight = labels[0:1, :], labels[1:2, :], labels[2:3, :]
    row = lax.broadcasted_iota(jnp.int32, w_scr.shape, 0)
    chosen = ((row // block).astype(jnp.float32) == rotation) & ((row % block).astype(jnp.float32) == member)
    w_scr[...] = jnp.where(chosen, weight, 0.0).astype(w_scr.dtype)
    class_row = lax.broadcasted_iota(jnp.int32, (block, x_ref.shape[0]), 0).astype(jnp.float32)
    w_out_ref[...] = jnp.sum(jnp.where(class_row == member, weight, 0.0), axis=1, keepdims=True)
    s_scr[...] = jnp.dot(w_scr[...], x_ref[:, :flat_len], preferred_element_type=jnp.float32)
    step = 8
    total = None
    for part in range(step):
        partial = None
        for whole in range(ANGLES // step):
            angle = whole * step + part
            rows = s_scr[pl.ds(angle * block, block), :]
            if whole:
                rows = pltpu.roll(rows, whole * step * RADII, 1)
            partial = rows if partial is None else partial + rows
        if part:
            partial = pltpu.roll(partial, part * RADII, 1)
        total = partial if total is None else total + partial
    o_ref[...] = total


def ring_factors(count):
    factors = []
    while count > 1:
        factor = 4 if count % 4 == 0 else count
        factors.append(factor)
        count //= factor
    return factors


def staged_gather(rows, axis, held):
    count = lax.axis_size(axis)
    stride = 1
    factors = ring_factors(count)
    for round_index, factor in enumerate(factors):
        parts = [rows]
        for step in range(1, factor):
            pairs = []
            for source in range(count):
                digit = (source // stride) % factor
                pairs.append((source, source + ((digit + step) % factor - digit) * stride))
            parts.append(lax.ppermute(rows, axis, pairs))
        rows = jnp.concatenate(parts, axis=0)
        if round_index == len(factors) - 1:
            parts, held = lax.optimization_barrier((parts, held))
        stride *= factor
    return parts, held


def local(particles, references, classes, angles, weights):
    row_count, flat_len = particles.shape
    grp_size = lax.axis_size("grp")
    half_rows = row_count // grp_size
    grp_index = lax.axis_index("grp")
    particle_rows = angle_major(particles)
    own_rows = lax.dynamic_slice_in_dim(particle_rows, grp_index * half_rows, half_rows, 0)
    owner_count = lax.axis_size("loop")
    per_owner = references.shape[0] * grp_size
    capacity = max(2, row_count // owner_count)
    slot_count = owner_count * capacity
    owner_of = classes // per_owner
    member_of = classes % per_owner
    owner_hits = (owner_of[:, None] == jnp.arange(owner_count, dtype=jnp.int32)[None, :]).astype(
        jnp.int32
    )
    earlier = jnp.cumsum(owner_hits, axis=0) - owner_hits
    slot_index = jnp.sum(earlier * owner_hits, axis=1)
    target_slot = owner_of * capacity + slot_index
    placement = (jnp.arange(slot_count, dtype=jnp.int32)[:, None] == target_slot[None, :]).astype(
        jnp.bfloat16
    )
    labels = jnp.stack([member_of, angles, weights], axis=1).astype(jnp.bfloat16)
    label_lanes = 128
    labels = jnp.pad(labels, ((0, 0), (0, label_lanes - labels.shape[1])))
    own_rows = jnp.concatenate([own_rows, labels], axis=1)
    outgoing = jnp.dot(placement, own_rows, preferred_element_type=jnp.float32).astype(jnp.bfloat16)
    outgoing = outgoing.reshape(owner_count, capacity, flat_len + label_lanes)
    pieces, outgoing = staged_gather(references, "loop", outgoing)
    incoming = lax.all_to_all(outgoing, "loop", split_axis=0, concat_axis=0, tiled=True)
    highest, summed = score_all(particle_rows, pieces)
    incoming, highest, summed = lax.optimization_barrier((incoming, highest, summed))
    incoming = incoming.reshape(slot_count, flat_len + label_lanes)
    block = -(-per_owner // 8) * 8
    partial_sums, partial_weight = pl.pallas_call(
        average_kernel,
        out_shape=(
            jax.ShapeDtypeStruct((block, flat_len), jnp.float32),
            jax.ShapeDtypeStruct((block, 1), jnp.float32),
        ),
        scratch_shapes=[
            pltpu.VMEM((ANGLES * block, slot_count), jnp.bfloat16),
            pltpu.VMEM((ANGLES * block, flat_len), jnp.float32),
        ],
    )(incoming)
    partial_sums = partial_sums[:per_owner].reshape(per_owner, ANGLES, RADII).transpose(0, 2, 1)
    partial_sums = partial_sums.reshape(per_owner, flat_len)
    partial_weight = partial_weight[:per_owner, 0]
    own_classes = references.shape[0]
    stats = jnp.stack([highest, summed], axis=0)
    if grp_size == 2:
        partner = 1 - grp_index
        weight_row = jnp.zeros((1, flat_len), jnp.float32)
        weight_row = lax.dynamic_update_slice_in_dim(
            weight_row, lax.dynamic_slice_in_dim(partial_weight, partner * own_classes, own_classes, 0)[None], 0, 1
        )
        stat_rows = jnp.pad(
            lax.dynamic_slice_in_dim(stats, partner * half_rows, half_rows, 1), ((0, 0), (0, flat_len - half_rows))
        )
        sent = jnp.concatenate(
            [lax.dynamic_slice_in_dim(partial_sums, partner * own_classes, own_classes, 0), weight_row, stat_rows], axis=0
        )
        got = lax.ppermute(sent, "grp", [(0, 1), (1, 0)])
        class_sums = lax.dynamic_slice_in_dim(partial_sums, grp_index * own_classes, own_classes, 0) + got[:own_classes]
        class_weight = (
            lax.dynamic_slice_in_dim(partial_weight, grp_index * own_classes, own_classes, 0)
            + got[own_classes, :own_classes]
        )
        stats = jnp.stack(
            [lax.dynamic_slice_in_dim(stats, grp_index * half_rows, half_rows, 1), got[own_classes + 1 :, :half_rows]],
            axis=0,
        )
    else:
        slots = jnp.arange(grp_size, dtype=jnp.int32)[:, None, None] == grp_index
        stats = jnp.where(slots, stats[None], 0.0)
        partial_sums, partial_weight, stats = lax.psum((partial_sums, partial_weight, stats), "grp")
        class_sums = lax.dynamic_slice_in_dim(partial_sums, grp_index * own_classes, own_classes, 0)
        class_weight = lax.dynamic_slice_in_dim(partial_weight, grp_index * own_classes, own_classes, 0)
        stats = lax.dynamic_slice_in_dim(stats, grp_index * half_rows, half_rows, 2)
    class_average = class_sums / class_weight[:, None]
    highest = jnp.max(stats[:, 0], axis=0)
    summed = jnp.sum(stats[:, 1] * jnp.exp(stats[:, 0] - highest[None, :]), axis=0)
    log_evidence = highest + jnp.log(summed)
    return (log_evidence, class_average)


def solution(mesh):
    return jax.shard_map(
        local,
        mesh=mesh,
        in_specs=(
            P("loop", None),
            P(("loop", "grp"), None),
            P(("loop", "grp")),
            P(("loop", "grp")),
            P(("loop", "grp")),
        ),
        out_specs=(P(("loop", "grp")), P(("loop", "grp"), None)),
        check_vma=False,
    )
```

```python
import functools
import math

import jax
import jax.numpy as jnp
from jax import lax
from jax.experimental import pallas as pl
from jax.experimental.pallas import tpu as pltpu
from jax.sharding import PartitionSpec as P

RADII = 48
ANGLES = 72


score_factor = 2.0


def angle_major(rows):
    count = rows.shape[0]
    return rows.reshape(count, RADII, ANGLES).transpose(0, 2, 1).reshape(count, RADII * ANGLES)


def score_kernel(*refs, scale):
    p_ref, piece_refs = refs[0], refs[1:-7]
    max_ref, sum_ref, r_scr, t_scr, s_scr, pt_scr, pa_scr = refs[-7:]
    flat_len = p_ref.shape[1]
    t_scr[...] = jnp.concatenate([piece[...] for piece in piece_refs], axis=0).astype(jnp.float32).T
    for angle in range(ANGLES):
        picked = t_scr[pl.ds(angle, RADII, stride=ANGLES), :].astype(r_scr.dtype)
        r_scr[pl.ds(angle * RADII, RADII), :] = picked
        r_scr[pl.ds(flat_len + angle * RADII, RADII), :] = picked
    pt_scr[...] = p_ref[...].astype(jnp.float32).T
    for angle in range(ANGLES):
        pa_scr[pl.ds(angle * RADII, RADII), :] = pt_scr[pl.ds(angle, RADII, stride=ANGLES), :]
    images = pa_scr[...].T.astype(p_ref.dtype)
    half = ANGLES // 2

    def shift_scores(s, carry):
        turned = jnp.concatenate(
            [
                r_scr[pl.ds(pl.multiple_of(s * RADII, 16), flat_len), :],
                r_scr[pl.ds(pl.multiple_of((s + half) * RADII, 16), flat_len), :],
            ],
            axis=1,
        )
        scores = jnp.dot(images, turned, preferred_element_type=jnp.float32) * scale
        s_scr[s] = scores
        return jnp.maximum(carry, scores)

    first = jnp.full(s_scr.shape[1:], -jnp.inf, jnp.float32)
    lane_max = lax.fori_loop(0, half, shift_scores, first, unroll=9)
    highest = jnp.max(lane_max.T, axis=0, keepdims=True)
    highest_col = jnp.max(lane_max, axis=1, keepdims=True)

    def shift_sum(s, carry):
        return carry + jnp.exp(s_scr[s] - highest_col)

    lane_sum = lax.fori_loop(0, half, shift_sum, jnp.zeros(s_scr.shape[1:], jnp.float32), unroll=4)
    max_ref[...] = highest
    sum_ref[...] = jnp.sum(lane_sum.T, axis=0, keepdims=True)


def score_all(lhs, pieces):
    row_count, flat_len = lhs.shape
    ref_count = sum(piece.shape[0] for piece in pieces)
    scale = score_factor / math.sqrt(flat_len)
    highest, summed = pl.pallas_call(
        functools.partial(score_kernel, scale=scale),
        out_shape=(
            jax.ShapeDtypeStruct((1, row_count), jnp.float32),
            jax.ShapeDtypeStruct((1, row_count), jnp.float32),
        ),
        scratch_shapes=[
            pltpu.VMEM((2 * flat_len, ref_count), jnp.bfloat16),
            pltpu.VMEM((flat_len, ref_count), jnp.float32),
            pltpu.VMEM((ANGLES // 2, row_count, 2 * ref_count), jnp.float32),
            pltpu.VMEM((flat_len, row_count), jnp.float32),
            pltpu.VMEM((flat_len, row_count), jnp.float32),
        ],
    )(lhs, *pieces)
    return highest[0], summed[0]


def average_kernel(w_ref, x_ref, o_ref, s_scr):
    block = o_ref.shape[0]
    flat_len = o_ref.shape[1]
    s_scr[...] = jnp.dot(w_ref[...], x_ref[:, :flat_len], preferred_element_type=jnp.float32)
    step = 8
    total = None
    for part in range(step):
        partial = None
        for whole in range(ANGLES // step):
            angle = whole * step + part
            rows = s_scr[pl.ds(angle * block, block), :]
            if whole:
                rows = pltpu.roll(rows, whole * step * RADII, 1)
            partial = rows if partial is None else partial + rows
        if part:
            partial = pltpu.roll(partial, part * RADII, 1)
        total = partial if total is None else total + partial
    o_ref[...] = total


def ring_factors(count):
    factors = []
    while count > 1:
        factor = 4 if count % 4 == 0 else count
        factors.append(factor)
        count //= factor
    return factors


def staged_gather(rows, axis, held):
    count = lax.axis_size(axis)
    stride = 1
    factors = ring_factors(count)
    for round_index, factor in enumerate(factors):
        parts = [rows]
        for step in range(1, factor):
            pairs = []
            for source in range(count):
                digit = (source // stride) % factor
                pairs.append((source, source + ((digit + step) % factor - digit) * stride))
            parts.append(lax.ppermute(rows, axis, pairs))
        rows = jnp.concatenate(parts, axis=0)
        if round_index == len(factors) - 1:
            parts, held = lax.optimization_barrier((parts, held))
        stride *= factor
    return parts, held


def local(particles, references, classes, angles, weights):
    row_count, flat_len = particles.shape
    grp_size = lax.axis_size("grp")
    half_rows = row_count // grp_size
    grp_index = lax.axis_index("grp")
    own_rows = angle_major(lax.dynamic_slice_in_dim(particles, grp_index * half_rows, half_rows, 0))
    owner_count = lax.axis_size("loop")
    per_owner = references.shape[0] * grp_size
    capacity = max(2, row_count // owner_count)
    slot_count = owner_count * capacity
    owner_of = classes // per_owner
    member_of = classes % per_owner
    owner_hits = (owner_of[:, None] == jnp.arange(owner_count, dtype=jnp.int32)[None, :]).astype(
        jnp.int32
    )
    earlier = jnp.cumsum(owner_hits, axis=0) - owner_hits
    slot_index = jnp.sum(earlier * owner_hits, axis=1)
    target_slot = owner_of * capacity + slot_index
    placement = (jnp.arange(slot_count, dtype=jnp.int32)[:, None] == target_slot[None, :]).astype(
        jnp.bfloat16
    )
    labels = jnp.stack([member_of, angles, weights], axis=1).astype(jnp.bfloat16)
    label_lanes = 128
    labels = jnp.pad(labels, ((0, 0), (0, label_lanes - labels.shape[1])))
    own_rows = jnp.concatenate([own_rows, labels], axis=1)
    outgoing = jnp.dot(placement, own_rows, preferred_element_type=jnp.float32).astype(jnp.bfloat16)
    outgoing = outgoing.reshape(owner_count, capacity, flat_len + label_lanes)
    pieces, outgoing = staged_gather(references, "loop", outgoing)
    incoming = lax.all_to_all(outgoing, "loop", split_axis=0, concat_axis=0, tiled=True)
    highest, summed = score_all(particles, pieces)
    incoming, highest, summed = lax.optimization_barrier((incoming, highest, summed))
    incoming = incoming.reshape(slot_count, flat_len + label_lanes)
    labels_in = incoming[:, flat_len : flat_len + 3]
    labels_in = labels_in.astype(jnp.float32)
    member_in = labels_in[:, 0]
    rotation = labels_in[:, 1]
    weight_of = labels_in[:, 2]
    block = -(-per_owner // 8) * 8
    angle_grid = jnp.arange(ANGLES, dtype=jnp.float32)
    member_grid = jnp.arange(block, dtype=jnp.float32)
    chosen = (angle_grid[:, None, None] == rotation[None, None, :]) & (
        member_grid[None, :, None] == member_in[None, None, :]
    )
    by_angle = jnp.where(chosen, weight_of[None, None, :], 0.0).astype(jnp.bfloat16)
    by_angle = by_angle.reshape(ANGLES * block, slot_count)
    partial_sums = pl.pallas_call(
        average_kernel,
        out_shape=jax.ShapeDtypeStruct((block, flat_len), jnp.float32),
        scratch_shapes=[pltpu.VMEM((ANGLES * block, flat_len), jnp.float32)],
    )(by_angle, incoming)
    partial_sums = partial_sums[:per_owner].reshape(per_owner, ANGLES, RADII).transpose(0, 2, 1)
    partial_sums = partial_sums.reshape(per_owner, flat_len)
    weighted = (member_grid[:per_owner, None] == member_in[None, :]).astype(jnp.float32) * weight_of[None, :]
    partial_weight = jnp.sum(weighted, axis=1)
    own_classes = references.shape[0]
    stats = jnp.stack([highest, summed], axis=0)
    if grp_size == 2:
        partner = 1 - grp_index
        weight_row = jnp.zeros((1, flat_len), jnp.float32)
        weight_row = lax.dynamic_update_slice_in_dim(
            weight_row, lax.dynamic_slice_in_dim(partial_weight, partner * own_classes, own_classes, 0)[None], 0, 1
        )
        stat_rows = jnp.pad(
            lax.dynamic_slice_in_dim(stats, partner * half_rows, half_rows, 1), ((0, 0), (0, flat_len - half_rows))
        )
        sent = jnp.concatenate(
            [lax.dynamic_slice_in_dim(partial_sums, partner * own_classes, own_classes, 0), weight_row, stat_rows], axis=0
        )
        got = lax.ppermute(sent, "grp", [(0, 1), (1, 0)])
        class_sums = lax.dynamic_slice_in_dim(partial_sums, grp_index * own_classes, own_classes, 0) + got[:own_classes]
        class_weight = (
            lax.dynamic_slice_in_dim(partial_weight, grp_index * own_classes, own_classes, 0)
            + got[own_classes, :own_classes]
        )
        stats = jnp.stack(
            [lax.dynamic_slice_in_dim(stats, grp_index * half_rows, half_rows, 1), got[own_classes + 1 :, :half_rows]],
            axis=0,
        )
    else:
        slots = jnp.arange(grp_size, dtype=jnp.int32)[:, None, None] == grp_index
        stats = jnp.where(slots, stats[None], 0.0)
        partial_sums, partial_weight, stats = lax.psum((partial_sums, partial_weight, stats), "grp")
        class_sums = lax.dynamic_slice_in_dim(partial_sums, grp_index * own_classes, own_classes, 0)
        class_weight = lax.dynamic_slice_in_dim(partial_weight, grp_index * own_classes, own_classes, 0)
        stats = lax.dynamic_slice_in_dim(stats, grp_index * half_rows, half_rows, 2)
    class_average = class_sums / class_weight[:, None]
    highest = jnp.max(stats[:, 0], axis=0)
    summed = jnp.sum(stats[:, 1] * jnp.exp(stats[:, 0] - highest[None, :]), axis=0)
    log_evidence = highest + jnp.log(summed)
    return (log_evidence, class_average)


def solution(mesh):
    return jax.shard_map(
        local,
        mesh=mesh,
        in_specs=(
            P("loop", None),
            P(("loop", "grp"), None),
            P(("loop", "grp")),
            P(("loop", "grp")),
            P(("loop", "grp")),
        ),
        out_specs=(P(("loop", "grp")), P(("loop", "grp"), None)),
        check_vma=False,
    )
```

```python
import functools
import math

import jax
import jax.numpy as jnp
from jax import lax
from jax.experimental import pallas as pl
from jax.experimental.pallas import tpu as pltpu
from jax.sharding import PartitionSpec as P

RADII = 48
ANGLES = 72


score_factor = 2.0


def angle_major(rows):
    count = rows.shape[0]
    return rows.reshape(count, RADII, ANGLES).transpose(0, 2, 1).reshape(count, RADII * ANGLES)


def score_kernel(*refs, scale):
    p_ref, piece_refs = refs[0], refs[1:-5]
    max_ref, sum_ref, r_scr, t_scr, s_scr = refs[-5:]
    flat_len = p_ref.shape[1]
    t_scr[...] = jnp.concatenate([piece[...] for piece in piece_refs], axis=0).astype(jnp.float32).T
    for angle in range(ANGLES):
        picked = t_scr[pl.ds(angle, RADII, stride=ANGLES), :].astype(r_scr.dtype)
        r_scr[pl.ds(angle * RADII, RADII), :] = picked
        r_scr[pl.ds(flat_len + angle * RADII, RADII), :] = picked
    images = p_ref[...]
    half = ANGLES // 2

    def shift_scores(s, carry):
        turned = jnp.concatenate(
            [
                r_scr[pl.ds(pl.multiple_of(s * RADII, 16), flat_len), :],
                r_scr[pl.ds(pl.multiple_of((s + half) * RADII, 16), flat_len), :],
            ],
            axis=1,
        )
        scores = jnp.dot(images, turned, preferred_element_type=jnp.float32) * scale
        s_scr[s] = scores
        return jnp.maximum(carry, scores)

    first = jnp.full(s_scr.shape[1:], -jnp.inf, jnp.float32)
    lane_max = lax.fori_loop(0, half, shift_scores, first, unroll=12)
    highest = jnp.max(lane_max.T, axis=0, keepdims=True)
    highest_col = jnp.max(lane_max, axis=1, keepdims=True)

    def shift_sum(s, carry):
        return carry + jnp.exp(s_scr[s] - highest_col)

    lane_sum = lax.fori_loop(0, half, shift_sum, jnp.zeros(s_scr.shape[1:], jnp.float32), unroll=4)
    max_ref[...] = highest
    sum_ref[...] = jnp.sum(lane_sum.T, axis=0, keepdims=True)


def score_all(lhs, pieces):
    row_count, flat_len = lhs.shape
    ref_count = sum(piece.shape[0] for piece in pieces)
    scale = score_factor / math.sqrt(flat_len)
    highest, summed = pl.pallas_call(
        functools.partial(score_kernel, scale=scale),
        out_shape=(
            jax.ShapeDtypeStruct((1, row_count), jnp.float32),
            jax.ShapeDtypeStruct((1, row_count), jnp.float32),
        ),
        scratch_shapes=[
            pltpu.VMEM((2 * flat_len, ref_count), jnp.bfloat16),
            pltpu.VMEM((flat_len, ref_count), jnp.float32),
            pltpu.VMEM((ANGLES // 2, row_count, 2 * ref_count), jnp.float32),
        ],
    )(lhs, *pieces)
    return highest[0], summed[0]


def average_kernel(w_ref, x_ref, o_ref, s_scr):
    block = o_ref.shape[0]
    flat_len = o_ref.shape[1]
    s_scr[...] = jnp.dot(w_ref[...], x_ref[:, :flat_len], preferred_element_type=jnp.float32)
    step = 8
    total = None
    for part in range(step):
        partial = None
        for whole in range(ANGLES // step):
            angle = whole * step + part
            rows = s_scr[pl.ds(angle * block, block), :]
            if whole:
                rows = pltpu.roll(rows, whole * step * RADII, 1)
            partial = rows if partial is None else partial + rows
        if part:
            partial = pltpu.roll(partial, part * RADII, 1)
        total = partial if total is None else total + partial
    o_ref[...] = total


def ring_factors(count):
    factors = []
    while count > 1:
        factor = 4 if count % 4 == 0 else count
        factors.append(factor)
        count //= factor
    return factors


def staged_gather(rows, axis, held):
    count = lax.axis_size(axis)
    stride = 1
    factors = ring_factors(count)
    for round_index, factor in enumerate(factors):
        parts = [rows]
        for step in range(1, factor):
            pairs = []
            for source in range(count):
                digit = (source // stride) % factor
                pairs.append((source, source + ((digit + step) % factor - digit) * stride))
            parts.append(lax.ppermute(rows, axis, pairs))
        rows = jnp.concatenate(parts, axis=0)
        if round_index == len(factors) - 1:
            parts, held = lax.optimization_barrier((parts, held))
        stride *= factor
    return parts, held


def local(particles, references, classes, angles, weights):
    row_count, flat_len = particles.shape
    grp_size = lax.axis_size("grp")
    half_rows = row_count // grp_size
    grp_index = lax.axis_index("grp")
    particle_rows = angle_major(particles)
    own_rows = lax.dynamic_slice_in_dim(particle_rows, grp_index * half_rows, half_rows, 0)
    owner_count = lax.axis_size("loop")
    per_owner = references.shape[0] * grp_size
    capacity = max(2, row_count // owner_count)
    slot_count = owner_count * capacity
    owner_of = classes // per_owner
    member_of = classes % per_owner
    owner_hits = (owner_of[:, None] == jnp.arange(owner_count, dtype=jnp.int32)[None, :]).astype(
        jnp.int32
    )
    earlier = jnp.cumsum(owner_hits, axis=0) - owner_hits
    slot_index = jnp.sum(earlier * owner_hits, axis=1)
    target_slot = owner_of * capacity + slot_index
    placement = (jnp.arange(slot_count, dtype=jnp.int32)[:, None] == target_slot[None, :]).astype(
        jnp.bfloat16
    )
    labels = jnp.stack([member_of, angles, weights], axis=1).astype(jnp.bfloat16)
    label_lanes = 128
    labels = jnp.pad(labels, ((0, 0), (0, label_lanes - labels.shape[1])))
    own_rows = jnp.concatenate([own_rows, labels], axis=1)
    outgoing = jnp.dot(placement, own_rows, preferred_element_type=jnp.float32).astype(jnp.bfloat16)
    outgoing = outgoing.reshape(owner_count, capacity, flat_len + label_lanes)
    pieces, outgoing = staged_gather(references, "loop", outgoing)
    incoming = lax.all_to_all(outgoing, "loop", split_axis=0, concat_axis=0, tiled=True)
    highest, summed = score_all(particle_rows, pieces)
    incoming, highest, summed = lax.optimization_barrier((incoming, highest, summed))
    incoming = incoming.reshape(slot_count, flat_len + label_lanes)
    labels_in = incoming[:, flat_len : flat_len + 3]
    labels_in = labels_in.astype(jnp.float32)
    member_in = labels_in[:, 0]
    rotation = labels_in[:, 1]
    weight_of = labels_in[:, 2]
    block = -(-per_owner // 8) * 8
    angle_grid = jnp.arange(ANGLES, dtype=jnp.float32)
    member_grid = jnp.arange(block, dtype=jnp.float32)
    chosen = (angle_grid[:, None, None] == rotation[None, None, :]) & (
        member_grid[None, :, None] == member_in[None, None, :]
    )
    by_angle = jnp.where(chosen, weight_of[None, None, :], 0.0).astype(jnp.bfloat16)
    by_angle = by_angle.reshape(ANGLES * block, slot_count)
    partial_sums = pl.pallas_call(
        average_kernel,
        out_shape=jax.ShapeDtypeStruct((block, flat_len), jnp.float32),
        scratch_shapes=[pltpu.VMEM((ANGLES * block, flat_len), jnp.float32)],
    )(by_angle, incoming)
    partial_sums = partial_sums[:per_owner].reshape(per_owner, ANGLES, RADII).transpose(0, 2, 1)
    partial_sums = partial_sums.reshape(per_owner, flat_len)
    weighted = (member_grid[:per_owner, None] == member_in[None, :]).astype(jnp.float32) * weight_of[None, :]
    partial_weight = jnp.sum(weighted, axis=1)
    own_classes = references.shape[0]
    stats = jnp.stack([highest, summed], axis=0)
    if grp_size == 2:
        partner = 1 - grp_index
        weight_row = jnp.zeros((1, flat_len), jnp.float32)
        weight_row = lax.dynamic_update_slice_in_dim(
            weight_row, lax.dynamic_slice_in_dim(partial_weight, partner * own_classes, own_classes, 0)[None], 0, 1
        )
        stat_rows = jnp.pad(
            lax.dynamic_slice_in_dim(stats, partner * half_rows, half_rows, 1), ((0, 0), (0, flat_len - half_rows))
        )
        sent = jnp.concatenate(
            [lax.dynamic_slice_in_dim(partial_sums, partner * own_classes, own_classes, 0), weight_row, stat_rows], axis=0
        )
        got = lax.ppermute(sent, "grp", [(0, 1), (1, 0)])
        class_sums = lax.dynamic_slice_in_dim(partial_sums, grp_index * own_classes, own_classes, 0) + got[:own_classes]
        class_weight = (
            lax.dynamic_slice_in_dim(partial_weight, grp_index * own_classes, own_classes, 0)
            + got[own_classes, :own_classes]
        )
        stats = jnp.stack(
            [lax.dynamic_slice_in_dim(stats, grp_index * half_rows, half_rows, 1), got[own_classes + 1 :, :half_rows]],
            axis=0,
        )
    else:
        slots = jnp.arange(grp_size, dtype=jnp.int32)[:, None, None] == grp_index
        stats = jnp.where(slots, stats[None], 0.0)
        partial_sums, partial_weight, stats = lax.psum((partial_sums, partial_weight, stats), "grp")
        class_sums = lax.dynamic_slice_in_dim(partial_sums, grp_index * own_classes, own_classes, 0)
        class_weight = lax.dynamic_slice_in_dim(partial_weight, grp_index * own_classes, own_classes, 0)
        stats = lax.dynamic_slice_in_dim(stats, grp_index * half_rows, half_rows, 2)
    class_average = class_sums / class_weight[:, None]
    highest = jnp.max(stats[:, 0], axis=0)
    summed = jnp.sum(stats[:, 1] * jnp.exp(stats[:, 0] - highest[None, :]), axis=0)
    log_evidence = highest + jnp.log(summed)
    return (log_evidence, class_average)


def solution(mesh):
    return jax.shard_map(
        local,
        mesh=mesh,
        in_specs=(
            P("loop", None),
            P(("loop", "grp"), None),
            P(("loop", "grp")),
            P(("loop", "grp")),
            P(("loop", "grp")),
        ),
        out_specs=(P(("loop", "grp")), P(("loop", "grp"), None)),
        check_vma=False,
    )
```

```python
import functools
import math

import jax
import jax.numpy as jnp
from jax import lax
from jax.experimental import pallas as pl
from jax.experimental.pallas import tpu as pltpu
from jax.sharding import PartitionSpec as P

RADII = 48
ANGLES = 72


score_factor = 2.0


def angle_major(rows):
    count = rows.shape[0]
    return rows.reshape(count, RADII, ANGLES).transpose(0, 2, 1).reshape(count, RADII * ANGLES)


def score_kernel(*refs, scale):
    p_ref, piece_refs = refs[0], refs[1:-5]
    max_ref, sum_ref, r_scr, t_scr, s_scr = refs[-5:]
    flat_len = p_ref.shape[1]
    t_scr[...] = jnp.concatenate([piece[...] for piece in piece_refs], axis=0).astype(jnp.float32).T
    for angle in range(ANGLES):
        picked = t_scr[pl.ds(angle, RADII, stride=ANGLES), :].astype(r_scr.dtype)
        r_scr[pl.ds(angle * RADII, RADII), :] = picked
        r_scr[pl.ds(flat_len + angle * RADII, RADII), :] = picked
    images = p_ref[...]
    half = ANGLES // 2

    def shift_scores(s, carry):
        turned = jnp.concatenate(
            [
                r_scr[pl.ds(pl.multiple_of(s * RADII, 16), flat_len), :],
                r_scr[pl.ds(pl.multiple_of((s + half) * RADII, 16), flat_len), :],
            ],
            axis=1,
        )
        scores = jnp.dot(images, turned, preferred_element_type=jnp.float32) * scale
        s_scr[s] = scores
        return jnp.maximum(carry, scores)

    first = jnp.full(s_scr.shape[1:], -jnp.inf, jnp.float32)
    lane_max = lax.fori_loop(0, half, shift_scores, first, unroll=9)
    highest = jnp.max(lane_max.T, axis=0, keepdims=True)
    highest_col = jnp.max(lane_max, axis=1, keepdims=True)

    def shift_sum(s, carry):
        return carry + jnp.exp(s_scr[s] - highest_col)

    lane_sum = lax.fori_loop(0, half, shift_sum, jnp.zeros(s_scr.shape[1:], jnp.float32), unroll=4)
    max_ref[...] = highest
    sum_ref[...] = jnp.sum(lane_sum.T, axis=0, keepdims=True)


def score_all(lhs, pieces):
    row_count, flat_len = lhs.shape
    ref_count = sum(piece.shape[0] for piece in pieces)
    scale = score_factor / math.sqrt(flat_len)
    highest, summed = pl.pallas_call(
        functools.partial(score_kernel, scale=scale),
        out_shape=(
            jax.ShapeDtypeStruct((1, row_count), jnp.float32),
            jax.ShapeDtypeStruct((1, row_count), jnp.float32),
        ),
        scratch_shapes=[
            pltpu.VMEM((2 * flat_len, ref_count), jnp.bfloat16),
            pltpu.VMEM((flat_len, ref_count), jnp.float32),
            pltpu.VMEM((ANGLES // 2, row_count, 2 * ref_count), jnp.float32),
        ],
    )(lhs, *pieces)
    return highest[0], summed[0]


def average_kernel(w_ref, x_ref, o_ref, s_scr):
    block = o_ref.shape[0]
    flat_len = o_ref.shape[1]
    s_scr[...] = jnp.dot(w_ref[...], x_ref[:, :flat_len], preferred_element_type=jnp.float32)
    step = 8
    total = None
    for part in range(step):
        partial = None
        for whole in range(ANGLES // step):
            angle = whole * step + part
            rows = s_scr[pl.ds(angle * block, block), :]
            if whole:
                rows = pltpu.roll(rows, whole * step * RADII, 1)
            partial = rows if partial is None else partial + rows
        if part:
            partial = pltpu.roll(partial, part * RADII, 1)
        total = partial if total is None else total + partial
    o_ref[...] = total


def ring_factors(count):
    factors = []
    while count > 1:
        factor = 4 if count % 4 == 0 else count
        factors.append(factor)
        count //= factor
    return factors


def staged_gather(rows, axis, held):
    count = lax.axis_size(axis)
    stride = 1
    factors = ring_factors(count)
    for round_index, factor in enumerate(factors):
        parts = [rows]
        for step in range(1, factor):
            pairs = []
            for source in range(count):
                digit = (source // stride) % factor
                pairs.append((source, source + ((digit + step) % factor - digit) * stride))
            parts.append(lax.ppermute(rows, axis, pairs))
        rows = jnp.concatenate(parts, axis=0)
        if round_index == len(factors) - 1:
            parts, held = lax.optimization_barrier((parts, held))
        stride *= factor
    return parts, held


def local(particles, references, classes, angles, weights):
    row_count, flat_len = particles.shape
    grp_size = lax.axis_size("grp")
    half_rows = row_count // grp_size
    grp_index = lax.axis_index("grp")
    particle_rows = angle_major(particles)
    own_rows = lax.dynamic_slice_in_dim(particle_rows, grp_index * half_rows, half_rows, 0)
    owner_count = lax.axis_size("loop")
    per_owner = references.shape[0] * grp_size
    capacity = max(2, row_count // owner_count)
    slot_count = owner_count * capacity
    owner_of = classes // per_owner
    member_of = classes % per_owner
    owner_hits = (owner_of[:, None] == jnp.arange(owner_count, dtype=jnp.int32)[None, :]).astype(
        jnp.int32
    )
    earlier = jnp.cumsum(owner_hits, axis=0) - owner_hits
    slot_index = jnp.sum(earlier * owner_hits, axis=1)
    target_slot = owner_of * capacity + slot_index
    placement = (jnp.arange(slot_count, dtype=jnp.int32)[:, None] == target_slot[None, :]).astype(
        jnp.bfloat16
    )
    labels = jnp.stack([member_of, angles, weights], axis=1).astype(jnp.bfloat16)
    label_lanes = 128
    labels = jnp.pad(labels, ((0, 0), (0, label_lanes - labels.shape[1])))
    own_rows = jnp.concatenate([own_rows, labels], axis=1)
    outgoing = jnp.dot(placement, own_rows, preferred_element_type=jnp.float32).astype(jnp.bfloat16)
    outgoing = outgoing.reshape(owner_count, capacity, flat_len + label_lanes)
    pieces, outgoing = staged_gather(references, "loop", outgoing)
    incoming = lax.all_to_all(outgoing, "loop", split_axis=0, concat_axis=0, tiled=True)
    highest, summed = score_all(particle_rows, pieces)
    incoming, highest, summed = lax.optimization_barrier((incoming, highest, summed))
    incoming = incoming.reshape(slot_count, flat_len + label_lanes)
    labels_in = incoming[:, flat_len : flat_len + 3]
    labels_in = labels_in.astype(jnp.float32)
    member_in = labels_in[:, 0]
    rotation = labels_in[:, 1]
    weight_of = labels_in[:, 2]
    block = -(-per_owner // 8) * 8
    angle_grid = jnp.arange(ANGLES, dtype=jnp.float32)
    member_grid = jnp.arange(block, dtype=jnp.float32)
    chosen = (angle_grid[:, None, None] == rotation[None, None, :]) & (
        member_grid[None, :, None] == member_in[None, None, :]
    )
    by_angle = jnp.where(chosen, weight_of[None, None, :], 0.0).astype(jnp.bfloat16)
    by_angle = by_angle.reshape(ANGLES * block, slot_count)
    partial_sums = pl.pallas_call(
        average_kernel,
        out_shape=jax.ShapeDtypeStruct((block, flat_len), jnp.float32),
        scratch_shapes=[pltpu.VMEM((ANGLES * block, flat_len), jnp.float32)],
    )(by_angle, incoming)
    partial_sums = partial_sums[:per_owner]
    weighted = (member_grid[:per_owner, None] == member_in[None, :]).astype(jnp.float32) * weight_of[None, :]
    partial_weight = jnp.sum(weighted, axis=1)
    own_classes = references.shape[0]
    stats = jnp.stack([highest, summed], axis=0)
    if grp_size == 2:
        partner = 1 - grp_index
        weight_row = jnp.zeros((1, flat_len), jnp.float32)
        weight_row = lax.dynamic_update_slice_in_dim(
            weight_row, lax.dynamic_slice_in_dim(partial_weight, partner * own_classes, own_classes, 0)[None], 0, 1
        )
        stat_rows = jnp.pad(
            lax.dynamic_slice_in_dim(stats, partner * half_rows, half_rows, 1), ((0, 0), (0, flat_len - half_rows))
        )
        sent = jnp.concatenate(
            [lax.dynamic_slice_in_dim(partial_sums, partner * own_classes, own_classes, 0), weight_row, stat_rows], axis=0
        )
        got = lax.ppermute(sent, "grp", [(0, 1), (1, 0)])
        class_sums = lax.dynamic_slice_in_dim(partial_sums, grp_index * own_classes, own_classes, 0) + got[:own_classes]
        class_weight = (
            lax.dynamic_slice_in_dim(partial_weight, grp_index * own_classes, own_classes, 0)
            + got[own_classes, :own_classes]
        )
        stats = jnp.stack(
            [lax.dynamic_slice_in_dim(stats, grp_index * half_rows, half_rows, 1), got[own_classes + 1 :, :half_rows]],
            axis=0,
        )
    else:
        slots = jnp.arange(grp_size, dtype=jnp.int32)[:, None, None] == grp_index
        stats = jnp.where(slots, stats[None], 0.0)
        partial_sums, partial_weight, stats = lax.psum((partial_sums, partial_weight, stats), "grp")
        class_sums = lax.dynamic_slice_in_dim(partial_sums, grp_index * own_classes, own_classes, 0)
        class_weight = lax.dynamic_slice_in_dim(partial_weight, grp_index * own_classes, own_classes, 0)
        stats = lax.dynamic_slice_in_dim(stats, grp_index * half_rows, half_rows, 2)
    class_average = class_sums / class_weight[:, None]
    class_average = class_average.reshape(-1, ANGLES, RADII).transpose(0, 2, 1).reshape(-1, flat_len)
    highest = jnp.max(stats[:, 0], axis=0)
    summed = jnp.sum(stats[:, 1] * jnp.exp(stats[:, 0] - highest[None, :]), axis=0)
    log_evidence = highest + jnp.log(summed)
    return (log_evidence, class_average)


def solution(mesh):
    return jax.shard_map(
        local,
        mesh=mesh,
        in_specs=(
            P("loop", None),
            P(("loop", "grp"), None),
            P(("loop", "grp")),
            P(("loop", "grp")),
            P(("loop", "grp")),
        ),
        out_specs=(P(("loop", "grp")), P(("loop", "grp"), None)),
        check_vma=False,
    )
```

```python
import functools
import math

import jax
import jax.numpy as jnp
from jax import lax
from jax.experimental import pallas as pl
from jax.experimental.pallas import tpu as pltpu
from jax.sharding import PartitionSpec as P

RADII = 48
ANGLES = 72


score_factor = 2.0


def angle_major(rows):
    count = rows.shape[0]
    return rows.reshape(count, RADII, ANGLES).transpose(0, 2, 1).reshape(count, RADII * ANGLES)


def score_kernel(*refs, scale):
    p_ref, piece_refs = refs[0], refs[1:-5]
    max_ref, sum_ref, r_scr, t_scr, s_scr = refs[-5:]
    flat_len = p_ref.shape[1]
    t_scr[...] = jnp.concatenate([piece[...] for piece in piece_refs], axis=0).astype(jnp.float32).T
    for angle in range(ANGLES):
        picked = t_scr[pl.ds(angle, RADII, stride=ANGLES), :].astype(r_scr.dtype)
        r_scr[pl.ds(angle * RADII, RADII), :] = picked
        r_scr[pl.ds(flat_len + angle * RADII, RADII), :] = picked
    images = p_ref[...]
    half = ANGLES // 2

    def shift_scores(s, carry):
        turned = jnp.concatenate(
            [
                r_scr[pl.ds(pl.multiple_of(s * RADII, 16), flat_len), :],
                r_scr[pl.ds(pl.multiple_of((s + half) * RADII, 16), flat_len), :],
            ],
            axis=1,
        )
        scores = jnp.dot(images, turned, preferred_element_type=jnp.float32) * scale
        s_scr[s] = scores
        return jnp.maximum(carry, scores)

    first = jnp.full(s_scr.shape[1:], -jnp.inf, jnp.float32)
    lane_max = lax.fori_loop(0, half, shift_scores, first, unroll=9)
    highest = jnp.max(lane_max.T, axis=0, keepdims=True)
    highest_col = jnp.max(lane_max, axis=1, keepdims=True)

    def shift_sum(s, carry):
        return carry + jnp.exp(s_scr[s] - highest_col)

    lane_sum = lax.fori_loop(0, half, shift_sum, jnp.zeros(s_scr.shape[1:], jnp.float32), unroll=9)
    max_ref[...] = highest
    sum_ref[...] = jnp.sum(lane_sum.T, axis=0, keepdims=True)


def score_all(lhs, pieces):
    row_count, flat_len = lhs.shape
    ref_count = sum(piece.shape[0] for piece in pieces)
    scale = score_factor / math.sqrt(flat_len)
    highest, summed = pl.pallas_call(
        functools.partial(score_kernel, scale=scale),
        out_shape=(
            jax.ShapeDtypeStruct((1, row_count), jnp.float32),
            jax.ShapeDtypeStruct((1, row_count), jnp.float32),
        ),
        scratch_shapes=[
            pltpu.VMEM((2 * flat_len, ref_count), jnp.bfloat16),
            pltpu.VMEM((flat_len, ref_count), jnp.float32),
            pltpu.VMEM((ANGLES // 2, row_count, 2 * ref_count), jnp.float32),
        ],
    )(lhs, *pieces)
    return highest[0], summed[0]


def average_kernel(w_ref, x_ref, o_ref, s_scr):
    block = o_ref.shape[0]
    flat_len = o_ref.shape[1]
    s_scr[...] = jnp.dot(w_ref[...], x_ref[:, :flat_len], preferred_element_type=jnp.float32)
    step = 8
    total = None
    for part in range(step):
        partial = None
        for whole in range(ANGLES // step):
            angle = whole * step + part
            rows = s_scr[pl.ds(angle * block, block), :]
            if whole:
                rows = pltpu.roll(rows, whole * step * RADII, 1)
            partial = rows if partial is None else partial + rows
        if part:
            partial = pltpu.roll(partial, part * RADII, 1)
        total = partial if total is None else total + partial
    o_ref[...] = total


def ring_factors(count):
    factors = []
    while count > 1:
        factor = 4 if count % 4 == 0 else count
        factors.append(factor)
        count //= factor
    return factors


def staged_gather(rows, axis, held):
    count = lax.axis_size(axis)
    stride = 1
    factors = ring_factors(count)
    for round_index, factor in enumerate(factors):
        parts = [rows]
        for step in range(1, factor):
            pairs = []
            for source in range(count):
                digit = (source // stride) % factor
                pairs.append((source, source + ((digit + step) % factor - digit) * stride))
            parts.append(lax.ppermute(rows, axis, pairs))
        rows = jnp.concatenate(parts, axis=0)
        if round_index == len(factors) - 1:
            parts, held = lax.optimization_barrier((parts, held))
        stride *= factor
    return parts, held


def local(particles, references, classes, angles, weights):
    row_count, flat_len = particles.shape
    grp_size = lax.axis_size("grp")
    half_rows = row_count // grp_size
    grp_index = lax.axis_index("grp")
    particle_rows = angle_major(particles)
    own_rows = lax.dynamic_slice_in_dim(particle_rows, grp_index * half_rows, half_rows, 0)
    owner_count = lax.axis_size("loop")
    per_owner = references.shape[0] * grp_size
    capacity = max(2, row_count // owner_count)
    slot_count = owner_count * capacity
    owner_of = classes // per_owner
    member_of = classes % per_owner
    owner_hits = (owner_of[:, None] == jnp.arange(owner_count, dtype=jnp.int32)[None, :]).astype(
        jnp.int32
    )
    earlier = jnp.cumsum(owner_hits, axis=0) - owner_hits
    slot_index = jnp.sum(earlier * owner_hits, axis=1)
    target_slot = owner_of * capacity + slot_index
    placement = (jnp.arange(slot_count, dtype=jnp.int32)[:, None] == target_slot[None, :]).astype(
        jnp.bfloat16
    )
    labels = jnp.stack([member_of, angles, weights], axis=1).astype(jnp.bfloat16)
    label_lanes = 128
    labels = jnp.pad(labels, ((0, 0), (0, label_lanes - labels.shape[1])))
    own_rows = jnp.concatenate([own_rows, labels], axis=1)
    outgoing = jnp.dot(placement, own_rows, preferred_element_type=jnp.float32).astype(jnp.bfloat16)
    outgoing = outgoing.reshape(owner_count, capacity, flat_len + label_lanes)
    pieces, outgoing = staged_gather(references, "loop", outgoing)
    incoming = lax.all_to_all(outgoing, "loop", split_axis=0, concat_axis=0, tiled=True)
    highest, summed = score_all(particle_rows, pieces)
    incoming, highest, summed = lax.optimization_barrier((incoming, highest, summed))
    incoming = incoming.reshape(slot_count, flat_len + label_lanes)
    labels_in = incoming[:, flat_len : flat_len + 3]
    labels_in = labels_in.astype(jnp.float32)
    member_in = labels_in[:, 0]
    rotation = labels_in[:, 1]
    weight_of = labels_in[:, 2]
    block = -(-per_owner // 8) * 8
    angle_grid = jnp.arange(ANGLES, dtype=jnp.float32)
    member_grid = jnp.arange(block, dtype=jnp.float32)
    chosen = (angle_grid[:, None, None] == rotation[None, None, :]) & (
        member_grid[None, :, None] == member_in[None, None, :]
    )
    by_angle = jnp.where(chosen, weight_of[None, None, :], 0.0).astype(jnp.bfloat16)
    by_angle = by_angle.reshape(ANGLES * block, slot_count)
    partial_sums = pl.pallas_call(
        average_kernel,
        out_shape=jax.ShapeDtypeStruct((block, flat_len), jnp.float32),
        scratch_shapes=[pltpu.VMEM((ANGLES * block, flat_len), jnp.float32)],
    )(by_angle, incoming)
    partial_sums = partial_sums[:per_owner].reshape(per_owner, ANGLES, RADII).transpose(0, 2, 1)
    partial_sums = partial_sums.reshape(per_owner, flat_len)
    weighted = (member_grid[:per_owner, None] == member_in[None, :]).astype(jnp.float32) * weight_of[None, :]
    partial_weight = jnp.sum(weighted, axis=1)
    own_classes = references.shape[0]
    stats = jnp.stack([highest, summed], axis=0)
    if grp_size == 2:
        partner = 1 - grp_index
        weight_row = jnp.zeros((1, flat_len), jnp.float32)
        weight_row = lax.dynamic_update_slice_in_dim(
            weight_row, lax.dynamic_slice_in_dim(partial_weight, partner * own_classes, own_classes, 0)[None], 0, 1
        )
        stat_rows = jnp.pad(
            lax.dynamic_slice_in_dim(stats, partner * half_rows, half_rows, 1), ((0, 0), (0, flat_len - half_rows))
        )
        sent = jnp.concatenate(
            [lax.dynamic_slice_in_dim(partial_sums, partner * own_classes, own_classes, 0), weight_row, stat_rows], axis=0
        )
        got = lax.ppermute(sent, "grp", [(0, 1), (1, 0)])
        class_sums = lax.dynamic_slice_in_dim(partial_sums, grp_index * own_classes, own_classes, 0) + got[:own_classes]
        class_weight = (
            lax.dynamic_slice_in_dim(partial_weight, grp_index * own_classes, own_classes, 0)
            + got[own_classes, :own_classes]
        )
        stats = jnp.stack(
            [lax.dynamic_slice_in_dim(stats, grp_index * half_rows, half_rows, 1), got[own_classes + 1 :, :half_rows]],
            axis=0,
        )
    else:
        slots = jnp.arange(grp_size, dtype=jnp.int32)[:, None, None] == grp_index
        stats = jnp.where(slots, stats[None], 0.0)
        partial_sums, partial_weight, stats = lax.psum((partial_sums, partial_weight, stats), "grp")
        class_sums = lax.dynamic_slice_in_dim(partial_sums, grp_index * own_classes, own_classes, 0)
        class_weight = lax.dynamic_slice_in_dim(partial_weight, grp_index * own_classes, own_classes, 0)
        stats = lax.dynamic_slice_in_dim(stats, grp_index * half_rows, half_rows, 2)
    class_average = class_sums / class_weight[:, None]
    highest = jnp.max(stats[:, 0], axis=0)
    summed = jnp.sum(stats[:, 1] * jnp.exp(stats[:, 0] - highest[None, :]), axis=0)
    log_evidence = highest + jnp.log(summed)
    return (log_evidence, class_average)


def solution(mesh):
    return jax.shard_map(
        local,
        mesh=mesh,
        in_specs=(
            P("loop", None),
            P(("loop", "grp"), None),
            P(("loop", "grp")),
            P(("loop", "grp")),
            P(("loop", "grp")),
        ),
        out_specs=(P(("loop", "grp")), P(("loop", "grp"), None)),
        check_vma=False,
    )
```
